32 devices in a mesh: pix: 16 (over z, y, core), ch: 2 (over x).
Axes of the slice: x: 2, y: 2, z: 4, core: 2. Of those that a mesh axis runs over, the one named last changes fastest.
Arguments:
- fine_pixels: bfloat16 [16384, 768], P('pix', 'ch'), as said below
- pool_kernel: bfloat16 [768, 384], P('ch'), may hold values from -0.21875 to 0.21875
- projections: bfloat16 [3, 384, 384], P(None, None, 'ch'), may hold values from -0.3125 to 0.3125
- mixing_weight: bfloat16 [384, 384], P('ch'), may hold values from -1.25 to 1.25
- send_list: int32 [256, 32], P('pix'), may hold values from 0 to 1023, as said below
- neighbours: int32 [16384, 8], P('pix'), may hold values from -1 to 1535, as said below
- cotangent: bfloat16 [16384, 384], P('pix', 'ch'), may hold values from -6 to 6
Outputs:
- section_output: bfloat16 [16384, 384], P('pix', 'ch')
- fine_gradient: bfloat16 [16384, 768], P('pix', 'ch')
- kernel_gradient: float32 [768, 384], P('ch')
- projection_gradient: float32 [3, 384, 384], P(None, None, 'ch')
- mixing_gradient: float32 [384, 384], P('ch')
The draws below stay inside these ranges and needn't reach their ends.
Inputs may be any that keep to these rules, and one draw needn't show every extreme that they name: `send_list`: row s * 16 + d lists rows of block s read by block d; the first n of its 32 slots are used (n from 2 to 32, 0 when s = d) and the others hold 0. Some block reads 32 rows from every other block, and block 15 sends 32 rows to block 0. `neighbours`: in block b, -1 marks a missing neighbour, which occurs only in the last slot of 8 pixels of each block; values under 1024 are rows of block b; 1024 + s * 32 + k names used slot k of send_list row s * 16 + b, and every used slot is named exactly once. `fine_pixels`: fine activations, finite, of order one in most rows.
All inputs are finite; a program needn't handle non-finite values.
Results may differ from the reference program's by a relative error of at most 0.012.
The reference program's roundings to bfloat16 on the way (of `pooled`, `projected`, `weights`, `attended`, `grad_attended`, `grad_projected` and `grad_pooled`) count: a program that leaves them out, or rounds other values in their place, can miss the bound.
Values may be sent and summed in bfloat16 or wider, within the bound.
No kernel may reach another device: no remote copies, remote signals or barrier semaphores. Data moves between devices by JAX's collectives and lax.ppermute only.
A program may use at most 64 MiB of HBM per device.

```python
import math
import jax
import jax.numpy as jnp
from jax import lax

CF = 192
C = 384
HD = 64
NEIGH = 8
CORNERS = 8
CP_DEV = 1024
PEERS = 16
SLOT = 32
COARSE = 16384


def halo_plan(key):
    base = jax.random.fold_in(key, 4242)
    subkeys = jax.random.split(base, 5)
    counts = jax.random.randint(subkeys[0], (PEERS, PEERS), 2, SLOT + 1)
    busiest = jax.random.randint(subkeys[1], (), 0, PEERS)
    source_grid = jnp.arange(PEERS)[:, None]
    dest_ids = jnp.arange(PEERS)[None, :]
    counts = jnp.where(dest_ids == busiest, SLOT, counts)
    counts = jnp.where((source_grid == PEERS - 1) & (dest_ids == 0), SLOT, counts)
    counts = jnp.where(source_grid == dest_ids, 0, counts)
    sent_rows = jax.random.randint(subkeys[2], (PEERS, PEERS, SLOT), 0, CP_DEV)
    live_slot = jnp.arange(SLOT)[None, None, :] < counts[:, :, None]
    send_rows = jnp.where(live_slot, sent_rows, 0).astype(jnp.int32)
    send_list = send_rows.reshape(PEERS * PEERS, SLOT)
    local_picks = jax.random.randint(subkeys[3], (PEERS, CP_DEV, NEIGH), 0, CP_DEV)
    orders = jax.vmap(lambda subkey: jax.random.permutation(subkey, CP_DEV))(jax.random.split(subkeys[4], PEERS))
    entry_ids = jnp.arange(PEERS * SLOT)
    source_ids = entry_ids // SLOT
    slot_ids = entry_ids % SLOT
    used_slot = slot_ids[None, :] < counts[source_ids, :].T
    targets = orders[:, :PEERS * SLOT]
    slot_column = jnp.broadcast_to((entry_ids % NEIGH)[None, :], targets.shape)
    dest_grid = jnp.broadcast_to(jnp.arange(PEERS)[:, None], targets.shape)
    current = local_picks[dest_grid, targets, slot_column]
    local_picks = local_picks.at[dest_grid, targets, slot_column].set(jnp.where(used_slot, CP_DEV + entry_ids[None, :], current))
    corners = orders[:, PEERS * SLOT:PEERS * SLOT + CORNERS]
    corner_grid = jnp.broadcast_to(jnp.arange(PEERS)[:, None], corners.shape)
    local_picks = local_picks.at[corner_grid, corners, NEIGH - 1].set(-1)
    return (send_list, local_picks.reshape(PEERS * CP_DEV, NEIGH).astype(jnp.int32))


def draw_send_list(key, part):
    return halo_plan(key)[0]


def draw_neighbours(key, part):
    return halo_plan(key)[1]


def draw_fine_pixels(key, part):
    subkeys = jax.random.split(jax.random.fold_in(key, 77), 1)
    values = jnp.clip(jax.random.normal(subkeys[0], (COARSE, 4 * CF), jnp.float32), -4.0, 4.0)
    return values.astype(jnp.bfloat16)


def level_of(key, dims, pieces, least, high):
    gain = 1.0
    for dim, shards_of in pieces:
        steps = jax.random.uniform(jax.random.fold_in(jax.random.fold_in(key, 6), dim), (shards_of,), jnp.float32, least / len(pieces), high / len(pieces))
        gain = gain * jnp.repeat(jnp.exp(steps), dims[dim] // shards_of).reshape((-1,) + (1,) * (len(dims) - 1 - dim))
    return gain


def normal_values(own_key, extent, spread, bound, pieces=(), kind=jnp.bfloat16):
    result = jax.random.normal(own_key, extent, jnp.float32) * spread
    if len(pieces) > 0:
        result = level_of(own_key, extent, pieces, -0.22, 0.18) * result
    return jnp.clip(result, min=-bound, max=bound).astype(kind)


def setup_inputs(seed: int = 0) -> dict:
    key_list = jax.random.split(jax.random.key(seed), 8)
    fine_pixels = draw_fine_pixels(jax.random.fold_in(key_list[7], 71), 0)
    pool_kernel = normal_values(key_list[1], (4 * CF, C), (4 * CF) ** -0.5, 0.21875, ((0, 2),))
    projections = normal_values(key_list[2], (3, C, C), C ** -0.5, 0.3125, ((2, 2),))
    mixing_weight = normal_values(key_list[3], (C, C), (C // 16) ** -0.5, 1.25, ((0, 2),))
    send_list = draw_send_list(jax.random.fold_in(key_list[7], 71), 0)
    neighbours = draw_neighbours(jax.random.fold_in(key_list[7], 71), 0)
    cotangent = normal_values(key_list[6], (COARSE, C), 1.0, 6.0, ((0, 16), (1, 2)))
    return dict(fine_pixels=fine_pixels, pool_kernel=pool_kernel, projections=projections, mixing_weight=mixing_weight, send_list=send_list, neighbours=neighbours, cotangent=cotangent)


def resolve(neighbours, send_list):
    row_ids = jnp.arange(COARSE, dtype=jnp.int32)
    owner_dev = (row_ids // CP_DEV).astype(jnp.int32)
    entry_ids = (neighbours - CP_DEV).astype(jnp.int32)
    remote = entry_ids >= 0
    entry_ids = jnp.clip(entry_ids, 0, PEERS * SLOT - 1).astype(jnp.int32)
    source = (entry_ids // SLOT).astype(jnp.int32)
    slot_pos = (entry_ids % SLOT).astype(jnp.int32)
    sent_rows = send_list[source * PEERS + owner_dev[:, None], slot_pos].astype(jnp.int32)
    global_rows = jnp.where(remote, source * CP_DEV + sent_rows, owner_dev[:, None] * CP_DEV + jnp.maximum(neighbours, 0))
    present = neighbours >= 0
    slot_rows = jnp.concatenate([row_ids[:, None], jnp.where(present, global_rows, 0)], axis=1).astype(jnp.int32)
    slot_live = jnp.concatenate([jnp.ones((COARSE, 1), bool), present], axis=1)
    return (slot_rows, slot_live)

def reference(fine_pixels, pool_kernel, projections, mixing_weight, send_list, neighbours, cotangent):
    f32 = jnp.float32
    bf16 = jnp.bfloat16
    heads = C // HD
    score_scale = 1.0 / math.sqrt(HD)
    grad_scale = 1.0 / math.sqrt(COARSE)
    pooled = jnp.dot(fine_pixels, pool_kernel, preferred_element_type=f32).astype(bf16)
    projected = jnp.einsum('rc,kcd->rkd', pooled.astype(f32), projections.astype(f32)).astype(bf16)
    queries = projected[:, 0]
    key_value = projected[:, 1:]
    slot_rows, slot_live = resolve(neighbours, send_list)
    block_rows = math.gcd(COARSE, 4096)
    block_count = COARSE // block_rows
    query_blocks = queries.reshape(block_count, block_rows, C)
    row_blocks = slot_rows.reshape(block_count, block_rows, NEIGH + 1)
    live_blocks = slot_live.reshape(block_count, block_rows, NEIGH + 1)

    def forward_block(inputs):
        query_block, rows_here, live_here = inputs
        gathered = jnp.take(key_value, rows_here, axis=0)
        block_keys = gathered[:, :, 0].reshape(block_rows, NEIGH + 1, heads, HD).astype(f32)
        block_values = gathered[:, :, 1].reshape(block_rows, NEIGH + 1, heads, HD).astype(f32)
        query_wide = query_block.reshape(block_rows, heads, HD).astype(f32)
        scores = jnp.einsum('bhd,bmhd->bhm', query_wide, block_keys) * score_scale
        shut = live_here[:, None, :]
        masked = jnp.where(shut, scores, -1e+30)
        largest = lax.optimization_barrier(jnp.max(masked, axis=2, keepdims=True))
        raised = jnp.where(shut, jnp.exp(masked - largest), 0.0)
        probabilities = raised / lax.optimization_barrier(jnp.sum(raised, axis=2, keepdims=True))
        weights = probabilities.astype(bf16).astype(f32)
        mixture = jnp.einsum('bhm,bmhd->bhd', weights, block_values)
        return (mixture.reshape(block_rows, C).astype(bf16), probabilities)
    attn_blocks, prob_blocks = lax.map(forward_block, (query_blocks, row_blocks, live_blocks))
    attended = attn_blocks.reshape(COARSE, C)
    section_output = (pooled.astype(f32) + jnp.dot(attended, mixing_weight, preferred_element_type=f32)).astype(bf16)
    grad_attended = jnp.dot(cotangent, mixing_weight.T, preferred_element_type=f32).astype(bf16)
    mixing_gradient = jnp.dot(attended.T, cotangent, preferred_element_type=f32) * grad_scale
    grad_blocks = grad_attended.reshape(block_count, block_rows, C)

    def backward_block(carried, inputs):
        query_block, rows_here, grad_block, probabilities = inputs
        gathered = jnp.take(key_value, rows_here, axis=0)
        block_keys = gathered[:, :, 0].reshape(block_rows, NEIGH + 1, heads, HD).astype(f32)
        block_values = gathered[:, :, 1].reshape(block_rows, NEIGH + 1, heads, HD).astype(f32)
        grad_mix = grad_block.reshape(block_rows, heads, HD).astype(f32)
        grad_weights = jnp.einsum('bhd,bmhd->bhm', grad_mix, block_values)
        grad_scores = probabilities * (grad_weights - lax.optimization_barrier(jnp.sum(probabilities * grad_weights, axis=2, keepdims=True))) * score_scale
        grad_query = jnp.einsum('bhm,bmhd->bhd', grad_scores, block_keys).reshape(block_rows, C)
        query_wide = query_block.reshape(block_rows, heads, HD).astype(f32)
        grad_keys = jnp.einsum('bhm,bhd->bmhd', grad_scores, query_wide)
        weights = probabilities.astype(bf16).astype(f32)
        grad_values = jnp.einsum('bhm,bhd->bmhd', weights, grad_mix)
        contribution = jnp.stack([grad_keys, grad_values], axis=2).reshape(block_rows * (NEIGH + 1), 2, C)
        contribution = lax.optimization_barrier(contribution.astype(bf16)).astype(f32)
        carried = carried.at[rows_here.reshape(-1)].add(contribution)
        return (carried, grad_query)
    start_grads = jnp.zeros((COARSE, 2, C), f32)
    key_grads, query_grads = lax.scan(backward_block, start_grads, (query_blocks, row_blocks, grad_blocks, prob_blocks))
    grad_projected = jnp.concatenate([query_grads.reshape(COARSE, 1, C), key_grads], axis=1).astype(bf16)
    projection_gradient = jnp.einsum('rc,rkd->kcd', pooled.astype(f32), grad_projected.astype(f32)) * grad_scale
    grad_pooled = (cotangent.astype(f32) + jnp.einsum('rkd,kcd->rc', grad_projected.astype(f32), projections.astype(f32))).astype(bf16)
    kernel_gradient = jnp.dot(fine_pixels.T, grad_pooled, preferred_element_type=f32) * grad_scale
    fine_gradient = jnp.dot(grad_pooled, pool_kernel.T, preferred_element_type=f32).astype(bf16)
    return (section_output, fine_gradient, kernel_gradient, projection_gradient, mixing_gradient)
```

```python
import math

import jax
import jax.numpy as jnp
from jax import lax
from jax.sharding import PartitionSpec as P

HD = 64


def pick_table(row_ids, total):
    return (row_ids[:, None] == jnp.arange(total, dtype=jnp.int32)[None, :]).astype(jnp.bfloat16)


def slot_index(neighbour_block, first_row, block_rows):
    present = neighbour_block >= 0
    own_rows = first_row + jnp.arange(block_rows, dtype=jnp.int32)
    slot_rows = jnp.concatenate([own_rows[:, None], jnp.where(present, neighbour_block, 0)], axis=1)
    slot_live = jnp.concatenate([jnp.ones((block_rows, 1), bool), present], axis=1)
    return (slot_rows, slot_live)


def attention_forward(queries, extended, neighbours, row_offset):
    f32 = jnp.float32
    bf16 = jnp.bfloat16
    row_count = queries.shape[0]
    span = queries.shape[1]
    ext_rows = extended.shape[0]
    heads_here = span // HD
    slot_width = neighbours.shape[1] + 1
    score_scale = 1.0 / math.sqrt(HD)
    block_rows = math.gcd(row_count, 512)
    block_count = row_count // block_rows
    block_starts = row_offset + jnp.arange(block_count, dtype=jnp.int32) * block_rows
    query_blocks = queries.reshape(block_count, block_rows, span)
    neighbour_blocks = neighbours.reshape(block_count, block_rows, slot_width - 1)
    flattened = extended.reshape(ext_rows, 2 * span)

    def forward_block(inputs):
        query_block, neighbour_block, first_row = inputs
        slot_rows, slot_live = slot_index(neighbour_block, first_row, block_rows)
        pieces = [
            jnp.dot(
                pick_table(slot_rows[:, slot], ext_rows), flattened, preferred_element_type=f32
            ).astype(bf16)
            for slot in range(slot_width)
        ]
        gathered = jnp.stack(pieces, axis=1).reshape(block_rows, slot_width, 2, span)
        block_keys = gathered[:, :, 0].reshape(block_rows, slot_width, heads_here, HD)
        block_values = gathered[:, :, 1].reshape(block_rows, slot_width, heads_here, HD)
        scores = (
            jnp.einsum(
                "bhd,bmhd->bhm",
                query_block.reshape(block_rows, heads_here, HD),
                block_keys,
                preferred_element_type=f32,
            )
            * score_scale
        )
        shut = slot_live[:, None, :]
        masked = jnp.where(shut, scores, -1e30)
        largest = jnp.max(masked, axis=2, keepdims=True)
        raised = jnp.where(shut, jnp.exp(masked - largest), 0.0)
        probabilities = raised / jnp.sum(raised, axis=2, keepdims=True)
        weights = probabilities.astype(bf16)
        mixture = jnp.einsum("bhm,bmhd->bhd", weights, block_values, preferred_element_type=f32)
        return (mixture.reshape(block_rows, span).astype(bf16), probabilities, gathered)

    attn_blocks, prob_blocks, kv_blocks = lax.map(
        forward_block, (query_blocks, neighbour_blocks, block_starts)
    )
    return (attn_blocks.reshape(row_count, span), prob_blocks, kv_blocks)


def attention_backward(
    queries, ext_rows, neighbours, row_offset, grad_attended, prob_blocks, kv_blocks
):
    f32 = jnp.float32
    bf16 = jnp.bfloat16
    row_count = queries.shape[0]
    span = queries.shape[1]
    heads_here = span // HD
    slot_width = neighbours.shape[1] + 1
    score_scale = 1.0 / math.sqrt(HD)
    block_rows = math.gcd(row_count, 512)
    block_count = row_count // block_rows
    block_starts = row_offset + jnp.arange(block_count, dtype=jnp.int32) * block_rows
    query_blocks = queries.reshape(block_count, block_rows, span)
    neighbour_blocks = neighbours.reshape(block_count, block_rows, slot_width - 1)
    grad_blocks = grad_attended.reshape(block_count, block_rows, span)

    def backward_block(carried, inputs):
        query_block, neighbour_block, first_row, grad_block, probabilities, gathered = inputs
        slot_rows, slot_live = slot_index(neighbour_block, first_row, block_rows)
        block_keys = gathered[:, :, 0].reshape(block_rows, slot_width, heads_here, HD).astype(f32)
        block_values = gathered[:, :, 1].reshape(block_rows, slot_width, heads_here, HD).astype(f32)
        grad_mix = grad_block.reshape(block_rows, heads_here, HD).astype(f32)
        grad_weights = jnp.einsum("bhd,bmhd->bhm", grad_mix, block_values)
        grad_scores = (
            probabilities
            * (grad_weights - jnp.sum(probabilities * grad_weights, axis=2, keepdims=True))
            * score_scale
        )
        grad_query = jnp.einsum("bhm,bmhd->bhd", grad_scores, block_keys).reshape(block_rows, span)
        query_wide = query_block.reshape(block_rows, heads_here, HD).astype(f32)
        grad_keys = jnp.einsum("bhm,bhd->bmhd", grad_scores, query_wide)
        rounded = lax.optimization_barrier(probabilities.astype(bf16))
        grad_values = jnp.einsum("bhm,bhd->bmhd", rounded.astype(f32), grad_mix)
        contribution = (
            jnp.stack([grad_keys, grad_values], axis=2)
            .reshape(block_rows, slot_width, 2 * span)
            .astype(bf16)
        )
        for slot in range(slot_width):
            carried = carried + jnp.einsum(
                "bx,bc->xc",
                pick_table(slot_rows[:, slot], ext_rows),
                contribution[:, slot],
                preferred_element_type=f32,
            )
        return (carried, grad_query)

    start_grads = jnp.zeros((ext_rows, 2 * span), f32)
    carried, query_grads = lax.scan(
        backward_block,
        start_grads,
        (query_blocks, neighbour_blocks, block_starts, grad_blocks, prob_blocks, kv_blocks),
    )
    return (carried.reshape(ext_rows, 2, span), query_grads.reshape(row_count, span))


def ch_exchange(value):
    size = lax.axis_size("ch")
    return [
        lax.ppermute(value, "ch", [(i, (i + shift) % size) for i in range(size)])
        for shift in range(1, size)
    ]


def ch_assemble(own, others, axis):
    size = len(others) + 1
    index = lax.axis_index("ch")
    pieces = [own] + others
    result = None
    for case in range(size):
        ordered = jnp.concatenate([pieces[(case - j) % size] for j in range(size)], axis=axis)
        result = ordered if result is None else jnp.where(index == case, ordered, result)
    return result


def per_device(
    fine_pixels, pool_kernel, projections, mixing_weight, send_list, neighbours, cotangent
):
    f32 = jnp.float32
    bf16 = jnp.bfloat16
    row_count = fine_pixels.shape[0]
    half_width = projections.shape[2]
    ch_size = lax.axis_size("ch")
    ch_index = lax.axis_index("ch")
    peer_count = lax.axis_size("pix")
    slot_count = send_list.shape[1]
    grad_scale = 1.0 / math.sqrt(row_count * peer_count)
    send_pick = pick_table(send_list.reshape(-1), row_count)
    fine_others = ch_exchange(fine_pixels)
    kernel_others = ch_exchange(pool_kernel)
    cot_others = ch_exchange(cotangent)
    proj_others = ch_exchange(projections)
    mix_pieces = mixing_weight.reshape(mixing_weight.shape[0], ch_size, half_width)
    mix_others = [
        lax.ppermute(
            jnp.take(mix_pieces, (ch_index + shift) % ch_size, axis=1),
            "ch",
            [(i, (i + shift) % ch_size) for i in range(ch_size)],
        )
        for shift in range(1, ch_size)
    ]
    mix_own = jnp.take(mix_pieces, ch_index, axis=1)
    pooled_sum = jnp.dot(fine_pixels, pool_kernel, preferred_element_type=f32)
    for fine_other, kernel_other in zip(fine_others, kernel_others):
        pooled_sum = pooled_sum + jnp.dot(fine_other, kernel_other, preferred_element_type=f32)
    pooled_all = pooled_sum.astype(bf16)
    pooled = lax.dynamic_slice_in_dim(pooled_all, ch_index * half_width, half_width, axis=1)
    upstream = ch_assemble(cotangent, cot_others, axis=1)
    projected = jnp.einsum(
        "rc,kcd->rkd", pooled_all, projections, preferred_element_type=f32
    ).astype(bf16)
    queries = projected[:, 0]
    key_value = projected[:, 1:]
    outgoing = (
        jnp.dot(send_pick, key_value.reshape(row_count, 2 * half_width), preferred_element_type=f32)
        .astype(bf16)
        .reshape(peer_count, slot_count, 2, half_width)
    )
    incoming = lax.all_to_all(outgoing, "pix", split_axis=0, concat_axis=0, tiled=True)
    extended = jnp.concatenate(
        [key_value, incoming.reshape(peer_count * slot_count, 2, half_width)], axis=0
    )
    attended, prob_blocks, kv_blocks = attention_forward(queries, extended, neighbours, 0)
    attended_others = ch_exchange(attended)
    branch = jnp.dot(attended, mix_own, preferred_element_type=f32)
    for attended_other, mix_other in zip(attended_others, mix_others):
        branch = branch + jnp.dot(attended_other, mix_other, preferred_element_type=f32)
    section_output = (pooled.astype(f32) + branch).astype(bf16)
    grad_attended = jnp.dot(upstream, mixing_weight.T, preferred_element_type=f32).astype(bf16)
    mixing_term = jnp.dot(attended.T, upstream, preferred_element_type=f32) * grad_scale
    mixing_gradient = lax.psum(mixing_term, "pix")
    carried, query_grads = attention_backward(
        queries, extended.shape[0], neighbours, 0, grad_attended, prob_blocks, kv_blocks
    )
    remote_grads = carried[row_count:].reshape(peer_count, slot_count, 2, half_width)
    returned = lax.all_to_all(remote_grads, "pix", split_axis=0, concat_axis=0, tiled=True)
    returned_rows = jnp.einsum(
        "px,pc->xc",
        send_pick,
        returned.reshape(peer_count * slot_count, 2 * half_width).astype(bf16),
        preferred_element_type=f32,
    )
    local_grads = carried[:row_count] + returned_rows.reshape(row_count, 2, half_width)
    grad_projected = jnp.concatenate(
        [query_grads.reshape(row_count, 1, half_width), local_grads], axis=1
    ).astype(bf16)
    grad_others = ch_exchange(grad_projected)
    projection_term = (
        jnp.einsum("rc,rkd->kcd", pooled_all, grad_projected, preferred_element_type=f32)
        * grad_scale
    )
    mixing_gradient, projection_term = lax.optimization_barrier((mixing_gradient, projection_term))
    projection_gradient = lax.psum(projection_term, "pix")
    pooled_sum = upstream.astype(f32) + jnp.einsum(
        "rkd,kcd->rc", grad_projected, projections, preferred_element_type=f32
    )
    for grad_other, proj_other in zip(grad_others, proj_others):
        pooled_sum = pooled_sum + jnp.einsum(
            "rkd,kcd->rc", grad_other, proj_other, preferred_element_type=f32
        )
    grad_pooled = pooled_sum.astype(bf16)
    kernel_term = jnp.dot(fine_pixels.T, grad_pooled, preferred_element_type=f32) * grad_scale
    fine_gradient = jnp.dot(grad_pooled, pool_kernel.T, preferred_element_type=f32).astype(bf16)
    projection_gradient, kernel_term = lax.optimization_barrier((projection_gradient, kernel_term))
    kernel_gradient = lax.psum(kernel_term, "pix")
    return (section_output, fine_gradient, kernel_gradient, projection_gradient, mixing_gradient)


def solution(mesh):
    placed = (
        P("pix", "ch"),
        P("ch", None),
        P(None, None, "ch"),
        P("ch", None),
        P("pix", None),
        P("pix", None),
        P("pix", "ch"),
    )
    return jax.shard_map(
        per_device,
        mesh=mesh,
        in_specs=placed,
        out_specs=(
            P("pix", "ch"),
            P("pix", "ch"),
            P("ch", None),
            P(None, None, "ch"),
            P("ch", None),
        ),
        check_vma=False,
    )
```

```python
import math

import jax
import jax.numpy as jnp
from jax import lax
from jax.sharding import PartitionSpec as P

HD = 64


def pick_table(row_ids, total):
    return (row_ids[:, None] == jnp.arange(total, dtype=jnp.int32)[None, :]).astype(jnp.bfloat16)


def slot_index(neighbour_block, first_row, block_rows):
    present = neighbour_block >= 0
    own_rows = first_row + jnp.arange(block_rows, dtype=jnp.int32)
    slot_rows = jnp.concatenate([own_rows[:, None], jnp.where(present, neighbour_block, 0)], axis=1)
    slot_live = jnp.concatenate([jnp.ones((block_rows, 1), bool), present], axis=1)
    return (slot_rows, slot_live)


def attention_forward(queries, extended, neighbours, row_offset):
    f32 = jnp.float32
    bf16 = jnp.bfloat16
    row_count = queries.shape[0]
    span = queries.shape[1]
    ext_rows = extended.shape[0]
    heads_here = span // HD
    slot_width = neighbours.shape[1] + 1
    score_scale = 1.0 / math.sqrt(HD)
    block_rows = math.gcd(row_count, 512)
    block_count = row_count // block_rows
    block_starts = row_offset + jnp.arange(block_count, dtype=jnp.int32) * block_rows
    query_blocks = queries.reshape(block_count, block_rows, span)
    neighbour_blocks = neighbours.reshape(block_count, block_rows, slot_width - 1)
    flattened = extended.reshape(ext_rows, 2 * span)

    def forward_block(inputs):
        query_block, neighbour_block, first_row = inputs
        slot_rows, slot_live = slot_index(neighbour_block, first_row, block_rows)
        pieces = [
            jnp.dot(
                pick_table(slot_rows[:, slot], ext_rows), flattened, preferred_element_type=f32
            ).astype(bf16)
            for slot in range(slot_width)
        ]
        gathered = jnp.stack(pieces, axis=1).reshape(block_rows, slot_width, 2, span)
        block_keys = gathered[:, :, 0].reshape(block_rows, slot_width, heads_here, HD)
        block_values = gathered[:, :, 1].reshape(block_rows, slot_width, heads_here, HD)
        scores = (
            jnp.einsum(
                "bhd,bmhd->bhm",
                query_block.reshape(block_rows, heads_here, HD),
                block_keys,
                preferred_element_type=f32,
            )
            * score_scale
        )
        shut = slot_live[:, None, :]
        masked = jnp.where(shut, scores, -1e30)
        largest = jnp.max(masked, axis=2, keepdims=True)
        raised = jnp.where(shut, jnp.exp(masked - largest), 0.0)
        probabilities = raised / jnp.sum(raised, axis=2, keepdims=True)
        weights = probabilities.astype(bf16)
        mixture = jnp.einsum("bhm,bmhd->bhd", weights, block_values, preferred_element_type=f32)
        return (mixture.reshape(block_rows, span).astype(bf16), probabilities, gathered)

    attn_blocks, prob_blocks, kv_blocks = lax.map(
        forward_block, (query_blocks, neighbour_blocks, block_starts)
    )
    return (attn_blocks.reshape(row_count, span), prob_blocks, kv_blocks)


def attention_backward(
    queries, ext_rows, neighbours, row_offset, grad_attended, prob_blocks, kv_blocks
):
    f32 = jnp.float32
    bf16 = jnp.bfloat16
    row_count = queries.shape[0]
    span = queries.shape[1]
    heads_here = span // HD
    slot_width = neighbours.shape[1] + 1
    score_scale = 1.0 / math.sqrt(HD)
    block_rows = math.gcd(row_count, 512)
    block_count = row_count // block_rows
    block_starts = row_offset + jnp.arange(block_count, dtype=jnp.int32) * block_rows
    query_blocks = queries.reshape(block_count, block_rows, span)
    neighbour_blocks = neighbours.reshape(block_count, block_rows, slot_width - 1)
    grad_blocks = grad_attended.reshape(block_count, block_rows, span)

    def backward_block(carried, inputs):
        query_block, neighbour_block, first_row, grad_block, probabilities, gathered = inputs
        slot_rows, slot_live = slot_index(neighbour_block, first_row, block_rows)
        block_keys = gathered[:, :, 0].reshape(block_rows, slot_width, heads_here, HD).astype(f32)
        block_values = gathered[:, :, 1].reshape(block_rows, slot_width, heads_here, HD).astype(f32)
        grad_mix = grad_block.reshape(block_rows, heads_here, HD).astype(f32)
        grad_weights = jnp.einsum("bhd,bmhd->bhm", grad_mix, block_values)
        grad_scores = (
            probabilities
            * (grad_weights - jnp.sum(probabilities * grad_weights, axis=2, keepdims=True))
            * score_scale
        )
        grad_query = jnp.einsum("bhm,bmhd->bhd", grad_scores, block_keys).reshape(block_rows, span)
        query_wide = query_block.reshape(block_rows, heads_here, HD).astype(f32)
        grad_keys = jnp.einsum("bhm,bhd->bmhd", grad_scores, query_wide)
        rounded = lax.optimization_barrier(probabilities.astype(bf16))
        grad_values = jnp.einsum("bhm,bhd->bmhd", rounded.astype(f32), grad_mix)
        contribution = (
            jnp.stack([grad_keys, grad_values], axis=2)
            .reshape(block_rows, slot_width, 2 * span)
            .astype(bf16)
        )
        for slot in range(slot_width):
            carried = carried + jnp.einsum(
                "bx,bc->xc",
                pick_table(slot_rows[:, slot], ext_rows),
                contribution[:, slot],
                preferred_element_type=f32,
            )
        return (carried, grad_query)

    start_grads = jnp.zeros((ext_rows, 2 * span), f32)
    carried, query_grads = lax.scan(
        backward_block,
        start_grads,
        (query_blocks, neighbour_blocks, block_starts, grad_blocks, prob_blocks, kv_blocks),
    )
    return (carried.reshape(ext_rows, 2, span), query_grads.reshape(row_count, span))


def ch_exchange(value):
    size = lax.axis_size("ch")
    return [
        lax.ppermute(value, "ch", [(i, (i + shift) % size) for i in range(size)])
        for shift in range(1, size)
    ]


def ch_assemble(own, others, axis):
    size = len(others) + 1
    index = lax.axis_index("ch")
    pieces = [own] + others
    result = None
    for case in range(size):
        ordered = jnp.concatenate([pieces[(case - j) % size] for j in range(size)], axis=axis)
        result = ordered if result is None else jnp.where(index == case, ordered, result)
    return result


def pix_sum(terms):
    size = lax.axis_size("pix")
    width = terms[0].shape[-1]
    flat = jnp.concatenate([term.reshape(-1, width) for term in terms], axis=0)
    rows = flat.shape[0]
    chunk = -(-rows // size)
    flat = jnp.pad(flat, ((0, chunk * size - rows), (0, 0)))
    parts = lax.all_to_all(flat.reshape(size, chunk, width), "pix", 0, 0, tiled=True)
    reduced = jnp.sum(parts, axis=0)
    spread = jnp.broadcast_to(reduced[None], (size, chunk, width))
    gathered = lax.all_to_all(spread, "pix", 0, 0, tiled=True).reshape(size * chunk, width)
    results = []
    offset = 0
    for term in terms:
        count = term.size // width
        results.append(gathered[offset : offset + count].reshape(term.shape))
        offset += count
    return results


def per_device(
    fine_pixels, pool_kernel, projections, mixing_weight, send_list, neighbours, cotangent
):
    f32 = jnp.float32
    bf16 = jnp.bfloat16
    row_count = fine_pixels.shape[0]
    half_width = projections.shape[2]
    ch_size = lax.axis_size("ch")
    ch_index = lax.axis_index("ch")
    peer_count = lax.axis_size("pix")
    slot_count = send_list.shape[1]
    grad_scale = 1.0 / math.sqrt(row_count * peer_count)
    send_pick = pick_table(send_list.reshape(-1), row_count)
    fine_others = ch_exchange(fine_pixels)
    kernel_others = ch_exchange(pool_kernel)
    cot_others = ch_exchange(cotangent)
    proj_others = ch_exchange(projections)
    mix_pieces = mixing_weight.reshape(mixing_weight.shape[0], ch_size, half_width)
    mix_others = [
        lax.ppermute(
            jnp.take(mix_pieces, (ch_index + shift) % ch_size, axis=1),
            "ch",
            [(i, (i + shift) % ch_size) for i in range(ch_size)],
        )
        for shift in range(1, ch_size)
    ]
    mix_own = jnp.take(mix_pieces, ch_index, axis=1)
    pooled_sum = jnp.dot(fine_pixels, pool_kernel, preferred_element_type=f32)
    for fine_other, kernel_other in zip(fine_others, kernel_others):
        pooled_sum = pooled_sum + jnp.dot(fine_other, kernel_other, preferred_element_type=f32)
    pooled_all = pooled_sum.astype(bf16)
    pooled = lax.dynamic_slice_in_dim(pooled_all, ch_index * half_width, half_width, axis=1)
    upstream = ch_assemble(cotangent, cot_others, axis=1)
    projected = jnp.einsum(
        "rc,kcd->rkd", pooled_all, projections, preferred_element_type=f32
    ).astype(bf16)
    queries = projected[:, 0]
    key_value = projected[:, 1:]
    outgoing = (
        jnp.dot(send_pick, key_value.reshape(row_count, 2 * half_width), preferred_element_type=f32)
        .astype(bf16)
        .reshape(peer_count, slot_count, 2, half_width)
    )
    incoming = lax.all_to_all(outgoing, "pix", split_axis=0, concat_axis=0, tiled=True)
    extended = jnp.concatenate(
        [key_value, incoming.reshape(peer_count * slot_count, 2, half_width)], axis=0
    )
    attended, prob_blocks, kv_blocks = attention_forward(queries, extended, neighbours, 0)
    attended_others = ch_exchange(attended)
    branch = jnp.dot(attended, mix_own, preferred_element_type=f32)
    for attended_other, mix_other in zip(attended_others, mix_others):
        branch = branch + jnp.dot(attended_other, mix_other, preferred_element_type=f32)
    section_output = (pooled.astype(f32) + branch).astype(bf16)
    grad_attended = jnp.dot(upstream, mixing_weight.T, preferred_element_type=f32).astype(bf16)
    mixing_term = jnp.dot(attended.T, upstream, preferred_element_type=f32) * grad_scale
    carried, query_grads = attention_backward(
        queries, extended.shape[0], neighbours, 0, grad_attended, prob_blocks, kv_blocks
    )
    remote_grads = carried[row_count:].reshape(peer_count, slot_count, 2, half_width)
    returned = lax.all_to_all(remote_grads, "pix", split_axis=0, concat_axis=0, tiled=True)
    returned_rows = jnp.einsum(
        "px,pc->xc",
        send_pick,
        returned.reshape(peer_count * slot_count, 2 * half_width).astype(bf16),
        preferred_element_type=f32,
    )
    local_grads = carried[:row_count] + returned_rows.reshape(row_count, 2, half_width)
    grad_projected = jnp.concatenate(
        [query_grads.reshape(row_count, 1, half_width), local_grads], axis=1
    ).astype(bf16)
    grad_others = ch_exchange(grad_projected)
    projection_term = (
        jnp.einsum("rc,rkd->kcd", pooled_all, grad_projected, preferred_element_type=f32)
        * grad_scale
    )
    pooled_sum = upstream.astype(f32) + jnp.einsum(
        "rkd,kcd->rc", grad_projected, projections, preferred_element_type=f32
    )
    for grad_other, proj_other in zip(grad_others, proj_others):
        pooled_sum = pooled_sum + jnp.einsum(
            "rkd,kcd->rc", grad_other, proj_other, preferred_element_type=f32
        )
    grad_pooled = pooled_sum.astype(bf16)
    kernel_term = jnp.dot(fine_pixels.T, grad_pooled, preferred_element_type=f32) * grad_scale
    fine_gradient = jnp.dot(grad_pooled, pool_kernel.T, preferred_element_type=f32).astype(bf16)
    kernel_gradient, projection_gradient, mixing_gradient = pix_sum(
        (kernel_term, projection_term, mixing_term)
    )
    return (section_output, fine_gradient, kernel_gradient, projection_gradient, mixing_gradient)


def solution(mesh):
    placed = (
        P("pix", "ch"),
        P("ch", None),
        P(None, None, "ch"),
        P("ch", None),
        P("pix", None),
        P("pix", None),
        P("pix", "ch"),
    )
    return jax.shard_map(
        per_device,
        mesh=mesh,
        in_specs=placed,
        out_specs=(
            P("pix", "ch"),
            P("pix", "ch"),
            P("ch", None),
            P(None, None, "ch"),
            P("ch", None),
        ),
        check_vma=False,
    )
```

```python
import math

import jax
import jax.numpy as jnp
from jax import lax
from jax.sharding import PartitionSpec as P

HD = 64


def pick_table(row_ids, total):
    return (row_ids[:, None] == jnp.arange(total, dtype=jnp.int32)[None, :]).astype(jnp.bfloat16)


def slot_index(neighbour_block, first_row, block_rows):
    present = neighbour_block >= 0
    own_rows = first_row + jnp.arange(block_rows, dtype=jnp.int32)
    slot_rows = jnp.concatenate([own_rows[:, None], jnp.where(present, neighbour_block, 0)], axis=1)
    slot_live = jnp.concatenate([jnp.ones((block_rows, 1), bool), present], axis=1)
    return (slot_rows, slot_live)


def attention_forward(queries, extended, neighbours, row_offset):
    f32 = jnp.float32
    bf16 = jnp.bfloat16
    row_count = queries.shape[0]
    span = queries.shape[1]
    ext_rows = extended.shape[0]
    heads_here = span // HD
    slot_width = neighbours.shape[1] + 1
    score_scale = 1.0 / math.sqrt(HD)
    block_rows = math.gcd(row_count, 512)
    block_count = row_count // block_rows
    block_starts = row_offset + jnp.arange(block_count, dtype=jnp.int32) * block_rows
    query_blocks = queries.reshape(block_count, block_rows, span)
    neighbour_blocks = neighbours.reshape(block_count, block_rows, slot_width - 1)
    flattened = extended.reshape(ext_rows, 2 * span)

    def forward_block(inputs):
        query_block, neighbour_block, first_row = inputs
        slot_rows, slot_live = slot_index(neighbour_block, first_row, block_rows)
        pieces = [
            jnp.dot(
                pick_table(slot_rows[:, slot], ext_rows), flattened, preferred_element_type=f32
            ).astype(bf16)
            for slot in range(slot_width)
        ]
        gathered = jnp.stack(pieces, axis=1).reshape(block_rows, slot_width, 2, span)
        block_keys = gathered[:, :, 0].reshape(block_rows, slot_width, heads_here, HD)
        block_values = gathered[:, :, 1].reshape(block_rows, slot_width, heads_here, HD)
        scores = (
            jnp.einsum(
                "bhd,bmhd->bhm",
                query_block.reshape(block_rows, heads_here, HD),
                block_keys,
                preferred_element_type=f32,
            )
            * score_scale
        )
        shut = slot_live[:, None, :]
        masked = jnp.where(shut, scores, -1e30)
        largest = jnp.max(masked, axis=2, keepdims=True)
        raised = jnp.where(shut, jnp.exp(masked - largest), 0.0)
        probabilities = raised / jnp.sum(raised, axis=2, keepdims=True)
        weights = probabilities.astype(bf16)
        mixture = jnp.einsum("bhm,bmhd->bhd", weights, block_values, preferred_element_type=f32)
        return (mixture.reshape(block_rows, span).astype(bf16), probabilities, gathered)

    outputs = [
        forward_block((query_blocks[b], neighbour_blocks[b], block_starts[b]))
        for b in range(block_count)
    ]
    attn_blocks = jnp.stack([out[0] for out in outputs])
    prob_blocks = [out[1] for out in outputs]
    kv_blocks = [out[2] for out in outputs]
    return (attn_blocks.reshape(row_count, span), prob_blocks, kv_blocks)


def attention_backward(
    queries, ext_rows, neighbours, row_offset, grad_attended, prob_blocks, kv_blocks, riders
):
    f32 = jnp.float32
    bf16 = jnp.bfloat16
    row_count = queries.shape[0]
    span = queries.shape[1]
    heads_here = span // HD
    slot_width = neighbours.shape[1] + 1
    score_scale = 1.0 / math.sqrt(HD)
    block_rows = math.gcd(row_count, 512)
    block_count = row_count // block_rows
    block_starts = row_offset + jnp.arange(block_count, dtype=jnp.int32) * block_rows
    query_blocks = queries.reshape(block_count, block_rows, span)
    neighbour_blocks = neighbours.reshape(block_count, block_rows, slot_width - 1)
    grad_blocks = grad_attended.reshape(block_count, block_rows, span)

    def backward_block(carried, inputs):
        query_block, neighbour_block, first_row, grad_block, probabilities, gathered = inputs
        slot_rows, slot_live = slot_index(neighbour_block, first_row, block_rows)
        block_keys = gathered[:, :, 0].reshape(block_rows, slot_width, heads_here, HD).astype(f32)
        block_values = gathered[:, :, 1].reshape(block_rows, slot_width, heads_here, HD).astype(f32)
        grad_mix = grad_block.reshape(block_rows, heads_here, HD).astype(f32)
        grad_weights = jnp.einsum("bhd,bmhd->bhm", grad_mix, block_values)
        grad_scores = (
            probabilities
            * (grad_weights - jnp.sum(probabilities * grad_weights, axis=2, keepdims=True))
            * score_scale
        )
        grad_query = jnp.einsum("bhm,bmhd->bhd", grad_scores, block_keys).reshape(block_rows, span)
        query_wide = query_block.reshape(block_rows, heads_here, HD).astype(f32)
        grad_keys = jnp.einsum("bhm,bhd->bmhd", grad_scores, query_wide)
        rounded = lax.optimization_barrier(probabilities.astype(bf16))
        grad_values = jnp.einsum("bhm,bhd->bmhd", rounded.astype(f32), grad_mix)
        contribution = (
            jnp.stack([grad_keys, grad_values], axis=2)
            .reshape(block_rows, slot_width, 2 * span)
            .astype(bf16)
        )
        for slot in range(slot_width):
            carried = carried + jnp.einsum(
                "bx,bc->xc",
                pick_table(slot_rows[:, slot], ext_rows),
                contribution[:, slot],
                preferred_element_type=f32,
            )
        return (carried, grad_query)

    carried = jnp.zeros((ext_rows, 2 * span), f32)
    query_grads = []
    for b in range(block_count):
        carried, grad_query = backward_block(
            carried,
            (query_blocks[b], neighbour_blocks[b], block_starts[b], grad_blocks[b],
             prob_blocks[b], kv_blocks[b]),
        )
        query_grads.append(grad_query)
        if b == 0:
            carried, riders = lax.optimization_barrier((carried, riders))
    query_grads = jnp.stack(query_grads)
    return (carried.reshape(ext_rows, 2, span), query_grads.reshape(row_count, span), riders)


def ch_exchange(value):
    size = lax.axis_size("ch")
    return [
        lax.ppermute(value, "ch", [(i, (i + shift) % size) for i in range(size)])
        for shift in range(1, size)
    ]


def ch_assemble(own, others, axis):
    size = len(others) + 1
    index = lax.axis_index("ch")
    pieces = [own] + others
    result = None
    for case in range(size):
        ordered = jnp.concatenate([pieces[(case - j) % size] for j in range(size)], axis=axis)
        result = ordered if result is None else jnp.where(index == case, ordered, result)
    return result


def pix_sum(terms):
    size = lax.axis_size("pix")
    width = terms[0].shape[-1]
    flat = jnp.concatenate([term.reshape(-1, width) for term in terms], axis=0)
    rows = flat.shape[0]
    chunk = -(-rows // size)
    flat = jnp.pad(flat, ((0, chunk * size - rows), (0, 0)))
    parts = lax.all_to_all(flat.reshape(size, chunk, width), "pix", 0, 0, tiled=True)
    reduced = jnp.sum(parts, axis=0)
    spread = jnp.broadcast_to(reduced[None], (size, chunk, width))
    gathered = lax.all_to_all(spread, "pix", 0, 0, tiled=True).reshape(size * chunk, width)
    results = []
    offset = 0
    for term in terms:
        count = term.size // width
        results.append(gathered[offset : offset + count].reshape(term.shape))
        offset += count
    return results


def per_device(
    fine_pixels, pool_kernel, projections, mixing_weight, send_list, neighbours, cotangent
):
    f32 = jnp.float32
    bf16 = jnp.bfloat16
    row_count = fine_pixels.shape[0]
    half_width = projections.shape[2]
    ch_size = lax.axis_size("ch")
    ch_index = lax.axis_index("ch")
    peer_count = lax.axis_size("pix")
    slot_count = send_list.shape[1]
    grad_scale = 1.0 / math.sqrt(row_count * peer_count)
    send_pick = pick_table(send_list.reshape(-1), row_count)
    fine_others = ch_exchange(fine_pixels)
    kernel_others = ch_exchange(pool_kernel)
    cot_others = ch_exchange(cotangent)
    proj_others = ch_exchange(projections)
    mix_pieces = mixing_weight.reshape(mixing_weight.shape[0], ch_size, half_width)
    mix_others = [
        lax.ppermute(
            jnp.take(mix_pieces, (ch_index + shift) % ch_size, axis=1),
            "ch",
            [(i, (i + shift) % ch_size) for i in range(ch_size)],
        )
        for shift in range(1, ch_size)
    ]
    mix_own = jnp.take(mix_pieces, ch_index, axis=1)
    pooled_sum = jnp.dot(fine_pixels, pool_kernel, preferred_element_type=f32)
    for fine_other, kernel_other in zip(fine_others, kernel_others):
        pooled_sum = pooled_sum + jnp.dot(fine_other, kernel_other, preferred_element_type=f32)
    pooled_all = pooled_sum.astype(bf16)
    pooled = lax.dynamic_slice_in_dim(pooled_all, ch_index * half_width, half_width, axis=1)
    upstream = ch_assemble(cotangent, cot_others, axis=1)
    projected = jnp.einsum(
        "rc,kcd->rkd", pooled_all, projections, preferred_element_type=f32
    ).astype(bf16)
    queries = projected[:, 0]
    key_value = projected[:, 1:]
    outgoing = (
        jnp.dot(send_pick, key_value.reshape(row_count, 2 * half_width), preferred_element_type=f32)
        .astype(bf16)
        .reshape(peer_count, slot_count, 2, half_width)
    )
    incoming = lax.all_to_all(outgoing, "pix", split_axis=0, concat_axis=0, tiled=True)
    extended = jnp.concatenate(
        [key_value, incoming.reshape(peer_count * slot_count, 2, half_width)], axis=0
    )
    attended, prob_blocks, kv_blocks = attention_forward(queries, extended, neighbours, 0)
    attended_others = ch_exchange(attended)
    grad_attended = jnp.dot(upstream, mixing_weight.T, preferred_element_type=f32).astype(bf16)
    grad_attended, proj_others = lax.optimization_barrier((grad_attended, proj_others))
    mixing_term = jnp.dot(attended.T, upstream, preferred_element_type=f32) * grad_scale
    carried, query_grads, (attended_others, mix_others) = attention_backward(
        queries, extended.shape[0], neighbours, 0, grad_attended, prob_blocks, kv_blocks,
        (attended_others, mix_others),
    )
    branch = jnp.dot(attended, mix_own, preferred_element_type=f32)
    for attended_other, mix_other in zip(attended_others, mix_others):
        branch = branch + jnp.dot(attended_other, mix_other, preferred_element_type=f32)
    section_output = (pooled.astype(f32) + branch).astype(bf16)
    remote_grads = carried[row_count:].reshape(peer_count, slot_count, 2, half_width)
    returned = lax.all_to_all(remote_grads, "pix", split_axis=0, concat_axis=0, tiled=True)
    returned_rows = jnp.einsum(
        "px,pc->xc",
        send_pick,
        returned.reshape(peer_count * slot_count, 2 * half_width).astype(bf16),
        preferred_element_type=f32,
    )
    local_grads = carried[:row_count] + returned_rows.reshape(row_count, 2, half_width)
    grad_projected = jnp.concatenate(
        [query_grads.reshape(row_count, 1, half_width), local_grads], axis=1
    ).astype(bf16)
    grad_others = ch_exchange(grad_projected)
    projection_term = (
        jnp.einsum("rc,rkd->kcd", pooled_all, grad_projected, preferred_element_type=f32)
        * grad_scale
    )
    pooled_sum = upstream.astype(f32) + jnp.einsum(
        "rkd,kcd->rc", grad_projected, projections, preferred_element_type=f32
    )
    for grad_other, proj_other in zip(grad_others, proj_others):
        pooled_sum = pooled_sum + jnp.einsum(
            "rkd,kcd->rc", grad_other, proj_other, preferred_element_type=f32
        )
    grad_pooled = pooled_sum.astype(bf16)
    kernel_term = jnp.dot(fine_pixels.T, grad_pooled, preferred_element_type=f32) * grad_scale
    fine_gradient = jnp.dot(grad_pooled, pool_kernel.T, preferred_element_type=f32).astype(bf16)
    kernel_gradient, projection_gradient, mixing_gradient = pix_sum(
        (kernel_term, projection_term, mixing_term)
    )
    return (section_output, fine_gradient, kernel_gradient, projection_gradient, mixing_gradient)


def solution(mesh):
    placed = (
        P("pix", "ch"),
        P("ch", None),
        P(None, None, "ch"),
        P("ch", None),
        P("pix", None),
        P("pix", None),
        P("pix", "ch"),
    )
    return jax.shard_map(
        per_device,
        mesh=mesh,
        in_specs=placed,
        out_specs=(
            P("pix", "ch"),
            P("pix", "ch"),
            P("ch", None),
            P(None, None, "ch"),
            P("ch", None),
        ),
        check_vma=False,
    )
```

```python
import math

import jax
import jax.numpy as jnp
from jax import lax
from jax.sharding import PartitionSpec as P

HD = 64


def pick_table(row_ids, total):
    return (row_ids[:, None] == jnp.arange(total, dtype=jnp.int32)[None, :]).astype(jnp.bfloat16)


def slot_index(neighbour_block, first_row, block_rows):
    present = neighbour_block >= 0
    own_rows = first_row + jnp.arange(block_rows, dtype=jnp.int32)
    slot_rows = jnp.concatenate([own_rows[:, None], jnp.where(present, neighbour_block, 0)], axis=1)
    slot_live = jnp.concatenate([jnp.ones((block_rows, 1), bool), present], axis=1)
    return (slot_rows, slot_live)


def attention_forward(queries, extended, neighbours, row_offset):
    f32 = jnp.float32
    bf16 = jnp.bfloat16
    row_count = queries.shape[0]
    span = queries.shape[1]
    ext_rows = extended.shape[0]
    heads_here = span // HD
    slot_width = neighbours.shape[1] + 1
    score_scale = 1.0 / math.sqrt(HD)
    block_rows = math.gcd(row_count, 512)
    block_count = row_count // block_rows
    block_starts = row_offset + jnp.arange(block_count, dtype=jnp.int32) * block_rows
    query_blocks = queries.reshape(block_count, block_rows, span)
    neighbour_blocks = neighbours.reshape(block_count, block_rows, slot_width - 1)
    flattened = extended.reshape(ext_rows, 2 * span)

    def forward_block(inputs):
        query_block, neighbour_block, first_row = inputs
        slot_rows, slot_live = slot_index(neighbour_block, first_row, block_rows)
        pieces = [
            jnp.dot(
                pick_table(slot_rows[:, slot], ext_rows), flattened, preferred_element_type=f32
            ).astype(bf16)
            for slot in range(slot_width)
        ]
        gathered = jnp.stack(pieces, axis=1).reshape(block_rows, slot_width, 2, span)
        block_keys = gathered[:, :, 0].reshape(block_rows, slot_width, heads_here, HD)
        block_values = gathered[:, :, 1].reshape(block_rows, slot_width, heads_here, HD)
        scores = (
            jnp.einsum(
                "bhd,bmhd->bhm",
                query_block.reshape(block_rows, heads_here, HD),
                block_keys,
                preferred_element_type=f32,
            )
            * score_scale
        )
        shut = slot_live[:, None, :]
        masked = jnp.where(shut, scores, -1e30)
        largest = jnp.max(masked, axis=2, keepdims=True)
        raised = jnp.where(shut, jnp.exp(masked - largest), 0.0)
        probabilities = raised / jnp.sum(raised, axis=2, keepdims=True)
        weights = probabilities.astype(bf16)
        mixture = jnp.einsum("bhm,bmhd->bhd", weights, block_values, preferred_element_type=f32)
        return (mixture.reshape(block_rows, span).astype(bf16), probabilities, gathered)

    outputs = [
        forward_block((query_blocks[b], neighbour_blocks[b], block_starts[b]))
        for b in range(block_count)
    ]
    attn_blocks = jnp.stack([out[0] for out in outputs])
    prob_blocks = [out[1] for out in outputs]
    kv_blocks = [out[2] for out in outputs]
    return (attn_blocks.reshape(row_count, span), prob_blocks, kv_blocks)


def attention_backward(
    queries, ext_rows, neighbours, row_offset, grad_attended, prob_blocks, kv_blocks, riders
):
    f32 = jnp.float32
    bf16 = jnp.bfloat16
    row_count = queries.shape[0]
    span = queries.shape[1]
    heads_here = span // HD
    slot_width = neighbours.shape[1] + 1
    score_scale = 1.0 / math.sqrt(HD)
    block_rows = math.gcd(row_count, 512)
    block_count = row_count // block_rows
    block_starts = row_offset + jnp.arange(block_count, dtype=jnp.int32) * block_rows
    query_blocks = queries.reshape(block_count, block_rows, span)
    neighbour_blocks = neighbours.reshape(block_count, block_rows, slot_width - 1)
    grad_blocks = grad_attended.reshape(block_count, block_rows, span)

    def backward_block(carried, inputs):
        query_block, neighbour_block, first_row, grad_block, probabilities, gathered = inputs
        slot_rows, slot_live = slot_index(neighbour_block, first_row, block_rows)
        block_keys = gathered[:, :, 0].reshape(block_rows, slot_width, heads_here, HD).astype(f32)
        block_values = gathered[:, :, 1].reshape(block_rows, slot_width, heads_here, HD).astype(f32)
        grad_mix = grad_block.reshape(block_rows, heads_here, HD).astype(f32)
        grad_weights = jnp.einsum("bhd,bmhd->bhm", grad_mix, block_values)
        grad_scores = (
            probabilities
            * (grad_weights - jnp.sum(probabilities * grad_weights, axis=2, keepdims=True))
            * score_scale
        )
        grad_query = jnp.einsum("bhm,bmhd->bhd", grad_scores, block_keys).reshape(block_rows, span)
        query_wide = query_block.reshape(block_rows, heads_here, HD).astype(f32)
        grad_keys = jnp.einsum("bhm,bhd->bmhd", grad_scores, query_wide)
        rounded = lax.optimization_barrier(probabilities.astype(bf16))
        grad_values = jnp.einsum("bhm,bhd->bmhd", rounded.astype(f32), grad_mix)
        contribution = (
            jnp.stack([grad_keys, grad_values], axis=2)
            .reshape(block_rows, slot_width, 2 * span)
            .astype(bf16)
        )
        for slot in range(slot_width):
            carried = carried + jnp.einsum(
                "bx,bc->xc",
                pick_table(slot_rows[:, slot], ext_rows),
                contribution[:, slot],
                preferred_element_type=f32,
            )
        return (carried, grad_query)

    carried = jnp.zeros((ext_rows, 2 * span), f32)
    query_grads = []
    for b in range(block_count):
        carried, grad_query = backward_block(
            carried,
            (query_blocks[b], neighbour_blocks[b], block_starts[b], grad_blocks[b],
             prob_blocks[b], kv_blocks[b]),
        )
        query_grads.append(grad_query)
        if b == 0:
            carried, riders = lax.optimization_barrier((carried, riders))
    query_grads = jnp.stack(query_grads)
    return (carried.reshape(ext_rows, 2, span), query_grads.reshape(row_count, span), riders)


def ch_exchange(value):
    size = lax.axis_size("ch")
    return [
        lax.ppermute(value, "ch", [(i, (i + shift) % size) for i in range(size)])
        for shift in range(1, size)
    ]


def ch_assemble(own, others, axis):
    size = len(others) + 1
    index = lax.axis_index("ch")
    pieces = [own] + others
    result = None
    for case in range(size):
        ordered = jnp.concatenate([pieces[(case - j) % size] for j in range(size)], axis=axis)
        result = ordered if result is None else jnp.where(index == case, ordered, result)
    return result


def pix_scatter(terms, width):
    size = lax.axis_size("pix")
    flat = jnp.concatenate([term.reshape(-1, width) for term in terms], axis=0)
    rows = flat.shape[0]
    chunk = -(-rows // size)
    flat = jnp.pad(flat, ((0, chunk * size - rows), (0, 0)))
    parts = lax.all_to_all(flat.reshape(size, chunk, width), "pix", 0, 0, tiled=True)
    return jnp.sum(parts, axis=0)


def pix_gather(reduced_groups, term_groups):
    size = lax.axis_size("pix")
    width = reduced_groups[0].shape[-1]
    joined = jnp.concatenate(reduced_groups, axis=0)
    spread = jnp.broadcast_to(joined[None], (size,) + joined.shape)
    gathered = lax.all_to_all(spread, "pix", 0, 0, tiled=True)
    results = []
    offset = 0
    for reduced, terms in zip(reduced_groups, term_groups):
        chunk = reduced.shape[0]
        flat = gathered[:, offset : offset + chunk].reshape(size * chunk, width)
        offset += chunk
        row = 0
        for term in terms:
            count = term.size // width
            results.append(flat[row : row + count].reshape(term.shape))
            row += count
    return results


def per_device(
    fine_pixels, pool_kernel, projections, mixing_weight, send_list, neighbours, cotangent
):
    f32 = jnp.float32
    bf16 = jnp.bfloat16
    row_count = fine_pixels.shape[0]
    half_width = projections.shape[2]
    ch_size = lax.axis_size("ch")
    ch_index = lax.axis_index("ch")
    peer_count = lax.axis_size("pix")
    slot_count = send_list.shape[1]
    grad_scale = 1.0 / math.sqrt(row_count * peer_count)
    send_pick = pick_table(send_list.reshape(-1), row_count)
    fine_others = ch_exchange(fine_pixels)
    kernel_others = ch_exchange(pool_kernel)
    pooled_sum = jnp.dot(fine_pixels, pool_kernel, preferred_element_type=f32)
    for fine_other, kernel_other in zip(fine_others, kernel_others):
        pooled_sum = pooled_sum + jnp.dot(fine_other, kernel_other, preferred_element_type=f32)
    pooled_all = pooled_sum.astype(bf16)
    mix_pieces = mixing_weight.reshape(mixing_weight.shape[0], ch_size, half_width)
    mix_sends = [
        jnp.take(mix_pieces, (ch_index + shift) % ch_size, axis=1) for shift in range(1, ch_size)
    ]
    pooled_all, cot_send, proj_send, mix_sends = lax.optimization_barrier(
        (pooled_all, cotangent, projections, mix_sends)
    )
    cot_others = ch_exchange(cot_send)
    proj_others = ch_exchange(proj_send)
    mix_others = [
        lax.ppermute(mix_send, "ch", [(i, (i + shift) % ch_size) for i in range(ch_size)])
        for shift, mix_send in zip(range(1, ch_size), mix_sends)
    ]
    mix_own = jnp.take(mix_pieces, ch_index, axis=1)
    pooled = lax.dynamic_slice_in_dim(pooled_all, ch_index * half_width, half_width, axis=1)
    upstream = ch_assemble(cotangent, cot_others, axis=1)
    projected = jnp.einsum(
        "rc,kcd->rkd", pooled_all, projections, preferred_element_type=f32
    ).astype(bf16)
    queries = projected[:, 0]
    key_value = projected[:, 1:]
    outgoing = (
        jnp.dot(send_pick, key_value.reshape(row_count, 2 * half_width), preferred_element_type=f32)
        .astype(bf16)
        .reshape(peer_count, slot_count, 2, half_width)
    )
    incoming = lax.all_to_all(outgoing, "pix", split_axis=0, concat_axis=0, tiled=True)
    extended = jnp.concatenate(
        [key_value, incoming.reshape(peer_count * slot_count, 2, half_width)], axis=0
    )
    attended, prob_blocks, kv_blocks = attention_forward(queries, extended, neighbours, 0)
    attended_others = ch_exchange(attended)
    grad_attended = jnp.dot(upstream, mixing_weight.T, preferred_element_type=f32).astype(bf16)
    grad_attended, proj_others = lax.optimization_barrier((grad_attended, proj_others))
    mixing_term = jnp.dot(attended.T, upstream, preferred_element_type=f32) * grad_scale
    carried, query_grads, (attended_others, mix_others) = attention_backward(
        queries, extended.shape[0], neighbours, 0, grad_attended, prob_blocks, kv_blocks,
        (attended_others, mix_others),
    )
    branch = jnp.dot(attended, mix_own, preferred_element_type=f32)
    for attended_other, mix_other in zip(attended_others, mix_others):
        branch = branch + jnp.dot(attended_other, mix_other, preferred_element_type=f32)
    section_output = (pooled.astype(f32) + branch).astype(bf16)
    remote_grads = carried[row_count:].reshape(peer_count, slot_count, 2, half_width)
    returned = lax.all_to_all(remote_grads, "pix", split_axis=0, concat_axis=0, tiled=True)
    returned_rows = jnp.einsum(
        "px,pc->xc",
        send_pick,
        returned.reshape(peer_count * slot_count, 2 * half_width).astype(bf16),
        preferred_element_type=f32,
    )
    local_grads = carried[:row_count] + returned_rows.reshape(row_count, 2, half_width)
    grad_projected = jnp.concatenate(
        [query_grads.reshape(row_count, 1, half_width), local_grads], axis=1
    ).astype(bf16)
    grad_others = ch_exchange(grad_projected)
    projection_term = (
        jnp.einsum("rc,rkd->kcd", pooled_all, grad_projected, preferred_element_type=f32)
        * grad_scale
    )
    early_reduced = pix_scatter((projection_term, mixing_term), mixing_weight.shape[1])
    early_reduced, grad_others = lax.optimization_barrier((early_reduced, grad_others))
    pooled_sum = upstream.astype(f32) + jnp.einsum(
        "rkd,kcd->rc", grad_projected, projections, preferred_element_type=f32
    )
    for grad_other, proj_other in zip(grad_others, proj_others):
        pooled_sum = pooled_sum + jnp.einsum(
            "rkd,kcd->rc", grad_other, proj_other, preferred_element_type=f32
        )
    grad_pooled = pooled_sum.astype(bf16)
    kernel_term = jnp.dot(fine_pixels.T, grad_pooled, preferred_element_type=f32) * grad_scale
    fine_gradient = jnp.dot(grad_pooled, pool_kernel.T, preferred_element_type=f32).astype(bf16)
    kernel_reduced = pix_scatter((kernel_term,), mixing_weight.shape[1])
    projection_gradient, mixing_gradient, kernel_gradient = pix_gather(
        (early_reduced, kernel_reduced), ((projection_term, mixing_term), (kernel_term,))
    )
    return (section_output, fine_gradient, kernel_gradient, projection_gradient, mixing_gradient)


def solution(mesh):
    placed = (
        P("pix", "ch"),
        P("ch", None),
        P(None, None, "ch"),
        P("ch", None),
        P("pix", None),
        P("pix", None),
        P("pix", "ch"),
    )
    return jax.shard_map(
        per_device,
        mesh=mesh,
        in_specs=placed,
        out_specs=(
            P("pix", "ch"),
            P("pix", "ch"),
            P("ch", None),
            P(None, None, "ch"),
            P("ch", None),
        ),
        check_vma=False,
    )
```

```python
import math

import jax
import jax.numpy as jnp
from jax import lax
from jax.sharding import PartitionSpec as P

HD = 64


def pick_table(row_ids, total):
    return (row_ids[:, None] == jnp.arange(total, dtype=jnp.int32)[None, :]).astype(jnp.bfloat16)


def slot_index(neighbour_block, first_row, block_rows):
    present = neighbour_block >= 0
    own_rows = first_row + jnp.arange(block_rows, dtype=jnp.int32)
    slot_rows = jnp.concatenate([own_rows[:, None], jnp.where(present, neighbour_block, 0)], axis=1)
    slot_live = jnp.concatenate([jnp.ones((block_rows, 1), bool), present], axis=1)
    return (slot_rows, slot_live)


def attention_forward(queries, extended, neighbours, row_offset):
    f32 = jnp.float32
    bf16 = jnp.bfloat16
    row_count = queries.shape[0]
    span = queries.shape[1]
    ext_rows = extended.shape[0]
    heads_here = span // HD
    slot_width = neighbours.shape[1] + 1
    score_scale = 1.0 / math.sqrt(HD)
    block_rows = math.gcd(row_count, 512)
    block_count = row_count // block_rows
    block_starts = row_offset + jnp.arange(block_count, dtype=jnp.int32) * block_rows
    query_blocks = queries.reshape(block_count, block_rows, span)
    neighbour_blocks = neighbours.reshape(block_count, block_rows, slot_width - 1)
    flattened = extended.reshape(ext_rows, 2 * span)

    def forward_block(inputs):
        query_block, neighbour_block, first_row = inputs
        slot_rows, slot_live = slot_index(neighbour_block, first_row, block_rows)
        pieces = [
            jnp.dot(
                pick_table(slot_rows[:, slot], ext_rows), flattened, preferred_element_type=f32
            ).astype(bf16)
            for slot in range(slot_width)
        ]
        gathered = jnp.stack(pieces, axis=1).reshape(block_rows, slot_width, 2, span)
        block_keys = gathered[:, :, 0].reshape(block_rows, slot_width, heads_here, HD)
        block_values = gathered[:, :, 1].reshape(block_rows, slot_width, heads_here, HD)
        scores = (
            jnp.einsum(
                "bhd,bmhd->bhm",
                query_block.reshape(block_rows, heads_here, HD),
                block_keys,
                preferred_element_type=f32,
            )
            * score_scale
        )
        shut = slot_live[:, None, :]
        masked = jnp.where(shut, scores, -1e30)
        largest = jnp.max(masked, axis=2, keepdims=True)
        raised = jnp.where(shut, jnp.exp(masked - largest), 0.0)
        probabilities = raised / jnp.sum(raised, axis=2, keepdims=True)
        weights = probabilities.astype(bf16)
        mixture = jnp.einsum("bhm,bmhd->bhd", weights, block_values, preferred_element_type=f32)
        return (mixture.reshape(block_rows, span).astype(bf16), probabilities, gathered)

    outputs = [
        forward_block((query_blocks[b], neighbour_blocks[b], block_starts[b]))
        for b in range(block_count)
    ]
    attn_blocks = jnp.stack([out[0] for out in outputs])
    prob_blocks = [out[1] for out in outputs]
    kv_blocks = [out[2] for out in outputs]
    return (attn_blocks.reshape(row_count, span), prob_blocks, kv_blocks)


def attention_backward(
    queries, ext_rows, neighbours, row_offset, grad_attended, prob_blocks, kv_blocks, riders
):
    f32 = jnp.float32
    bf16 = jnp.bfloat16
    row_count = queries.shape[0]
    span = queries.shape[1]
    heads_here = span // HD
    slot_width = neighbours.shape[1] + 1
    score_scale = 1.0 / math.sqrt(HD)
    block_rows = math.gcd(row_count, 512)
    block_count = row_count // block_rows
    block_starts = row_offset + jnp.arange(block_count, dtype=jnp.int32) * block_rows
    query_blocks = queries.reshape(block_count, block_rows, span)
    neighbour_blocks = neighbours.reshape(block_count, block_rows, slot_width - 1)
    grad_blocks = grad_attended.reshape(block_count, block_rows, span)

    def backward_block(carried, inputs):
        query_block, neighbour_block, first_row, grad_block, probabilities, gathered = inputs
        slot_rows, slot_live = slot_index(neighbour_block, first_row, block_rows)
        block_keys = gathered[:, :, 0].reshape(block_rows, slot_width, heads_here, HD).astype(f32)
        block_values = gathered[:, :, 1].reshape(block_rows, slot_width, heads_here, HD).astype(f32)
        grad_mix = grad_block.reshape(block_rows, heads_here, HD).astype(f32)
        grad_weights = jnp.einsum("bhd,bmhd->bhm", grad_mix, block_values)
        grad_scores = (
            probabilities
            * (grad_weights - jnp.sum(probabilities * grad_weights, axis=2, keepdims=True))
            * score_scale
        )
        grad_query = jnp.einsum("bhm,bmhd->bhd", grad_scores, block_keys).reshape(block_rows, span)
        query_wide = query_block.reshape(block_rows, heads_here, HD).astype(f32)
        grad_keys = jnp.einsum("bhm,bhd->bmhd", grad_scores, query_wide)
        rounded = lax.optimization_barrier(probabilities.astype(bf16))
        grad_values = jnp.einsum("bhm,bhd->bmhd", rounded.astype(f32), grad_mix)
        contribution = (
            jnp.stack([grad_keys, grad_values], axis=2)
            .reshape(block_rows, slot_width, 2 * span)
            .astype(bf16)
        )
        for slot in range(slot_width):
            carried = carried + jnp.einsum(
                "bx,bc->xc",
                pick_table(slot_rows[:, slot], ext_rows),
                contribution[:, slot],
                preferred_element_type=f32,
            )
        return (carried, grad_query)

    carried = jnp.zeros((ext_rows, 2 * span), f32)
    query_grads = []
    for b in range(block_count):
        carried, grad_query = backward_block(
            carried,
            (query_blocks[b], neighbour_blocks[b], block_starts[b], grad_blocks[b],
             prob_blocks[b], kv_blocks[b]),
        )
        query_grads.append(grad_query)
        if b == 0:
            carried, riders = lax.optimization_barrier((carried, riders))
    query_grads = jnp.stack(query_grads)
    return (carried.reshape(ext_rows, 2, span), query_grads.reshape(row_count, span), riders)


def ch_exchange(value):
    size = lax.axis_size("ch")
    return [
        lax.ppermute(value, "ch", [(i, (i + shift) % size) for i in range(size)])
        for shift in range(1, size)
    ]


def ch_assemble(own, others, axis):
    size = len(others) + 1
    index = lax.axis_index("ch")
    pieces = [own] + others
    result = None
    for case in range(size):
        ordered = jnp.concatenate([pieces[(case - j) % size] for j in range(size)], axis=axis)
        result = ordered if result is None else jnp.where(index == case, ordered, result)
    return result


def core_swap(value):
    size = lax.axis_size("pix")
    return lax.ppermute(value, "pix", [(i, i ^ 1) for i in range(size)])


def pix_scatter(terms, width):
    size = lax.axis_size("pix")
    core = lax.axis_index("pix") % 2
    flat = jnp.concatenate([term.reshape(-1, width) for term in terms], axis=0)
    rows = flat.shape[0]
    chunk = -(-rows // (2 * size))
    flat = jnp.pad(flat, ((0, 2 * size * chunk - rows), (0, 0)))
    halves = flat.reshape(2, size * chunk, width)
    keep = jnp.where(core == 0, halves[0], halves[1])
    send = jnp.where(core == 0, halves[1], halves[0])
    mine = keep + core_swap(send)
    parts = lax.all_to_all(mine.reshape(size, chunk, width), "pix", 0, 0, tiled=True)
    return jnp.sum(parts.reshape(size // 2, 2, chunk, width), axis=0)


def pix_gather(reduced_groups, term_groups):
    size = lax.axis_size("pix")
    core = lax.axis_index("pix") % 2
    width = reduced_groups[0].shape[-1]
    joined = jnp.concatenate(reduced_groups, axis=1)
    total = joined.shape[1]
    spread = jnp.broadcast_to(joined[None], (size // 2, 2, total, width))
    got = lax.all_to_all(spread.reshape(size, total, width), "pix", 0, 0, tiled=True)
    other = core_swap(got)
    first = jnp.where(core == 0, got, other)
    second = jnp.where(core == 0, other, got)
    results = []
    offset = 0
    for reduced, terms in zip(reduced_groups, term_groups):
        chunk = reduced.shape[1]
        flat = jnp.concatenate(
            [
                first[:, offset : offset + chunk].reshape(size * chunk, width),
                second[:, offset : offset + chunk].reshape(size * chunk, width),
            ],
            axis=0,
        )
        offset += chunk
        row = 0
        for term in terms:
            count = term.size // width
            results.append(flat[row : row + count].reshape(term.shape))
            row += count
    return results


def per_device(
    fine_pixels, pool_kernel, projections, mixing_weight, send_list, neighbours, cotangent
):
    f32 = jnp.float32
    bf16 = jnp.bfloat16
    row_count = fine_pixels.shape[0]
    half_width = projections.shape[2]
    ch_size = lax.axis_size("ch")
    ch_index = lax.axis_index("ch")
    peer_count = lax.axis_size("pix")
    slot_count = send_list.shape[1]
    grad_scale = 1.0 / math.sqrt(row_count * peer_count)
    send_pick = pick_table(send_list.reshape(-1), row_count)
    fine_others = ch_exchange(fine_pixels)
    kernel_others = ch_exchange(pool_kernel)
    pooled_sum = jnp.dot(fine_pixels, pool_kernel, preferred_element_type=f32)
    for fine_other, kernel_other in zip(fine_others, kernel_others):
        pooled_sum = pooled_sum + jnp.dot(fine_other, kernel_other, preferred_element_type=f32)
    pooled_all = pooled_sum.astype(bf16)
    mix_pieces = mixing_weight.reshape(mixing_weight.shape[0], ch_size, half_width)
    mix_sends = [
        jnp.take(mix_pieces, (ch_index + shift) % ch_size, axis=1) for shift in range(1, ch_size)
    ]
    pooled_all, cot_send, proj_send, mix_sends = lax.optimization_barrier(
        (pooled_all, cotangent, projections, mix_sends)
    )
    cot_others = ch_exchange(cot_send)
    proj_others = ch_exchange(proj_send)
    mix_others = [
        lax.ppermute(mix_send, "ch", [(i, (i + shift) % ch_size) for i in range(ch_size)])
        for shift, mix_send in zip(range(1, ch_size), mix_sends)
    ]
    mix_own = jnp.take(mix_pieces, ch_index, axis=1)
    pooled = lax.dynamic_slice_in_dim(pooled_all, ch_index * half_width, half_width, axis=1)
    upstream = ch_assemble(cotangent, cot_others, axis=1)
    projected = jnp.einsum(
        "rc,kcd->rkd", pooled_all, projections, preferred_element_type=f32
    ).astype(bf16)
    queries = projected[:, 0]
    key_value = projected[:, 1:]
    outgoing = (
        jnp.dot(send_pick, key_value.reshape(row_count, 2 * half_width), preferred_element_type=f32)
        .astype(bf16)
        .reshape(peer_count, slot_count, 2, half_width)
    )
    incoming = lax.all_to_all(outgoing, "pix", split_axis=0, concat_axis=0, tiled=True)
    extended = jnp.concatenate(
        [key_value, incoming.reshape(peer_count * slot_count, 2, half_width)], axis=0
    )
    attended, prob_blocks, kv_blocks = attention_forward(queries, extended, neighbours, 0)
    attended_others = ch_exchange(attended)
    grad_attended = jnp.dot(upstream, mixing_weight.T, preferred_element_type=f32).astype(bf16)
    grad_attended, proj_others = lax.optimization_barrier((grad_attended, proj_others))
    mixing_term = jnp.dot(attended.T, upstream, preferred_element_type=f32) * grad_scale
    carried, query_grads, (attended_others, mix_others) = attention_backward(
        queries, extended.shape[0], neighbours, 0, grad_attended, prob_blocks, kv_blocks,
        (attended_others, mix_others),
    )
    branch = jnp.dot(attended, mix_own, preferred_element_type=f32)
    for attended_other, mix_other in zip(attended_others, mix_others):
        branch = branch + jnp.dot(attended_other, mix_other, preferred_element_type=f32)
    section_output = (pooled.astype(f32) + branch).astype(bf16)
    remote_grads = carried[row_count:].reshape(peer_count, slot_count, 2, half_width)
    returned = lax.all_to_all(remote_grads, "pix", split_axis=0, concat_axis=0, tiled=True)
    returned_rows = jnp.einsum(
        "px,pc->xc",
        send_pick,
        returned.reshape(peer_count * slot_count, 2 * half_width).astype(bf16),
        preferred_element_type=f32,
    )
    local_grads = carried[:row_count] + returned_rows.reshape(row_count, 2, half_width)
    grad_projected = jnp.concatenate(
        [query_grads.reshape(row_count, 1, half_width), local_grads], axis=1
    ).astype(bf16)
    grad_others = ch_exchange(grad_projected)
    projection_term = (
        jnp.einsum("rc,rkd->kcd", pooled_all, grad_projected, preferred_element_type=f32)
        * grad_scale
    )
    early_reduced = pix_scatter((projection_term, mixing_term), mixing_weight.shape[1])
    early_reduced, grad_others = lax.optimization_barrier((early_reduced, grad_others))
    pooled_sum = upstream.astype(f32) + jnp.einsum(
        "rkd,kcd->rc", grad_projected, projections, preferred_element_type=f32
    )
    for grad_other, proj_other in zip(grad_others, proj_others):
        pooled_sum = pooled_sum + jnp.einsum(
            "rkd,kcd->rc", grad_other, proj_other, preferred_element_type=f32
        )
    grad_pooled = pooled_sum.astype(bf16)
    kernel_term = jnp.dot(fine_pixels.T, grad_pooled, preferred_element_type=f32) * grad_scale
    fine_gradient = jnp.dot(grad_pooled, pool_kernel.T, preferred_element_type=f32).astype(bf16)
    kernel_reduced = pix_scatter((kernel_term,), mixing_weight.shape[1])
    projection_gradient, mixing_gradient, kernel_gradient = pix_gather(
        (early_reduced, kernel_reduced), ((projection_term, mixing_term), (kernel_term,))
    )
    return (section_output, fine_gradient, kernel_gradient, projection_gradient, mixing_gradient)


def solution(mesh):
    placed = (
        P("pix", "ch"),
        P("ch", None),
        P(None, None, "ch"),
        P("ch", None),
        P("pix", None),
        P("pix", None),
        P("pix", "ch"),
    )
    return jax.shard_map(
        per_device,
        mesh=mesh,
        in_specs=placed,
        out_specs=(
            P("pix", "ch"),
            P("pix", "ch"),
            P("ch", None),
            P(None, None, "ch"),
            P("ch", None),
        ),
        check_vma=False,
    )
```

```python
import math

import jax
import jax.numpy as jnp
from jax import lax
from jax.sharding import PartitionSpec as P

HD = 64


def pick_table(row_ids, total):
    return (row_ids[:, None] == jnp.arange(total, dtype=jnp.int32)[None, :]).astype(jnp.bfloat16)


def slot_index(neighbour_block, first_row, block_rows):
    present = neighbour_block >= 0
    own_rows = first_row + jnp.arange(block_rows, dtype=jnp.int32)
    slot_rows = jnp.concatenate([own_rows[:, None], jnp.where(present, neighbour_block, 0)], axis=1)
    slot_live = jnp.concatenate([jnp.ones((block_rows, 1), bool), present], axis=1)
    return (slot_rows, slot_live)


def attention_forward(queries, extended, neighbours, row_offset, riders):
    f32 = jnp.float32
    bf16 = jnp.bfloat16
    row_count = queries.shape[0]
    span = queries.shape[1]
    ext_rows = extended.shape[0]
    heads_here = span // HD
    slot_width = neighbours.shape[1] + 1
    score_scale = 1.0 / math.sqrt(HD)
    block_rows = math.gcd(row_count, 512)
    block_count = row_count // block_rows
    block_starts = row_offset + jnp.arange(block_count, dtype=jnp.int32) * block_rows
    query_blocks = queries.reshape(block_count, block_rows, span)
    neighbour_blocks = neighbours.reshape(block_count, block_rows, slot_width - 1)
    flattened = extended.reshape(ext_rows, 2 * span)

    def forward_block(inputs):
        query_block, neighbour_block, first_row = inputs
        slot_rows, slot_live = slot_index(neighbour_block, first_row, block_rows)
        pieces = [
            jnp.dot(
                pick_table(slot_rows[:, slot], ext_rows), flattened, preferred_element_type=f32
            ).astype(bf16)
            for slot in range(slot_width)
        ]
        gathered = jnp.stack(pieces, axis=1).reshape(block_rows, slot_width, 2, span)
        block_keys = gathered[:, :, 0].reshape(block_rows, slot_width, heads_here, HD)
        block_values = gathered[:, :, 1].reshape(block_rows, slot_width, heads_here, HD)
        scores = (
            jnp.einsum(
                "bhd,bmhd->bhm",
                query_block.reshape(block_rows, heads_here, HD),
                block_keys,
                preferred_element_type=f32,
            )
            * score_scale
        )
        shut = slot_live[:, None, :]
        masked = jnp.where(shut, scores, -1e30)
        largest = jnp.max(masked, axis=2, keepdims=True)
        raised = jnp.where(shut, jnp.exp(masked - largest), 0.0)
        probabilities = raised / jnp.sum(raised, axis=2, keepdims=True)
        weights = probabilities.astype(bf16)
        mixture = jnp.einsum("bhm,bmhd->bhd", weights, block_values, preferred_element_type=f32)
        return (mixture.reshape(block_rows, span).astype(bf16), probabilities, gathered)

    outputs = []
    for b in range(block_count):
        out = forward_block((query_blocks[b], neighbour_blocks[b], block_starts[b]))
        if b == 0:
            out, riders = lax.optimization_barrier((out, riders))
        outputs.append(out)
    attn_blocks = jnp.stack([out[0] for out in outputs])
    prob_blocks = [out[1] for out in outputs]
    kv_blocks = [out[2] for out in outputs]
    return (attn_blocks.reshape(row_count, span), prob_blocks, kv_blocks, riders)


def attention_backward(
    queries, ext_rows, neighbours, row_offset, grad_attended, prob_blocks, kv_blocks, riders
):
    f32 = jnp.float32
    bf16 = jnp.bfloat16
    row_count = queries.shape[0]
    span = queries.shape[1]
    heads_here = span // HD
    slot_width = neighbours.shape[1] + 1
    score_scale = 1.0 / math.sqrt(HD)
    block_rows = math.gcd(row_count, 512)
    block_count = row_count // block_rows
    block_starts = row_offset + jnp.arange(block_count, dtype=jnp.int32) * block_rows
    query_blocks = queries.reshape(block_count, block_rows, span)
    neighbour_blocks = neighbours.reshape(block_count, block_rows, slot_width - 1)
    grad_blocks = grad_attended.reshape(block_count, block_rows, span)

    def backward_block(carried, inputs):
        query_block, neighbour_block, first_row, grad_block, probabilities, gathered = inputs
        slot_rows, slot_live = slot_index(neighbour_block, first_row, block_rows)
        block_keys = gathered[:, :, 0].reshape(block_rows, slot_width, heads_here, HD).astype(f32)
        block_values = gathered[:, :, 1].reshape(block_rows, slot_width, heads_here, HD).astype(f32)
        grad_mix = grad_block.reshape(block_rows, heads_here, HD).astype(f32)
        grad_weights = jnp.einsum("bhd,bmhd->bhm", grad_mix, block_values)
        grad_scores = (
            probabilities
            * (grad_weights - jnp.sum(probabilities * grad_weights, axis=2, keepdims=True))
            * score_scale
        )
        grad_query = jnp.einsum("bhm,bmhd->bhd", grad_scores, block_keys).reshape(block_rows, span)
        query_wide = query_block.reshape(block_rows, heads_here, HD).astype(f32)
        grad_keys = jnp.einsum("bhm,bhd->bmhd", grad_scores, query_wide)
        rounded = lax.optimization_barrier(probabilities.astype(bf16))
        grad_values = jnp.einsum("bhm,bhd->bmhd", rounded.astype(f32), grad_mix)
        contribution = (
            jnp.stack([grad_keys, grad_values], axis=2)
            .reshape(block_rows, slot_width, 2 * span)
            .astype(bf16)
        )
        for slot in range(slot_width):
            carried = carried + jnp.einsum(
                "bx,bc->xc",
                pick_table(slot_rows[:, slot], ext_rows),
                contribution[:, slot],
                preferred_element_type=f32,
            )
        return (carried, grad_query)

    carried = jnp.zeros((ext_rows, 2 * span), f32)
    query_grads = []
    for b in range(block_count):
        carried, grad_query = backward_block(
            carried,
            (query_blocks[b], neighbour_blocks[b], block_starts[b], grad_blocks[b],
             prob_blocks[b], kv_blocks[b]),
        )
        query_grads.append(grad_query)
        if b == 0:
            carried, riders = lax.optimization_barrier((carried, riders))
    query_grads = jnp.stack(query_grads)
    return (carried.reshape(ext_rows, 2, span), query_grads.reshape(row_count, span), riders)


def ch_exchange(value):
    size = lax.axis_size("ch")
    return [
        lax.ppermute(value, "ch", [(i, (i + shift) % size) for i in range(size)])
        for shift in range(1, size)
    ]


def ch_assemble(own, others, axis):
    size = len(others) + 1
    index = lax.axis_index("ch")
    pieces = [own] + others
    result = None
    for case in range(size):
        ordered = jnp.concatenate([pieces[(case - j) % size] for j in range(size)], axis=axis)
        result = ordered if result is None else jnp.where(index == case, ordered, result)
    return result


def core_swap(value):
    size = lax.axis_size("pix")
    return lax.ppermute(value, "pix", [(i, i ^ 1) for i in range(size)])


def pix_scatter(terms, width):
    size = lax.axis_size("pix")
    core = lax.axis_index("pix") % 2
    flat = jnp.concatenate([term.reshape(-1, width) for term in terms], axis=0)
    rows = flat.shape[0]
    chunk = -(-rows // (2 * size))
    flat = jnp.pad(flat, ((0, 2 * size * chunk - rows), (0, 0)))
    halves = flat.reshape(2, size * chunk, width)
    keep = jnp.where(core == 0, halves[0], halves[1])
    send = jnp.where(core == 0, halves[1], halves[0])
    mine = keep + core_swap(send)
    parts = lax.all_to_all(mine.reshape(size, chunk, width), "pix", 0, 0, tiled=True)
    return jnp.sum(parts.reshape(size // 2, 2, chunk, width), axis=0)


def pix_gather(reduced_groups, term_groups):
    size = lax.axis_size("pix")
    core = lax.axis_index("pix") % 2
    width = reduced_groups[0].shape[-1]
    joined = jnp.concatenate(reduced_groups, axis=1)
    total = joined.shape[1]
    spread = jnp.broadcast_to(joined[None], (size // 2, 2, total, width))
    got = lax.all_to_all(spread.reshape(size, total, width), "pix", 0, 0, tiled=True)
    other = core_swap(got)
    first = jnp.where(core == 0, got, other)
    second = jnp.where(core == 0, other, got)
    results = []
    offset = 0
    for reduced, terms in zip(reduced_groups, term_groups):
        chunk = reduced.shape[1]
        flat = jnp.concatenate(
            [
                first[:, offset : offset + chunk].reshape(size * chunk, width),
                second[:, offset : offset + chunk].reshape(size * chunk, width),
            ],
            axis=0,
        )
        offset += chunk
        row = 0
        for term in terms:
            count = term.size // width
            results.append(flat[row : row + count].reshape(term.shape))
            row += count
    return results


def per_device(
    fine_pixels, pool_kernel, projections, mixing_weight, send_list, neighbours, cotangent
):
    f32 = jnp.float32
    bf16 = jnp.bfloat16
    row_count = fine_pixels.shape[0]
    half_width = projections.shape[2]
    ch_size = lax.axis_size("ch")
    ch_index = lax.axis_index("ch")
    peer_count = lax.axis_size("pix")
    slot_count = send_list.shape[1]
    grad_scale = 1.0 / math.sqrt(row_count * peer_count)
    send_pick = pick_table(send_list.reshape(-1), row_count)
    fine_others = ch_exchange(fine_pixels)
    kernel_others = ch_exchange(pool_kernel)
    pooled_sum = jnp.dot(fine_pixels, pool_kernel, preferred_element_type=f32)
    for fine_other, kernel_other in zip(fine_others, kernel_others):
        pooled_sum = pooled_sum + jnp.dot(fine_other, kernel_other, preferred_element_type=f32)
    pooled_all = pooled_sum.astype(bf16)
    mix_pieces = mixing_weight.reshape(mixing_weight.shape[0], ch_size, half_width)
    mix_sends = [
        jnp.take(mix_pieces, (ch_index + shift) % ch_size, axis=1) for shift in range(1, ch_size)
    ]
    pooled_all, cot_send, proj_send, mix_sends = lax.optimization_barrier(
        (pooled_all, cotangent, projections, mix_sends)
    )
    cot_others = ch_exchange(cot_send)
    proj_others = ch_exchange(proj_send)
    mix_others = [
        lax.ppermute(mix_send, "ch", [(i, (i + shift) % ch_size) for i in range(ch_size)])
        for shift, mix_send in zip(range(1, ch_size), mix_sends)
    ]
    mix_own = jnp.take(mix_pieces, ch_index, axis=1)
    pooled = lax.dynamic_slice_in_dim(pooled_all, ch_index * half_width, half_width, axis=1)
    projected = jnp.einsum(
        "rc,kcd->rkd", pooled_all, projections, preferred_element_type=f32
    ).astype(bf16)
    queries = projected[:, 0]
    key_value = projected[:, 1:]
    outgoing = (
        jnp.dot(send_pick, key_value.reshape(row_count, 2 * half_width), preferred_element_type=f32)
        .astype(bf16)
        .reshape(peer_count, slot_count, 2, half_width)
    )
    incoming = lax.all_to_all(outgoing, "pix", split_axis=0, concat_axis=0, tiled=True)
    extended = jnp.concatenate(
        [key_value, incoming.reshape(peer_count * slot_count, 2, half_width)], axis=0
    )
    attended, prob_blocks, kv_blocks, (cot_others, proj_others) = attention_forward(
        queries, extended, neighbours, 0, (cot_others, proj_others)
    )
    upstream = ch_assemble(cotangent, cot_others, axis=1)
    attended_others = ch_exchange(attended)
    grad_attended = jnp.dot(upstream, mixing_weight.T, preferred_element_type=f32).astype(bf16)
    mixing_term = jnp.dot(attended.T, upstream, preferred_element_type=f32) * grad_scale
    carried, query_grads, (attended_others, mix_others) = attention_backward(
        queries, extended.shape[0], neighbours, 0, grad_attended, prob_blocks, kv_blocks,
        (attended_others, mix_others),
    )
    branch = jnp.dot(attended, mix_own, preferred_element_type=f32)
    for attended_other, mix_other in zip(attended_others, mix_others):
        branch = branch + jnp.dot(attended_other, mix_other, preferred_element_type=f32)
    section_output = (pooled.astype(f32) + branch).astype(bf16)
    remote_grads = carried[row_count:].reshape(peer_count, slot_count, 2, half_width)
    returned = lax.all_to_all(remote_grads, "pix", split_axis=0, concat_axis=0, tiled=True)
    returned_rows = jnp.einsum(
        "px,pc->xc",
        send_pick,
        returned.reshape(peer_count * slot_count, 2 * half_width).astype(bf16),
        preferred_element_type=f32,
    )
    local_grads = carried[:row_count] + returned_rows.reshape(row_count, 2, half_width)
    grad_projected = jnp.concatenate(
        [query_grads.reshape(row_count, 1, half_width), local_grads], axis=1
    ).astype(bf16)
    grad_others = ch_exchange(grad_projected)
    projection_term = (
        jnp.einsum("rc,rkd->kcd", pooled_all, grad_projected, preferred_element_type=f32)
        * grad_scale
    )
    early_reduced = pix_scatter((projection_term, mixing_term), mixing_weight.shape[1])
    projection_gradient, mixing_gradient = pix_gather(
        (early_reduced,), ((projection_term, mixing_term),)
    )
    projection_gradient, mixing_gradient, grad_others = lax.optimization_barrier(
        (projection_gradient, mixing_gradient, grad_others)
    )
    pooled_sum = upstream.astype(f32) + jnp.einsum(
        "rkd,kcd->rc", grad_projected, projections, preferred_element_type=f32
    )
    for grad_other, proj_other in zip(grad_others, proj_others):
        pooled_sum = pooled_sum + jnp.einsum(
            "rkd,kcd->rc", grad_other, proj_other, preferred_element_type=f32
        )
    grad_pooled = pooled_sum.astype(bf16)
    kernel_term = jnp.dot(fine_pixels.T, grad_pooled, preferred_element_type=f32) * grad_scale
    fine_gradient = jnp.dot(grad_pooled, pool_kernel.T, preferred_element_type=f32).astype(bf16)
    kernel_reduced = pix_scatter((kernel_term,), mixing_weight.shape[1])
    (kernel_gradient,) = pix_gather((kernel_reduced,), ((kernel_term,),))
    return (section_output, fine_gradient, kernel_gradient, projection_gradient, mixing_gradient)


def solution(mesh):
    placed = (
        P("pix", "ch"),
        P("ch", None),
        P(None, None, "ch"),
        P("ch", None),
        P("pix", None),
        P("pix", None),
        P("pix", "ch"),
    )
    return jax.shard_map(
        per_device,
        mesh=mesh,
        in_specs=placed,
        out_specs=(
            P("pix", "ch"),
            P("pix", "ch"),
            P("ch", None),
            P(None, None, "ch"),
            P("ch", None),
        ),
        check_vma=False,
    )
```

```python
import math

import jax
import jax.numpy as jnp
from jax import lax
from jax.sharding import PartitionSpec as P

HD = 64


def pick_table(row_ids, total):
    return (row_ids[:, None] == jnp.arange(total, dtype=jnp.int32)[None, :]).astype(jnp.bfloat16)


def slot_index(neighbour_block, first_row, block_rows):
    present = neighbour_block >= 0
    own_rows = first_row + jnp.arange(block_rows, dtype=jnp.int32)
    slot_rows = jnp.concatenate([own_rows[:, None], jnp.where(present, neighbour_block, 0)], axis=1)
    slot_live = jnp.concatenate([jnp.ones((block_rows, 1), bool), present], axis=1)
    return (slot_rows, slot_live)


def attention_forward(queries, extended, neighbours, row_offset, riders):
    f32 = jnp.float32
    bf16 = jnp.bfloat16
    row_count = queries.shape[0]
    span = queries.shape[1]
    ext_rows = extended.shape[0]
    heads_here = span // HD
    slot_width = neighbours.shape[1] + 1
    score_scale = 1.0 / math.sqrt(HD)
    block_rows = math.gcd(row_count, 512)
    block_count = row_count // block_rows
    block_starts = row_offset + jnp.arange(block_count, dtype=jnp.int32) * block_rows
    query_blocks = queries.reshape(block_count, block_rows, span)
    neighbour_blocks = neighbours.reshape(block_count, block_rows, slot_width - 1)
    flattened = extended.reshape(ext_rows, 2 * span)

    def forward_block(inputs):
        query_block, neighbour_block, first_row = inputs
        slot_rows, slot_live = slot_index(neighbour_block, first_row, block_rows)
        pieces = [
            jnp.dot(
                pick_table(slot_rows[:, slot], ext_rows), flattened, preferred_element_type=f32
            ).astype(bf16)
            for slot in range(slot_width)
        ]
        gathered = jnp.stack(pieces, axis=1).reshape(block_rows, slot_width, 2, span)
        block_keys = gathered[:, :, 0].reshape(block_rows, slot_width, heads_here, HD)
        block_values = gathered[:, :, 1].reshape(block_rows, slot_width, heads_here, HD)
        scores = (
            jnp.einsum(
                "bhd,bmhd->bhm",
                query_block.reshape(block_rows, heads_here, HD),
                block_keys,
                preferred_element_type=f32,
            )
            * score_scale
        )
        shut = slot_live[:, None, :]
        masked = jnp.where(shut, scores, -1e30)
        largest = jnp.max(masked, axis=2, keepdims=True)
        raised = jnp.where(shut, jnp.exp(masked - largest), 0.0)
        probabilities = raised / jnp.sum(raised, axis=2, keepdims=True)
        weights = probabilities.astype(bf16)
        mixture = jnp.einsum("bhm,bmhd->bhd", weights, block_values, preferred_element_type=f32)
        return (mixture.reshape(block_rows, span).astype(bf16), probabilities, gathered)

    outputs = []
    for b in range(block_count):
        out = forward_block((query_blocks[b], neighbour_blocks[b], block_starts[b]))
        if b == 0:
            out, riders = lax.optimization_barrier((out, riders))
        outputs.append(out)
    attn_blocks = jnp.stack([out[0] for out in outputs])
    prob_blocks = [out[1] for out in outputs]
    kv_blocks = [out[2] for out in outputs]
    return (attn_blocks.reshape(row_count, span), prob_blocks, kv_blocks, riders)


def attention_backward(
    queries, ext_rows, neighbours, row_offset, grad_attended, prob_blocks, kv_blocks, riders
):
    f32 = jnp.float32
    bf16 = jnp.bfloat16
    row_count = queries.shape[0]
    span = queries.shape[1]
    heads_here = span // HD
    slot_width = neighbours.shape[1] + 1
    score_scale = 1.0 / math.sqrt(HD)
    block_rows = math.gcd(row_count, 512)
    block_count = row_count // block_rows
    block_starts = row_offset + jnp.arange(block_count, dtype=jnp.int32) * block_rows
    query_blocks = queries.reshape(block_count, block_rows, span)
    neighbour_blocks = neighbours.reshape(block_count, block_rows, slot_width - 1)
    grad_blocks = grad_attended.reshape(block_count, block_rows, span)

    def backward_block(carried, inputs):
        query_block, neighbour_block, first_row, grad_block, probabilities, gathered = inputs
        slot_rows, slot_live = slot_index(neighbour_block, first_row, block_rows)
        block_keys = gathered[:, :, 0].reshape(block_rows, slot_width, heads_here, HD).astype(f32)
        block_values = gathered[:, :, 1].reshape(block_rows, slot_width, heads_here, HD).astype(f32)
        grad_mix = grad_block.reshape(block_rows, heads_here, HD).astype(f32)
        grad_weights = jnp.einsum("bhd,bmhd->bhm", grad_mix, block_values)
        grad_scores = (
            probabilities
            * (grad_weights - jnp.sum(probabilities * grad_weights, axis=2, keepdims=True))
            * score_scale
        )
        grad_query = jnp.einsum("bhm,bmhd->bhd", grad_scores, block_keys).reshape(block_rows, span)
        query_wide = query_block.reshape(block_rows, heads_here, HD).astype(f32)
        grad_keys = jnp.einsum("bhm,bhd->bmhd", grad_scores, query_wide)
        rounded = lax.optimization_barrier(probabilities.astype(bf16))
        grad_values = jnp.einsum("bhm,bhd->bmhd", rounded.astype(f32), grad_mix)
        contribution = (
            jnp.stack([grad_keys, grad_values], axis=2)
            .reshape(block_rows, slot_width, 2 * span)
            .astype(bf16)
        )
        for slot in range(slot_width):
            carried = carried + jnp.einsum(
                "bx,bc->xc",
                pick_table(slot_rows[:, slot], ext_rows),
                contribution[:, slot],
                preferred_element_type=f32,
            )
        return (carried, grad_query)

    carried = jnp.zeros((ext_rows, 2 * span), f32)
    query_grads = []
    for b in range(block_count):
        carried, grad_query = backward_block(
            carried,
            (query_blocks[b], neighbour_blocks[b], block_starts[b], grad_blocks[b],
             prob_blocks[b], kv_blocks[b]),
        )
        query_grads.append(grad_query)
        if b == 0:
            carried, riders = lax.optimization_barrier((carried, riders))
    query_grads = jnp.stack(query_grads)
    return (carried.reshape(ext_rows, 2, span), query_grads.reshape(row_count, span), riders)


def ch_exchange(value):
    size = lax.axis_size("ch")
    return [
        lax.ppermute(value, "ch", [(i, (i + shift) % size) for i in range(size)])
        for shift in range(1, size)
    ]


def ch_assemble(own, others, axis):
    size = len(others) + 1
    index = lax.axis_index("ch")
    pieces = [own] + others
    result = None
    for case in range(size):
        ordered = jnp.concatenate([pieces[(case - j) % size] for j in range(size)], axis=axis)
        result = ordered if result is None else jnp.where(index == case, ordered, result)
    return result


def core_swap(value):
    size = lax.axis_size("pix")
    return lax.ppermute(value, "pix", [(i, i ^ 1) for i in range(size)])


def pix_scatter(terms, width):
    size = lax.axis_size("pix")
    core = lax.axis_index("pix") % 2
    flat = jnp.concatenate([term.reshape(-1, width) for term in terms], axis=0)
    rows = flat.shape[0]
    chunk = -(-rows // (2 * size))
    flat = jnp.pad(flat, ((0, 2 * size * chunk - rows), (0, 0)))
    halves = flat.reshape(2, size * chunk, width)
    keep = jnp.where(core == 0, halves[0], halves[1])
    send = jnp.where(core == 0, halves[1], halves[0])
    mine = keep + core_swap(send)
    parts = lax.all_to_all(mine.reshape(size, chunk, width), "pix", 0, 0, tiled=True)
    return jnp.sum(parts.reshape(size // 2, 2, chunk, width), axis=0)


def pix_gather(reduced_groups, term_groups):
    size = lax.axis_size("pix")
    core = lax.axis_index("pix") % 2
    width = reduced_groups[0].shape[-1]
    joined = jnp.concatenate(reduced_groups, axis=1)
    total = joined.shape[1]
    spread = jnp.broadcast_to(joined[None], (size // 2, 2, total, width))
    got = lax.all_to_all(spread.reshape(size, total, width), "pix", 0, 0, tiled=True)
    other = core_swap(got)
    first = jnp.where(core == 0, got, other)
    second = jnp.where(core == 0, other, got)
    results = []
    offset = 0
    for reduced, terms in zip(reduced_groups, term_groups):
        chunk = reduced.shape[1]
        flat = jnp.concatenate(
            [
                first[:, offset : offset + chunk].reshape(size * chunk, width),
                second[:, offset : offset + chunk].reshape(size * chunk, width),
            ],
            axis=0,
        )
        offset += chunk
        row = 0
        for term in terms:
            count = term.size // width
            results.append(flat[row : row + count].reshape(term.shape))
            row += count
    return results


def per_device(
    fine_pixels, pool_kernel, projections, mixing_weight, send_list, neighbours, cotangent
):
    f32 = jnp.float32
    bf16 = jnp.bfloat16
    row_count = fine_pixels.shape[0]
    half_width = projections.shape[2]
    ch_size = lax.axis_size("ch")
    ch_index = lax.axis_index("ch")
    peer_count = lax.axis_size("pix")
    slot_count = send_list.shape[1]
    grad_scale = 1.0 / math.sqrt(row_count * peer_count)
    send_pick = pick_table(send_list.reshape(-1), row_count)
    fine_others = ch_exchange(fine_pixels)
    kernel_others = ch_exchange(pool_kernel)
    pooled_sum = jnp.dot(fine_pixels, pool_kernel, preferred_element_type=f32)
    for fine_other, kernel_other in zip(fine_others, kernel_others):
        pooled_sum = pooled_sum + jnp.dot(fine_other, kernel_other, preferred_element_type=f32)
    pooled_all = pooled_sum.astype(bf16)
    mix_pieces = mixing_weight.reshape(mixing_weight.shape[0], ch_size, half_width)
    mix_sends = [
        jnp.take(mix_pieces, (ch_index + shift) % ch_size, axis=1) for shift in range(1, ch_size)
    ]
    pooled_all, cot_send, proj_send, mix_sends = lax.optimization_barrier(
        (pooled_all, cotangent, projections, mix_sends)
    )
    cot_others = ch_exchange(cot_send)
    proj_others = ch_exchange(proj_send)
    mix_others = [
        lax.ppermute(mix_send, "ch", [(i, (i + shift) % ch_size) for i in range(ch_size)])
        for shift, mix_send in zip(range(1, ch_size), mix_sends)
    ]
    mix_own = jnp.take(mix_pieces, ch_index, axis=1)
    pooled = lax.dynamic_slice_in_dim(pooled_all, ch_index * half_width, half_width, axis=1)
    projected = jnp.einsum(
        "rc,kcd->rkd", pooled_all, projections, preferred_element_type=f32
    ).astype(bf16)
    queries = projected[:, 0]
    key_value = projected[:, 1:]
    outgoing = (
        jnp.dot(send_pick, key_value.reshape(row_count, 2 * half_width), preferred_element_type=f32)
        .astype(bf16)
        .reshape(peer_count, slot_count, 2, half_width)
    )
    incoming = lax.all_to_all(outgoing, "pix", split_axis=0, concat_axis=0, tiled=True)
    extended = jnp.concatenate(
        [key_value, incoming.reshape(peer_count * slot_count, 2, half_width)], axis=0
    )
    attended, prob_blocks, kv_blocks, (cot_others, proj_others) = attention_forward(
        queries, extended, neighbours, 0, (cot_others, proj_others)
    )
    upstream = ch_assemble(cotangent, cot_others, axis=1)
    attended_others = ch_exchange(attended)
    grad_attended = jnp.dot(upstream, mixing_weight.T, preferred_element_type=f32).astype(bf16)
    mixing_term = jnp.dot(attended.T, upstream, preferred_element_type=f32) * grad_scale
    carried, query_grads, (attended_others, mix_others) = attention_backward(
        queries, extended.shape[0], neighbours, 0, grad_attended, prob_blocks, kv_blocks,
        (attended_others, mix_others),
    )
    branch = jnp.dot(attended, mix_own, preferred_element_type=f32)
    for attended_other, mix_other in zip(attended_others, mix_others):
        branch = branch + jnp.dot(attended_other, mix_other, preferred_element_type=f32)
    section_output = (pooled.astype(f32) + branch).astype(bf16)
    remote_grads = carried[row_count:].reshape(peer_count, slot_count, 2, half_width)
    returned = lax.all_to_all(remote_grads, "pix", split_axis=0, concat_axis=0, tiled=True)
    returned_rows = jnp.einsum(
        "px,pc->xc",
        send_pick,
        returned.reshape(peer_count * slot_count, 2 * half_width).astype(bf16),
        preferred_element_type=f32,
    )
    local_grads = carried[:row_count] + returned_rows.reshape(row_count, 2, half_width)
    grad_projected = jnp.concatenate(
        [query_grads.reshape(row_count, 1, half_width), local_grads], axis=1
    ).astype(bf16)
    grad_others = ch_exchange(grad_projected)
    projection_term = (
        jnp.einsum("rc,rkd->kcd", pooled_all, grad_projected, preferred_element_type=f32)
        * grad_scale
    )
    early_reduced = pix_scatter((projection_term, mixing_term), mixing_weight.shape[1])
    early_reduced, grad_others = lax.optimization_barrier((early_reduced, grad_others))
    pooled_sum = upstream.astype(f32) + jnp.einsum(
        "rkd,kcd->rc", grad_projected, projections, preferred_element_type=f32
    )
    for grad_other, proj_other in zip(grad_others, proj_others):
        pooled_sum = pooled_sum + jnp.einsum(
            "rkd,kcd->rc", grad_other, proj_other, preferred_element_type=f32
        )
    grad_pooled = pooled_sum.astype(bf16)
    kernel_term = jnp.dot(fine_pixels.T, grad_pooled, preferred_element_type=f32) * grad_scale
    fine_gradient = jnp.dot(grad_pooled, pool_kernel.T, preferred_element_type=f32).astype(bf16)
    kernel_reduced = pix_scatter((kernel_term,), mixing_weight.shape[1])
    projection_gradient, mixing_gradient, kernel_gradient = pix_gather(
        (early_reduced, kernel_reduced), ((projection_term, mixing_term), (kernel_term,))
    )
    return (section_output, fine_gradient, kernel_gradient, projection_gradient, mixing_gradient)


def solution(mesh):
    placed = (
        P("pix", "ch"),
        P("ch", None),
        P(None, None, "ch"),
        P("ch", None),
        P("pix", None),
        P("pix", None),
        P("pix", "ch"),
    )
    return jax.shard_map(
        per_device,
        mesh=mesh,
        in_specs=placed,
        out_specs=(
            P("pix", "ch"),
            P("pix", "ch"),
            P("ch", None),
            P(None, None, "ch"),
            P("ch", None),
        ),
        check_vma=False,
    )
```

```python
import math

import jax
import jax.numpy as jnp
from jax import lax
from jax.sharding import PartitionSpec as P

HD = 64


def pick_table(row_ids, total):
    return (row_ids[:, None] == jnp.arange(total, dtype=jnp.int32)[None, :]).astype(jnp.bfloat16)


def slot_index(neighbour_block, first_row, block_rows):
    present = neighbour_block >= 0
    own_rows = first_row + jnp.arange(block_rows, dtype=jnp.int32)
    slot_rows = jnp.concatenate([own_rows[:, None], jnp.where(present, neighbour_block, 0)], axis=1)
    slot_live = jnp.concatenate([jnp.ones((block_rows, 1), bool), present], axis=1)
    return (slot_rows, slot_live)


def attention_forward(queries, extended, neighbours, row_offset):
    f32 = jnp.float32
    bf16 = jnp.bfloat16
    row_count = queries.shape[0]
    span = queries.shape[1]
    ext_rows = extended.shape[0]
    heads_here = span // HD
    slot_width = neighbours.shape[1] + 1
    score_scale = 1.0 / math.sqrt(HD)
    block_rows = math.gcd(row_count, 512)
    block_count = row_count // block_rows
    block_starts = row_offset + jnp.arange(block_count, dtype=jnp.int32) * block_rows
    query_blocks = queries.reshape(block_count, block_rows, span)
    neighbour_blocks = neighbours.reshape(block_count, block_rows, slot_width - 1)
    flattened = extended.reshape(ext_rows, 2 * span)

    def forward_block(inputs):
        query_block, neighbour_block, first_row = inputs
        slot_rows, slot_live = slot_index(neighbour_block, first_row, block_rows)
        pieces = [
            jnp.dot(
                pick_table(slot_rows[:, slot], ext_rows), flattened, preferred_element_type=f32
            ).astype(bf16)
            for slot in range(slot_width)
        ]
        gathered = jnp.stack(pieces, axis=1).reshape(block_rows, slot_width, 2, span)
        block_keys = gathered[:, :, 0].reshape(block_rows, slot_width, heads_here, HD)
        block_values = gathered[:, :, 1].reshape(block_rows, slot_width, heads_here, HD)
        scores = (
            jnp.einsum(
                "bhd,bmhd->bhm",
                query_block.reshape(block_rows, heads_here, HD),
                block_keys,
                preferred_element_type=f32,
            )
            * score_scale
        )
        shut = slot_live[:, None, :]
        masked = jnp.where(shut, scores, -1e30)
        largest = jnp.max(masked, axis=2, keepdims=True)
        raised = jnp.where(shut, jnp.exp(masked - largest), 0.0)
        probabilities = raised / jnp.sum(raised, axis=2, keepdims=True)
        weights = probabilities.astype(bf16)
        mixture = jnp.einsum("bhm,bmhd->bhd", weights, block_values, preferred_element_type=f32)
        return (mixture.reshape(block_rows, span).astype(bf16), probabilities, gathered)

    outputs = [
        forward_block((query_blocks[b], neighbour_blocks[b], block_starts[b]))
        for b in range(block_count)
    ]
    attn_blocks = jnp.stack([out[0] for out in outputs])
    prob_blocks = [out[1] for out in outputs]
    kv_blocks = [out[2] for out in outputs]
    return (attn_blocks.reshape(row_count, span), prob_blocks, kv_blocks)


def attention_backward(
    queries, ext_rows, neighbours, row_offset, grad_attended, prob_blocks, kv_blocks, riders
):
    f32 = jnp.float32
    bf16 = jnp.bfloat16
    row_count = queries.shape[0]
    span = queries.shape[1]
    heads_here = span // HD
    slot_width = neighbours.shape[1] + 1
    score_scale = 1.0 / math.sqrt(HD)
    block_rows = math.gcd(row_count, 512)
    block_count = row_count // block_rows
    block_starts = row_offset + jnp.arange(block_count, dtype=jnp.int32) * block_rows
    query_blocks = queries.reshape(block_count, block_rows, span)
    neighbour_blocks = neighbours.reshape(block_count, block_rows, slot_width - 1)
    grad_blocks = grad_attended.reshape(block_count, block_rows, span)

    def backward_block(carried, inputs):
        query_block, neighbour_block, first_row, grad_block, probabilities, gathered = inputs
        slot_rows, slot_live = slot_index(neighbour_block, first_row, block_rows)
        block_keys = gathered[:, :, 0].reshape(block_rows, slot_width, heads_here, HD).astype(f32)
        block_values = gathered[:, :, 1].reshape(block_rows, slot_width, heads_here, HD).astype(f32)
        grad_mix = grad_block.reshape(block_rows, heads_here, HD).astype(f32)
        grad_weights = jnp.einsum("bhd,bmhd->bhm", grad_mix, block_values)
        grad_scores = (
            probabilities
            * (grad_weights - jnp.sum(probabilities * grad_weights, axis=2, keepdims=True))
            * score_scale
        )
        grad_query = jnp.einsum("bhm,bmhd->bhd", grad_scores, block_keys).reshape(block_rows, span)
        query_wide = query_block.reshape(block_rows, heads_here, HD).astype(f32)
        grad_keys = jnp.einsum("bhm,bhd->bmhd", grad_scores, query_wide)
        rounded = lax.optimization_barrier(probabilities.astype(bf16))
        grad_values = jnp.einsum("bhm,bhd->bmhd", rounded.astype(f32), grad_mix)
        contribution = (
            jnp.stack([grad_keys, grad_values], axis=2)
            .reshape(block_rows, slot_width, 2 * span)
            .astype(bf16)
        )
        for slot in range(slot_width):
            carried = carried + jnp.einsum(
                "bx,bc->xc",
                pick_table(slot_rows[:, slot], ext_rows),
                contribution[:, slot],
                preferred_element_type=f32,
            )
        return (carried, grad_query)

    carried = jnp.zeros((ext_rows, 2 * span), f32)
    query_grads = []
    for b in range(block_count):
        carried, grad_query = backward_block(
            carried,
            (query_blocks[b], neighbour_blocks[b], block_starts[b], grad_blocks[b],
             prob_blocks[b], kv_blocks[b]),
        )
        query_grads.append(grad_query)
        if b == 0:
            carried, riders = lax.optimization_barrier((carried, riders))
    query_grads = jnp.stack(query_grads)
    return (carried.reshape(ext_rows, 2, span), query_grads.reshape(row_count, span), riders)


def ch_exchange(value):
    size = lax.axis_size("ch")
    return [
        lax.ppermute(value, "ch", [(i, (i + shift) % size) for i in range(size)])
        for shift in range(1, size)
    ]


def ch_assemble(own, others, axis):
    size = len(others) + 1
    index = lax.axis_index("ch")
    pieces = [own] + others
    result = None
    for case in range(size):
        ordered = jnp.concatenate([pieces[(case - j) % size] for j in range(size)], axis=axis)
        result = ordered if result is None else jnp.where(index == case, ordered, result)
    return result


HALVING_MASKS = (1, 2)


def pix_swap(value, mask):
    size = lax.axis_size("pix")
    return lax.ppermute(value, "pix", [(i, i ^ mask) for i in range(size)])


def pix_scatter(terms, width):
    size = lax.axis_size("pix")
    index = lax.axis_index("pix")
    groups = 2 ** len(HALVING_MASKS)
    flat = jnp.concatenate([term.reshape(-1, width) for term in terms], axis=0)
    rows = flat.shape[0]
    chunk = -(-rows // (groups * size))
    data = jnp.pad(flat, ((0, groups * size * chunk - rows), (0, 0)))
    for mask in HALVING_MASKS:
        high = (index // mask) % 2 == 1
        halves = data.reshape(2, -1, width)
        keep = jnp.where(high, halves[1], halves[0])
        send = jnp.where(high, halves[0], halves[1])
        data = keep + pix_swap(send, mask)
    parts = lax.all_to_all(data.reshape(size, chunk, width), "pix", 0, 0, tiled=True)
    return jnp.sum(parts.reshape(size // groups, groups, chunk, width), axis=0)


def pix_gather(reduced_groups, term_groups):
    size = lax.axis_size("pix")
    index = lax.axis_index("pix")
    groups = 2 ** len(HALVING_MASKS)
    width = reduced_groups[0].shape[-1]
    joined = jnp.concatenate(reduced_groups, axis=1)
    total = joined.shape[1]
    spread = jnp.broadcast_to(joined[None], (size // groups, groups, total, width))
    got = lax.all_to_all(spread.reshape(size, total, width), "pix", 0, 0, tiled=True)
    blocks = got[None]
    for mask in reversed(HALVING_MASKS):
        high = (index // mask) % 2 == 1
        other = pix_swap(blocks, mask)
        blocks = jnp.where(
            high,
            jnp.concatenate([other, blocks], axis=0),
            jnp.concatenate([blocks, other], axis=0),
        )
    results = []
    offset = 0
    for reduced, terms in zip(reduced_groups, term_groups):
        chunk = reduced.shape[1]
        flat = blocks[:, :, offset : offset + chunk].reshape(groups * size * chunk, width)
        offset += chunk
        row = 0
        for term in terms:
            count = term.size // width
            results.append(flat[row : row + count].reshape(term.shape))
            row += count
    return results


def per_device(
    fine_pixels, pool_kernel, projections, mixing_weight, send_list, neighbours, cotangent
):
    f32 = jnp.float32
    bf16 = jnp.bfloat16
    row_count = fine_pixels.shape[0]
    half_width = projections.shape[2]
    ch_size = lax.axis_size("ch")
    ch_index = lax.axis_index("ch")
    peer_count = lax.axis_size("pix")
    slot_count = send_list.shape[1]
    grad_scale = 1.0 / math.sqrt(row_count * peer_count)
    send_pick = pick_table(send_list.reshape(-1), row_count)
    fine_others = ch_exchange(fine_pixels)
    kernel_others = ch_exchange(pool_kernel)
    pooled_sum = jnp.dot(fine_pixels, pool_kernel, preferred_element_type=f32)
    for fine_other, kernel_other in zip(fine_others, kernel_others):
        pooled_sum = pooled_sum + jnp.dot(fine_other, kernel_other, preferred_element_type=f32)
    pooled_all = pooled_sum.astype(bf16)
    mix_pieces = mixing_weight.reshape(mixing_weight.shape[0], ch_size, half_width)
    mix_sends = [
        jnp.take(mix_pieces, (ch_index + shift) % ch_size, axis=1) for shift in range(1, ch_size)
    ]
    pooled_all, cot_send, proj_send, mix_sends = lax.optimization_barrier(
        (pooled_all, cotangent, projections, mix_sends)
    )
    cot_others = ch_exchange(cot_send)
    proj_others = ch_exchange(proj_send)
    mix_others = [
        lax.ppermute(mix_send, "ch", [(i, (i + shift) % ch_size) for i in range(ch_size)])
        for shift, mix_send in zip(range(1, ch_size), mix_sends)
    ]
    mix_own = jnp.take(mix_pieces, ch_index, axis=1)
    pooled = lax.dynamic_slice_in_dim(pooled_all, ch_index * half_width, half_width, axis=1)
    upstream = ch_assemble(cotangent, cot_others, axis=1)
    projected = jnp.einsum(
        "rc,kcd->rkd", pooled_all, projections, preferred_element_type=f32
    ).astype(bf16)
    queries = projected[:, 0]
    key_value = projected[:, 1:]
    outgoing = (
        jnp.dot(send_pick, key_value.reshape(row_count, 2 * half_width), preferred_element_type=f32)
        .astype(bf16)
        .reshape(peer_count, slot_count, 2, half_width)
    )
    incoming = lax.all_to_all(outgoing, "pix", split_axis=0, concat_axis=0, tiled=True)
    extended = jnp.concatenate(
        [key_value, incoming.reshape(peer_count * slot_count, 2, half_width)], axis=0
    )
    attended, prob_blocks, kv_blocks = attention_forward(queries, extended, neighbours, 0)
    attended_others = ch_exchange(attended)
    grad_attended = jnp.dot(upstream, mixing_weight.T, preferred_element_type=f32).astype(bf16)
    grad_attended, proj_others = lax.optimization_barrier((grad_attended, proj_others))
    mixing_term = jnp.dot(attended.T, upstream, preferred_element_type=f32) * grad_scale
    carried, query_grads, (attended_others, mix_others) = attention_backward(
        queries, extended.shape[0], neighbours, 0, grad_attended, prob_blocks, kv_blocks,
        (attended_others, mix_others),
    )
    branch = jnp.dot(attended, mix_own, preferred_element_type=f32)
    for attended_other, mix_other in zip(attended_others, mix_others):
        branch = branch + jnp.dot(attended_other, mix_other, preferred_element_type=f32)
    section_output = (pooled.astype(f32) + branch).astype(bf16)
    remote_grads = carried[row_count:].reshape(peer_count, slot_count, 2, half_width)
    returned = lax.all_to_all(remote_grads, "pix", split_axis=0, concat_axis=0, tiled=True)
    returned_rows = jnp.einsum(
        "px,pc->xc",
        send_pick,
        returned.reshape(peer_count * slot_count, 2 * half_width).astype(bf16),
        preferred_element_type=f32,
    )
    local_grads = carried[:row_count] + returned_rows.reshape(row_count, 2, half_width)
    grad_projected = jnp.concatenate(
        [query_grads.reshape(row_count, 1, half_width), local_grads], axis=1
    ).astype(bf16)
    grad_others = ch_exchange(grad_projected)
    projection_term = (
        jnp.einsum("rc,rkd->kcd", pooled_all, grad_projected, preferred_element_type=f32)
        * grad_scale
    )
    early_reduced = pix_scatter((projection_term, mixing_term), mixing_weight.shape[1])
    early_reduced, grad_others = lax.optimization_barrier((early_reduced, grad_others))
    pooled_sum = upstream.astype(f32) + jnp.einsum(
        "rkd,kcd->rc", grad_projected, projections, preferred_element_type=f32
    )
    for grad_other, proj_other in zip(grad_others, proj_others):
        pooled_sum = pooled_sum + jnp.einsum(
            "rkd,kcd->rc", grad_other, proj_other, preferred_element_type=f32
        )
    grad_pooled = pooled_sum.astype(bf16)
    kernel_term = jnp.dot(fine_pixels.T, grad_pooled, preferred_element_type=f32) * grad_scale
    fine_gradient = jnp.dot(grad_pooled, pool_kernel.T, preferred_element_type=f32).astype(bf16)
    kernel_reduced = pix_scatter((kernel_term,), mixing_weight.shape[1])
    projection_gradient, mixing_gradient, kernel_gradient = pix_gather(
        (early_reduced, kernel_reduced), ((projection_term, mixing_term), (kernel_term,))
    )
    return (section_output, fine_gradient, kernel_gradient, projection_gradient, mixing_gradient)


def solution(mesh):
    placed = (
        P("pix", "ch"),
        P("ch", None),
        P(None, None, "ch"),
        P("ch", None),
        P("pix", None),
        P("pix", None),
        P("pix", "ch"),
    )
    return jax.shard_map(
        per_device,
        mesh=mesh,
        in_specs=placed,
        out_specs=(
            P("pix", "ch"),
            P("pix", "ch"),
            P("ch", None),
            P(None, None, "ch"),
            P("ch", None),
        ),
        check_vma=False,
    )
```

```python
import math

import jax
import jax.numpy as jnp
from jax import lax
from jax.sharding import PartitionSpec as P

HD = 64


def pick_table(row_ids, total):
    return (row_ids[:, None] == jnp.arange(total, dtype=jnp.int32)[None, :]).astype(jnp.bfloat16)


def slot_index(neighbour_block, first_row, block_rows):
    present = neighbour_block >= 0
    own_rows = first_row + jnp.arange(block_rows, dtype=jnp.int32)
    slot_rows = jnp.concatenate([own_rows[:, None], jnp.where(present, neighbour_block, 0)], axis=1)
    slot_live = jnp.concatenate([jnp.ones((block_rows, 1), bool), present], axis=1)
    return (slot_rows, slot_live)


def attention_forward(queries, extended, neighbours, row_offset):
    f32 = jnp.float32
    bf16 = jnp.bfloat16
    row_count = queries.shape[0]
    span = queries.shape[1]
    ext_rows = extended.shape[0]
    heads_here = span // HD
    slot_width = neighbours.shape[1] + 1
    score_scale = 1.0 / math.sqrt(HD)
    block_rows = math.gcd(row_count, 512)
    block_count = row_count // block_rows
    block_starts = row_offset + jnp.arange(block_count, dtype=jnp.int32) * block_rows
    query_blocks = queries.reshape(block_count, block_rows, span)
    neighbour_blocks = neighbours.reshape(block_count, block_rows, slot_width - 1)
    flattened = extended.reshape(ext_rows, 2 * span)

    def forward_block(inputs):
        query_block, neighbour_block, first_row = inputs
        slot_rows, slot_live = slot_index(neighbour_block, first_row, block_rows)
        own = lax.dynamic_slice_in_dim(flattened, first_row, block_rows, axis=0)
        picks = pick_table(slot_rows[:, 1:].T.reshape(-1), ext_rows)
        others = (
            jnp.dot(picks, flattened, preferred_element_type=f32)
            .astype(bf16)
            .reshape(slot_width - 1, block_rows, 2 * span)
        )
        gathered = (
            jnp.concatenate([own[None], others], axis=0)
            .transpose(1, 0, 2)
            .reshape(block_rows, slot_width, 2, span)
        )
        block_keys = gathered[:, :, 0].reshape(block_rows, slot_width, heads_here, HD)
        block_values = gathered[:, :, 1].reshape(block_rows, slot_width, heads_here, HD)
        scores = (
            jnp.einsum(
                "bhd,bmhd->bhm",
                query_block.reshape(block_rows, heads_here, HD),
                block_keys,
                preferred_element_type=f32,
            )
            * score_scale
        )
        shut = slot_live[:, None, :]
        masked = jnp.where(shut, scores, -1e30)
        largest = jnp.max(masked, axis=2, keepdims=True)
        raised = jnp.where(shut, jnp.exp(masked - largest), 0.0)
        probabilities = raised / jnp.sum(raised, axis=2, keepdims=True)
        weights = probabilities.astype(bf16)
        mixture = jnp.einsum("bhm,bmhd->bhd", weights, block_values, preferred_element_type=f32)
        return (mixture.reshape(block_rows, span).astype(bf16), probabilities, gathered)

    outputs = [
        forward_block((query_blocks[b], neighbour_blocks[b], block_starts[b]))
        for b in range(block_count)
    ]
    attn_blocks = jnp.stack([out[0] for out in outputs])
    prob_blocks = [out[1] for out in outputs]
    kv_blocks = [out[2] for out in outputs]
    return (attn_blocks.reshape(row_count, span), prob_blocks, kv_blocks)


def attention_backward(
    queries, ext_rows, neighbours, row_offset, grad_attended, prob_blocks, kv_blocks, riders
):
    f32 = jnp.float32
    bf16 = jnp.bfloat16
    row_count = queries.shape[0]
    span = queries.shape[1]
    heads_here = span // HD
    slot_width = neighbours.shape[1] + 1
    score_scale = 1.0 / math.sqrt(HD)
    block_rows = math.gcd(row_count, 512)
    block_count = row_count // block_rows
    block_starts = row_offset + jnp.arange(block_count, dtype=jnp.int32) * block_rows
    query_blocks = queries.reshape(block_count, block_rows, span)
    neighbour_blocks = neighbours.reshape(block_count, block_rows, slot_width - 1)
    grad_blocks = grad_attended.reshape(block_count, block_rows, span)

    def backward_block(carried, inputs):
        query_block, neighbour_block, first_row, grad_block, probabilities, gathered = inputs
        slot_rows, slot_live = slot_index(neighbour_block, first_row, block_rows)
        block_keys = gathered[:, :, 0].reshape(block_rows, slot_width, heads_here, HD).astype(f32)
        block_values = gathered[:, :, 1].reshape(block_rows, slot_width, heads_here, HD).astype(f32)
        grad_mix = grad_block.reshape(block_rows, heads_here, HD).astype(f32)
        grad_weights = jnp.einsum("bhd,bmhd->bhm", grad_mix, block_values)
        grad_scores = (
            probabilities
            * (grad_weights - jnp.sum(probabilities * grad_weights, axis=2, keepdims=True))
            * score_scale
        )
        grad_query = jnp.einsum("bhm,bmhd->bhd", grad_scores, block_keys).reshape(block_rows, span)
        query_wide = query_block.reshape(block_rows, heads_here, HD).astype(f32)
        grad_keys = jnp.einsum("bhm,bhd->bmhd", grad_scores, query_wide)
        rounded = lax.optimization_barrier(probabilities.astype(bf16))
        grad_values = jnp.einsum("bhm,bhd->bmhd", rounded.astype(f32), grad_mix)
        contribution = (
            jnp.stack([grad_keys, grad_values], axis=2)
            .reshape(block_rows, slot_width, 2 * span)
            .astype(bf16)
        )
        picks = pick_table(slot_rows[:, 1:].T.reshape(-1), ext_rows)
        rest = contribution[:, 1:].transpose(1, 0, 2).reshape(-1, 2 * span)
        carried = carried + jnp.einsum("bx,bc->xc", picks, rest, preferred_element_type=f32)
        own_rows = lax.dynamic_slice_in_dim(carried, first_row, block_rows, axis=0)
        carried = lax.dynamic_update_slice_in_dim(
            carried, own_rows + contribution[:, 0].astype(f32), first_row, axis=0
        )
        return (carried, grad_query)

    carried = jnp.zeros((ext_rows, 2 * span), f32)
    query_grads = []
    for b in range(block_count):
        carried, grad_query = backward_block(
            carried,
            (query_blocks[b], neighbour_blocks[b], block_starts[b], grad_blocks[b],
             prob_blocks[b], kv_blocks[b]),
        )
        query_grads.append(grad_query)
        if b == 0:
            carried, riders = lax.optimization_barrier((carried, riders))
    query_grads = jnp.stack(query_grads)
    return (carried.reshape(ext_rows, 2, span), query_grads.reshape(row_count, span), riders)


def ch_exchange(value):
    size = lax.axis_size("ch")
    return [
        lax.ppermute(value, "ch", [(i, (i + shift) % size) for i in range(size)])
        for shift in range(1, size)
    ]


def ch_assemble(own, others, axis):
    size = len(others) + 1
    index = lax.axis_index("ch")
    pieces = [own] + others
    result = None
    for case in range(size):
        ordered = jnp.concatenate([pieces[(case - j) % size] for j in range(size)], axis=axis)
        result = ordered if result is None else jnp.where(index == case, ordered, result)
    return result


def core_swap(value):
    size = lax.axis_size("pix")
    return lax.ppermute(value, "pix", [(i, i ^ 1) for i in range(size)])


def pix_scatter(terms, width):
    size = lax.axis_size("pix")
    core = lax.axis_index("pix") % 2
    flat = jnp.concatenate([term.reshape(-1, width) for term in terms], axis=0)
    rows = flat.shape[0]
    chunk = -(-rows // (2 * size))
    flat = jnp.pad(flat, ((0, 2 * size * chunk - rows), (0, 0)))
    halves = flat.reshape(2, size * chunk, width)
    keep = jnp.where(core == 0, halves[0], halves[1])
    send = jnp.where(core == 0, halves[1], halves[0])
    mine = keep + core_swap(send)
    parts = lax.all_to_all(mine.reshape(size, chunk, width), "pix", 0, 0, tiled=True)
    return jnp.sum(parts.reshape(size // 2, 2, chunk, width), axis=0)


def pix_gather(reduced_groups, term_groups):
    size = lax.axis_size("pix")
    core = lax.axis_index("pix") % 2
    width = reduced_groups[0].shape[-1]
    joined = jnp.concatenate(reduced_groups, axis=1)
    total = joined.shape[1]
    spread = jnp.broadcast_to(joined[None], (size // 2, 2, total, width))
    got = lax.all_to_all(spread.reshape(size, total, width), "pix", 0, 0, tiled=True)
    other = core_swap(got)
    first = jnp.where(core == 0, got, other)
    second = jnp.where(core == 0, other, got)
    results = []
    offset = 0
    for reduced, terms in zip(reduced_groups, term_groups):
        chunk = reduced.shape[1]
        flat = jnp.concatenate(
            [
                first[:, offset : offset + chunk].reshape(size * chunk, width),
                second[:, offset : offset + chunk].reshape(size * chunk, width),
            ],
            axis=0,
        )
        offset += chunk
        row = 0
        for term in terms:
            count = term.size // width
            results.append(flat[row : row + count].reshape(term.shape))
            row += count
    return results


def per_device(
    fine_pixels, pool_kernel, projections, mixing_weight, send_list, neighbours, cotangent
):
    f32 = jnp.float32
    bf16 = jnp.bfloat16
    row_count = fine_pixels.shape[0]
    half_width = projections.shape[2]
    ch_size = lax.axis_size("ch")
    ch_index = lax.axis_index("ch")
    peer_count = lax.axis_size("pix")
    slot_count = send_list.shape[1]
    grad_scale = 1.0 / math.sqrt(row_count * peer_count)
    send_pick = pick_table(send_list.reshape(-1), row_count)
    fine_others = ch_exchange(fine_pixels)
    kernel_others = ch_exchange(pool_kernel)
    pooled_sum = jnp.dot(fine_pixels, pool_kernel, preferred_element_type=f32)
    for fine_other, kernel_other in zip(fine_others, kernel_others):
        pooled_sum = pooled_sum + jnp.dot(fine_other, kernel_other, preferred_element_type=f32)
    pooled_all = pooled_sum.astype(bf16)
    mix_pieces = mixing_weight.reshape(mixing_weight.shape[0], ch_size, half_width)
    mix_sends = [
        jnp.take(mix_pieces, (ch_index + shift) % ch_size, axis=1) for shift in range(1, ch_size)
    ]
    pooled_all, cot_send, proj_send, mix_sends = lax.optimization_barrier(
        (pooled_all, cotangent, projections, mix_sends)
    )
    cot_others = ch_exchange(cot_send)
    proj_others = ch_exchange(proj_send)
    mix_others = [
        lax.ppermute(mix_send, "ch", [(i, (i + shift) % ch_size) for i in range(ch_size)])
        for shift, mix_send in zip(range(1, ch_size), mix_sends)
    ]
    mix_own = jnp.take(mix_pieces, ch_index, axis=1)
    pooled = lax.dynamic_slice_in_dim(pooled_all, ch_index * half_width, half_width, axis=1)
    upstream = ch_assemble(cotangent, cot_others, axis=1)
    projected = jnp.einsum(
        "rc,kcd->rkd", pooled_all, projections, preferred_element_type=f32
    ).astype(bf16)
    queries = projected[:, 0]
    key_value = projected[:, 1:]
    outgoing = (
        jnp.dot(send_pick, key_value.reshape(row_count, 2 * half_width), preferred_element_type=f32)
        .astype(bf16)
        .reshape(peer_count, slot_count, 2, half_width)
    )
    incoming = lax.all_to_all(outgoing, "pix", split_axis=0, concat_axis=0, tiled=True)
    extended = jnp.concatenate(
        [key_value, incoming.reshape(peer_count * slot_count, 2, half_width)], axis=0
    )
    attended, prob_blocks, kv_blocks = attention_forward(queries, extended, neighbours, 0)
    attended_others = ch_exchange(attended)
    grad_attended = jnp.dot(upstream, mixing_weight.T, preferred_element_type=f32).astype(bf16)
    grad_attended, proj_others = lax.optimization_barrier((grad_attended, proj_others))
    mixing_term = jnp.dot(attended.T, upstream, preferred_element_type=f32) * grad_scale
    carried, query_grads, (attended_others, mix_others) = attention_backward(
        queries, extended.shape[0], neighbours, 0, grad_attended, prob_blocks, kv_blocks,
        (attended_others, mix_others),
    )
    branch = jnp.dot(attended, mix_own, preferred_element_type=f32)
    for attended_other, mix_other in zip(attended_others, mix_others):
        branch = branch + jnp.dot(attended_other, mix_other, preferred_element_type=f32)
    section_output = (pooled.astype(f32) + branch).astype(bf16)
    remote_grads = carried[row_count:].reshape(peer_count, slot_count, 2, half_width)
    returned = lax.all_to_all(remote_grads, "pix", split_axis=0, concat_axis=0, tiled=True)
    returned_rows = jnp.einsum(
        "px,pc->xc",
        send_pick,
        returned.reshape(peer_count * slot_count, 2 * half_width).astype(bf16),
        preferred_element_type=f32,
    )
    local_grads = carried[:row_count] + returned_rows.reshape(row_count, 2, half_width)
    grad_projected = jnp.concatenate(
        [query_grads.reshape(row_count, 1, half_width), local_grads], axis=1
    ).astype(bf16)
    grad_others = ch_exchange(grad_projected)
    projection_term = (
        jnp.einsum("rc,rkd->kcd", pooled_all, grad_projected, preferred_element_type=f32)
        * grad_scale
    )
    early_reduced = pix_scatter((projection_term, mixing_term), mixing_weight.shape[1])
    early_reduced, grad_others = lax.optimization_barrier((early_reduced, grad_others))
    pooled_sum = upstream.astype(f32) + jnp.einsum(
        "rkd,kcd->rc", grad_projected, projections, preferred_element_type=f32
    )
    for grad_other, proj_other in zip(grad_others, proj_others):
        pooled_sum = pooled_sum + jnp.einsum(
            "rkd,kcd->rc", grad_other, proj_other, preferred_element_type=f32
        )
    grad_pooled = pooled_sum.astype(bf16)
    kernel_term = jnp.dot(fine_pixels.T, grad_pooled, preferred_element_type=f32) * grad_scale
    fine_gradient = jnp.dot(grad_pooled, pool_kernel.T, preferred_element_type=f32).astype(bf16)
    kernel_reduced = pix_scatter((kernel_term,), mixing_weight.shape[1])
    projection_gradient, mixing_gradient, kernel_gradient = pix_gather(
        (early_reduced, kernel_reduced), ((projection_term, mixing_term), (kernel_term,))
    )
    return (section_output, fine_gradient, kernel_gradient, projection_gradient, mixing_gradient)


def solution(mesh):
    placed = (
        P("pix", "ch"),
        P("ch", None),
        P(None, None, "ch"),
        P("ch", None),
        P("pix", None),
        P("pix", None),
        P("pix", "ch"),
    )
    return jax.shard_map(
        per_device,
        mesh=mesh,
        in_specs=placed,
        out_specs=(
            P("pix", "ch"),
            P("pix", "ch"),
            P("ch", None),
            P(None, None, "ch"),
            P("ch", None),
        ),
        check_vma=False,
    )
```

```python
import math

import jax
import jax.numpy as jnp
from jax import lax
from jax.sharding import PartitionSpec as P

HD = 64


def pick_table(row_ids, total):
    return (row_ids[:, None] == jnp.arange(total, dtype=jnp.int32)[None, :]).astype(jnp.bfloat16)


def slot_index(neighbour_block, first_row, block_rows):
    present = neighbour_block >= 0
    own_rows = first_row + jnp.arange(block_rows, dtype=jnp.int32)
    slot_rows = jnp.concatenate([own_rows[:, None], jnp.where(present, neighbour_block, 0)], axis=1)
    slot_live = jnp.concatenate([jnp.ones((block_rows, 1), bool), present], axis=1)
    return (slot_rows, slot_live)


def attention_forward(queries, extended, neighbours, row_offset):
    f32 = jnp.float32
    bf16 = jnp.bfloat16
    row_count = queries.shape[0]
    span = queries.shape[1]
    ext_rows = extended.shape[0]
    heads_here = span // HD
    slot_width = neighbours.shape[1] + 1
    score_scale = 1.0 / math.sqrt(HD)
    block_rows = math.gcd(row_count, 512)
    block_count = row_count // block_rows
    block_starts = row_offset + jnp.arange(block_count, dtype=jnp.int32) * block_rows
    query_blocks = queries.reshape(block_count, block_rows, span)
    neighbour_blocks = neighbours.reshape(block_count, block_rows, slot_width - 1)
    flattened = extended.reshape(ext_rows, 2 * span)

    def forward_block(inputs):
        query_block, neighbour_block, first_row = inputs
        slot_rows, slot_live = slot_index(neighbour_block, first_row, block_rows)
        picks = pick_table(slot_rows.T.reshape(-1), ext_rows)
        gathered = (
            jnp.dot(picks, flattened, preferred_element_type=f32)
            .astype(bf16)
            .reshape(slot_width, block_rows, 2, span)
        )
        block_keys = gathered[:, :, 0].reshape(slot_width, block_rows, heads_here, HD)
        block_values = gathered[:, :, 1].reshape(slot_width, block_rows, heads_here, HD)
        scores = (
            jnp.einsum(
                "bhd,mbhd->bhm",
                query_block.reshape(block_rows, heads_here, HD),
                block_keys,
                preferred_element_type=f32,
            )
            * score_scale
        )
        shut = slot_live[:, None, :]
        masked = jnp.where(shut, scores, -1e30)
        largest = jnp.max(masked, axis=2, keepdims=True)
        raised = jnp.where(shut, jnp.exp(masked - largest), 0.0)
        probabilities = raised / jnp.sum(raised, axis=2, keepdims=True)
        weights = probabilities.astype(bf16)
        mixture = jnp.einsum("bhm,mbhd->bhd", weights, block_values, preferred_element_type=f32)
        return (mixture.reshape(block_rows, span).astype(bf16), probabilities, gathered)

    outputs = [
        forward_block((query_blocks[b], neighbour_blocks[b], block_starts[b]))
        for b in range(block_count)
    ]
    attn_blocks = jnp.stack([out[0] for out in outputs])
    prob_blocks = [out[1] for out in outputs]
    kv_blocks = [out[2] for out in outputs]
    return (attn_blocks.reshape(row_count, span), prob_blocks, kv_blocks)


def attention_backward(
    queries, ext_rows, neighbours, row_offset, grad_attended, prob_blocks, kv_blocks, riders
):
    f32 = jnp.float32
    bf16 = jnp.bfloat16
    row_count = queries.shape[0]
    span = queries.shape[1]
    heads_here = span // HD
    slot_width = neighbours.shape[1] + 1
    score_scale = 1.0 / math.sqrt(HD)
    block_rows = math.gcd(row_count, 512)
    block_count = row_count // block_rows
    block_starts = row_offset + jnp.arange(block_count, dtype=jnp.int32) * block_rows
    query_blocks = queries.reshape(block_count, block_rows, span)
    neighbour_blocks = neighbours.reshape(block_count, block_rows, slot_width - 1)
    grad_blocks = grad_attended.reshape(block_count, block_rows, span)

    def backward_block(carried, inputs):
        query_block, neighbour_block, first_row, grad_block, probabilities, gathered = inputs
        slot_rows, slot_live = slot_index(neighbour_block, first_row, block_rows)
        block_keys = gathered[:, :, 0].reshape(slot_width, block_rows, heads_here, HD).astype(f32)
        block_values = gathered[:, :, 1].reshape(slot_width, block_rows, heads_here, HD).astype(f32)
        grad_mix = grad_block.reshape(block_rows, heads_here, HD).astype(f32)
        grad_weights = jnp.einsum("bhd,mbhd->bhm", grad_mix, block_values)
        grad_scores = (
            probabilities
            * (grad_weights - jnp.sum(probabilities * grad_weights, axis=2, keepdims=True))
            * score_scale
        )
        grad_query = jnp.einsum("bhm,mbhd->bhd", grad_scores, block_keys).reshape(block_rows, span)
        query_wide = query_block.reshape(block_rows, heads_here, HD).astype(f32)
        grad_keys = jnp.einsum("bhm,bhd->mbhd", grad_scores, query_wide)
        rounded = lax.optimization_barrier(probabilities.astype(bf16))
        grad_values = jnp.einsum("bhm,bhd->mbhd", rounded.astype(f32), grad_mix)
        contribution = (
            jnp.stack([grad_keys, grad_values], axis=2)
            .reshape(slot_width * block_rows, 2 * span)
            .astype(bf16)
        )
        picks = pick_table(slot_rows.T.reshape(-1), ext_rows)
        carried = carried + jnp.einsum(
            "bx,bc->xc", picks, contribution, preferred_element_type=f32
        )
        return (carried, grad_query)

    carried = jnp.zeros((ext_rows, 2 * span), f32)
    query_grads = []
    for b in range(block_count):
        carried, grad_query = backward_block(
            carried,
            (query_blocks[b], neighbour_blocks[b], block_starts[b], grad_blocks[b],
             prob_blocks[b], kv_blocks[b]),
        )
        query_grads.append(grad_query)
        if b == 0:
            carried, riders = lax.optimization_barrier((carried, riders))
    query_grads = jnp.stack(query_grads)
    return (carried.reshape(ext_rows, 2, span), query_grads.reshape(row_count, span), riders)


def ch_exchange(value):
    size = lax.axis_size("ch")
    return [
        lax.ppermute(value, "ch", [(i, (i + shift) % size) for i in range(size)])
        for shift in range(1, size)
    ]


def ch_assemble(own, others, axis):
    size = len(others) + 1
    index = lax.axis_index("ch")
    pieces = [own] + others
    result = None
    for case in range(size):
        ordered = jnp.concatenate([pieces[(case - j) % size] for j in range(size)], axis=axis)
        result = ordered if result is None else jnp.where(index == case, ordered, result)
    return result


def core_swap(value):
    size = lax.axis_size("pix")
    return lax.ppermute(value, "pix", [(i, i ^ 1) for i in range(size)])


def pix_scatter(terms, width):
    size = lax.axis_size("pix")
    core = lax.axis_index("pix") % 2
    flat = jnp.concatenate([term.reshape(-1, width) for term in terms], axis=0)
    rows = flat.shape[0]
    chunk = -(-rows // (2 * size))
    flat = jnp.pad(flat, ((0, 2 * size * chunk - rows), (0, 0)))
    halves = flat.reshape(2, size * chunk, width)
    keep = jnp.where(core == 0, halves[0], halves[1])
    send = jnp.where(core == 0, halves[1], halves[0])
    mine = keep + core_swap(send)
    parts = lax.all_to_all(mine.reshape(size, chunk, width), "pix", 0, 0, tiled=True)
    return jnp.sum(parts.reshape(size // 2, 2, chunk, width), axis=0)


def pix_gather(reduced_groups, term_groups):
    size = lax.axis_size("pix")
    core = lax.axis_index("pix") % 2
    width = reduced_groups[0].shape[-1]
    joined = jnp.concatenate(reduced_groups, axis=1)
    total = joined.shape[1]
    spread = jnp.broadcast_to(joined[None], (size // 2, 2, total, width))
    got = lax.all_to_all(spread.reshape(size, total, width), "pix", 0, 0, tiled=True)
    other = core_swap(got)
    first = jnp.where(core == 0, got, other)
    second = jnp.where(core == 0, other, got)
    results = []
    offset = 0
    for reduced, terms in zip(reduced_groups, term_groups):
        chunk = reduced.shape[1]
        flat = jnp.concatenate(
            [
                first[:, offset : offset + chunk].reshape(size * chunk, width),
                second[:, offset : offset + chunk].reshape(size * chunk, width),
            ],
            axis=0,
        )
        offset += chunk
        row = 0
        for term in terms:
            count = term.size // width
            results.append(flat[row : row + count].reshape(term.shape))
            row += count
    return results


def per_device(
    fine_pixels, pool_kernel, projections, mixing_weight, send_list, neighbours, cotangent
):
    f32 = jnp.float32
    bf16 = jnp.bfloat16
    row_count = fine_pixels.shape[0]
    half_width = projections.shape[2]
    ch_size = lax.axis_size("ch")
    ch_index = lax.axis_index("ch")
    peer_count = lax.axis_size("pix")
    slot_count = send_list.shape[1]
    grad_scale = 1.0 / math.sqrt(row_count * peer_count)
    send_pick = pick_table(send_list.reshape(-1), row_count)
    fine_others = ch_exchange(fine_pixels)
    kernel_others = ch_exchange(pool_kernel)
    pooled_sum = jnp.dot(fine_pixels, pool_kernel, preferred_element_type=f32)
    for fine_other, kernel_other in zip(fine_others, kernel_others):
        pooled_sum = pooled_sum + jnp.dot(fine_other, kernel_other, preferred_element_type=f32)
    pooled_all = pooled_sum.astype(bf16)
    mix_pieces = mixing_weight.reshape(mixing_weight.shape[0], ch_size, half_width)
    mix_sends = [
        jnp.take(mix_pieces, (ch_index + shift) % ch_size, axis=1) for shift in range(1, ch_size)
    ]
    pooled_all, cot_send, proj_send, mix_sends = lax.optimization_barrier(
        (pooled_all, cotangent, projections, mix_sends)
    )
    cot_others = ch_exchange(cot_send)
    proj_others = ch_exchange(proj_send)
    mix_others = [
        lax.ppermute(mix_send, "ch", [(i, (i + shift) % ch_size) for i in range(ch_size)])
        for shift, mix_send in zip(range(1, ch_size), mix_sends)
    ]
    mix_own = jnp.take(mix_pieces, ch_index, axis=1)
    pooled = lax.dynamic_slice_in_dim(pooled_all, ch_index * half_width, half_width, axis=1)
    upstream = ch_assemble(cotangent, cot_others, axis=1)
    projected = jnp.einsum(
        "rc,kcd->rkd", pooled_all, projections, preferred_element_type=f32
    ).astype(bf16)
    queries = projected[:, 0]
    key_value = projected[:, 1:]
    outgoing = (
        jnp.dot(send_pick, key_value.reshape(row_count, 2 * half_width), preferred_element_type=f32)
        .astype(bf16)
        .reshape(peer_count, slot_count, 2, half_width)
    )
    incoming = lax.all_to_all(outgoing, "pix", split_axis=0, concat_axis=0, tiled=True)
    extended = jnp.concatenate(
        [key_value, incoming.reshape(peer_count * slot_count, 2, half_width)], axis=0
    )
    attended, prob_blocks, kv_blocks = attention_forward(queries, extended, neighbours, 0)
    attended_others = ch_exchange(attended)
    grad_attended = jnp.dot(upstream, mixing_weight.T, preferred_element_type=f32).astype(bf16)
    grad_attended, proj_others = lax.optimization_barrier((grad_attended, proj_others))
    mixing_term = jnp.dot(attended.T, upstream, preferred_element_type=f32) * grad_scale
    carried, query_grads, (attended_others, mix_others) = attention_backward(
        queries, extended.shape[0], neighbours, 0, grad_attended, prob_blocks, kv_blocks,
        (attended_others, mix_others),
    )
    branch = jnp.dot(attended, mix_own, preferred_element_type=f32)
    for attended_other, mix_other in zip(attended_others, mix_others):
        branch = branch + jnp.dot(attended_other, mix_other, preferred_element_type=f32)
    section_output = (pooled.astype(f32) + branch).astype(bf16)
    remote_grads = carried[row_count:].reshape(peer_count, slot_count, 2, half_width)
    returned = lax.all_to_all(remote_grads, "pix", split_axis=0, concat_axis=0, tiled=True)
    returned_rows = jnp.einsum(
        "px,pc->xc",
        send_pick,
        returned.reshape(peer_count * slot_count, 2 * half_width).astype(bf16),
        preferred_element_type=f32,
    )
    local_grads = carried[:row_count] + returned_rows.reshape(row_count, 2, half_width)
    grad_projected = jnp.concatenate(
        [query_grads.reshape(row_count, 1, half_width), local_grads], axis=1
    ).astype(bf16)
    grad_others = ch_exchange(grad_projected)
    projection_term = (
        jnp.einsum("rc,rkd->kcd", pooled_all, grad_projected, preferred_element_type=f32)
        * grad_scale
    )
    early_reduced = pix_scatter((projection_term, mixing_term), mixing_weight.shape[1])
    early_reduced, grad_others = lax.optimization_barrier((early_reduced, grad_others))
    pooled_sum = upstream.astype(f32) + jnp.einsum(
        "rkd,kcd->rc", grad_projected, projections, preferred_element_type=f32
    )
    for grad_other, proj_other in zip(grad_others, proj_others):
        pooled_sum = pooled_sum + jnp.einsum(
            "rkd,kcd->rc", grad_other, proj_other, preferred_element_type=f32
        )
    grad_pooled = pooled_sum.astype(bf16)
    kernel_term = jnp.dot(fine_pixels.T, grad_pooled, preferred_element_type=f32) * grad_scale
    fine_gradient = jnp.dot(grad_pooled, pool_kernel.T, preferred_element_type=f32).astype(bf16)
    kernel_reduced = pix_scatter((kernel_term,), mixing_weight.shape[1])
    projection_gradient, mixing_gradient, kernel_gradient = pix_gather(
        (early_reduced, kernel_reduced), ((projection_term, mixing_term), (kernel_term,))
    )
    return (section_output, fine_gradient, kernel_gradient, projection_gradient, mixing_gradient)


def solution(mesh):
    placed = (
        P("pix", "ch"),
        P("ch", None),
        P(None, None, "ch"),
        P("ch", None),
        P("pix", None),
        P("pix", None),
        P("pix", "ch"),
    )
    return jax.shard_map(
        per_device,
        mesh=mesh,
        in_specs=placed,
        out_specs=(
            P("pix", "ch"),
            P("pix", "ch"),
            P("ch", None),
            P(None, None, "ch"),
            P("ch", None),
        ),
        check_vma=False,
    )
```

```python
import math

import jax
import jax.numpy as jnp
from jax import lax
from jax.sharding import PartitionSpec as P

HD = 64


def pick_table(row_ids, total):
    return (row_ids[:, None] == jnp.arange(total, dtype=jnp.int32)[None, :]).astype(jnp.bfloat16)


def slot_index(neighbour_block, first_row, block_rows):
    present = neighbour_block >= 0
    own_rows = first_row + jnp.arange(block_rows, dtype=jnp.int32)
    slot_rows = jnp.concatenate([own_rows[:, None], jnp.where(present, neighbour_block, 0)], axis=1)
    slot_live = jnp.concatenate([jnp.ones((block_rows, 1), bool), present], axis=1)
    return (slot_rows, slot_live)


def attention_forward(queries, extended, neighbours, row_offset):
    f32 = jnp.float32
    bf16 = jnp.bfloat16
    row_count = queries.shape[0]
    span = queries.shape[1]
    ext_rows = extended.shape[0]
    heads_here = span // HD
    slot_width = neighbours.shape[1] + 1
    score_scale = 1.0 / math.sqrt(HD)
    block_rows = math.gcd(row_count, 512)
    block_count = row_count // block_rows
    block_starts = row_offset + jnp.arange(block_count, dtype=jnp.int32) * block_rows
    query_blocks = queries.reshape(block_count, block_rows, span)
    neighbour_blocks = neighbours.reshape(block_count, block_rows, slot_width - 1)
    flattened = extended.reshape(ext_rows, 2 * span)

    def forward_block(inputs):
        query_block, neighbour_block, first_row = inputs
        slot_rows, slot_live = slot_index(neighbour_block, first_row, block_rows)
        gathered = (
            jnp.dot(
                pick_table(slot_rows.reshape(-1), ext_rows), flattened, preferred_element_type=f32
            )
            .astype(bf16)
            .reshape(block_rows, slot_width, 2, span)
        )
        block_keys = gathered[:, :, 0].reshape(block_rows, slot_width, heads_here, HD)
        block_values = gathered[:, :, 1].reshape(block_rows, slot_width, heads_here, HD)
        scores = (
            jnp.einsum(
                "bhd,bmhd->bhm",
                query_block.reshape(block_rows, heads_here, HD),
                block_keys,
                preferred_element_type=f32,
            )
            * score_scale
        )
        shut = slot_live[:, None, :]
        masked = jnp.where(shut, scores, -1e30)
        largest = jnp.max(masked, axis=2, keepdims=True)
        raised = jnp.where(shut, jnp.exp(masked - largest), 0.0)
        probabilities = raised / jnp.sum(raised, axis=2, keepdims=True)
        weights = probabilities.astype(bf16)
        mixture = jnp.einsum("bhm,bmhd->bhd", weights, block_values, preferred_element_type=f32)
        return (mixture.reshape(block_rows, span).astype(bf16), probabilities, gathered)

    outputs = [
        forward_block((query_blocks[b], neighbour_blocks[b], block_starts[b]))
        for b in range(block_count)
    ]
    attn_blocks = jnp.stack([out[0] for out in outputs])
    prob_blocks = [out[1] for out in outputs]
    kv_blocks = [out[2] for out in outputs]
    return (attn_blocks.reshape(row_count, span), prob_blocks, kv_blocks)


def attention_backward(
    queries, ext_rows, neighbours, row_offset, grad_attended, prob_blocks, kv_blocks, riders
):
    f32 = jnp.float32
    bf16 = jnp.bfloat16
    row_count = queries.shape[0]
    span = queries.shape[1]
    heads_here = span // HD
    slot_width = neighbours.shape[1] + 1
    score_scale = 1.0 / math.sqrt(HD)
    block_rows = math.gcd(row_count, 512)
    block_count = row_count // block_rows
    block_starts = row_offset + jnp.arange(block_count, dtype=jnp.int32) * block_rows
    query_blocks = queries.reshape(block_count, block_rows, span)
    neighbour_blocks = neighbours.reshape(block_count, block_rows, slot_width - 1)
    grad_blocks = grad_attended.reshape(block_count, block_rows, span)

    def backward_block(carried, inputs):
        query_block, neighbour_block, first_row, grad_block, probabilities, gathered = inputs
        slot_rows, slot_live = slot_index(neighbour_block, first_row, block_rows)
        block_keys = gathered[:, :, 0].reshape(block_rows, slot_width, heads_here, HD).astype(f32)
        block_values = gathered[:, :, 1].reshape(block_rows, slot_width, heads_here, HD).astype(f32)
        grad_mix = grad_block.reshape(block_rows, heads_here, HD).astype(f32)
        grad_weights = jnp.einsum("bhd,bmhd->bhm", grad_mix, block_values)
        grad_scores = (
            probabilities
            * (grad_weights - jnp.sum(probabilities * grad_weights, axis=2, keepdims=True))
            * score_scale
        )
        grad_query = jnp.einsum("bhm,bmhd->bhd", grad_scores, block_keys).reshape(block_rows, span)
        query_wide = query_block.reshape(block_rows, heads_here, HD).astype(f32)
        grad_keys = jnp.einsum("bhm,bhd->bmhd", grad_scores, query_wide)
        rounded = lax.optimization_barrier(probabilities.astype(bf16))
        grad_values = jnp.einsum("bhm,bhd->bmhd", rounded.astype(f32), grad_mix)
        contribution = (
            jnp.stack([grad_keys, grad_values], axis=2)
            .reshape(block_rows, slot_width, 2 * span)
            .astype(bf16)
        )
        carried = carried + jnp.einsum(
            "bx,bc->xc",
            pick_table(slot_rows.reshape(-1), ext_rows),
            contribution.reshape(block_rows * slot_width, 2 * span),
            preferred_element_type=f32,
        )
        return (carried, grad_query)

    carried = jnp.zeros((ext_rows, 2 * span), f32)
    query_grads = []
    for b in range(block_count):
        carried, grad_query = backward_block(
            carried,
            (query_blocks[b], neighbour_blocks[b], block_starts[b], grad_blocks[b],
             prob_blocks[b], kv_blocks[b]),
        )
        query_grads.append(grad_query)
        if b == 0:
            carried, riders = lax.optimization_barrier((carried, riders))
    query_grads = jnp.stack(query_grads)
    return (carried.reshape(ext_rows, 2, span), query_grads.reshape(row_count, span), riders)


def ch_exchange(value):
    size = lax.axis_size("ch")
    return [
        lax.ppermute(value, "ch", [(i, (i + shift) % size) for i in range(size)])
        for shift in range(1, size)
    ]


def ch_assemble(own, others, axis):
    size = len(others) + 1
    index = lax.axis_index("ch")
    pieces = [own] + others
    result = None
    for case in range(size):
        ordered = jnp.concatenate([pieces[(case - j) % size] for j in range(size)], axis=axis)
        result = ordered if result is None else jnp.where(index == case, ordered, result)
    return result


def core_swap(value):
    size = lax.axis_size("pix")
    return lax.ppermute(value, "pix", [(i, i ^ 1) for i in range(size)])


def pix_scatter(terms, width):
    size = lax.axis_size("pix")
    core = lax.axis_index("pix") % 2
    flat = jnp.concatenate([term.reshape(-1, width) for term in terms], axis=0)
    rows = flat.shape[0]
    chunk = -(-rows // (2 * size))
    flat = jnp.pad(flat, ((0, 2 * size * chunk - rows), (0, 0)))
    halves = flat.reshape(2, size * chunk, width)
    keep = jnp.where(core == 0, halves[0], halves[1])
    send = jnp.where(core == 0, halves[1], halves[0])
    mine = keep + core_swap(send)
    parts = lax.all_to_all(mine.reshape(size, chunk, width), "pix", 0, 0, tiled=True)
    return jnp.sum(parts.reshape(size // 2, 2, chunk, width), axis=0)


def pix_gather(reduced_groups, term_groups):
    size = lax.axis_size("pix")
    core = lax.axis_index("pix") % 2
    width = reduced_groups[0].shape[-1]
    joined = jnp.concatenate(reduced_groups, axis=1)
    total = joined.shape[1]
    spread = jnp.broadcast_to(joined[None], (size // 2, 2, total, width))
    got = lax.all_to_all(spread.reshape(size, total, width), "pix", 0, 0, tiled=True)
    other = core_swap(got)
    first = jnp.where(core == 0, got, other)
    second = jnp.where(core == 0, other, got)
    results = []
    offset = 0
    for reduced, terms in zip(reduced_groups, term_groups):
        chunk = reduced.shape[1]
        flat = jnp.concatenate(
            [
                first[:, offset : offset + chunk].reshape(size * chunk, width),
                second[:, offset : offset + chunk].reshape(size * chunk, width),
            ],
            axis=0,
        )
        offset += chunk
        row = 0
        for term in terms:
            count = term.size // width
            results.append(flat[row : row + count].reshape(term.shape))
            row += count
    return results


def per_device(
    fine_pixels, pool_kernel, projections, mixing_weight, send_list, neighbours, cotangent
):
    f32 = jnp.float32
    bf16 = jnp.bfloat16
    row_count = fine_pixels.shape[0]
    half_width = projections.shape[2]
    ch_size = lax.axis_size("ch")
    ch_index = lax.axis_index("ch")
    peer_count = lax.axis_size("pix")
    slot_count = send_list.shape[1]
    grad_scale = 1.0 / math.sqrt(row_count * peer_count)
    send_pick = pick_table(send_list.reshape(-1), row_count)
    fine_others = ch_exchange(fine_pixels)
    kernel_others = ch_exchange(pool_kernel)
    pooled_sum = jnp.dot(fine_pixels, pool_kernel, preferred_element_type=f32)
    for fine_other, kernel_other in zip(fine_others, kernel_others):
        pooled_sum = pooled_sum + jnp.dot(fine_other, kernel_other, preferred_element_type=f32)
    pooled_all = pooled_sum.astype(bf16)
    mix_pieces = mixing_weight.reshape(mixing_weight.shape[0], ch_size, half_width)
    mix_sends = [
        jnp.take(mix_pieces, (ch_index + shift) % ch_size, axis=1) for shift in range(1, ch_size)
    ]
    pooled_all, cot_send, proj_send, mix_sends = lax.optimization_barrier(
        (pooled_all, cotangent, projections, mix_sends)
    )
    cot_others = ch_exchange(cot_send)
    proj_others = ch_exchange(proj_send)
    mix_others = [
        lax.ppermute(mix_send, "ch", [(i, (i + shift) % ch_size) for i in range(ch_size)])
        for shift, mix_send in zip(range(1, ch_size), mix_sends)
    ]
    mix_own = jnp.take(mix_pieces, ch_index, axis=1)
    pooled = lax.dynamic_slice_in_dim(pooled_all, ch_index * half_width, half_width, axis=1)
    upstream = ch_assemble(cotangent, cot_others, axis=1)
    projected = jnp.einsum(
        "rc,kcd->rkd", pooled_all, projections, preferred_element_type=f32
    ).astype(bf16)
    queries = projected[:, 0]
    key_value = projected[:, 1:]
    outgoing = (
        jnp.dot(send_pick, key_value.reshape(row_count, 2 * half_width), preferred_element_type=f32)
        .astype(bf16)
        .reshape(peer_count, slot_count, 2, half_width)
    )
    incoming = lax.all_to_all(outgoing, "pix", split_axis=0, concat_axis=0, tiled=True)
    extended = jnp.concatenate(
        [key_value, incoming.reshape(peer_count * slot_count, 2, half_width)], axis=0
    )
    attended, prob_blocks, kv_blocks = attention_forward(queries, extended, neighbours, 0)
    attended_others = ch_exchange(attended)
    grad_attended = jnp.dot(upstream, mixing_weight.T, preferred_element_type=f32).astype(bf16)
    grad_attended, proj_others = lax.optimization_barrier((grad_attended, proj_others))
    mixing_term = jnp.dot(attended.T, upstream, preferred_element_type=f32) * grad_scale
    carried, query_grads, (attended_others, mix_others) = attention_backward(
        queries, extended.shape[0], neighbours, 0, grad_attended, prob_blocks, kv_blocks,
        (attended_others, mix_others),
    )
    branch = jnp.dot(attended, mix_own, preferred_element_type=f32)
    for attended_other, mix_other in zip(attended_others, mix_others):
        branch = branch + jnp.dot(attended_other, mix_other, preferred_element_type=f32)
    section_output = (pooled.astype(f32) + branch).astype(bf16)
    remote_grads = carried[row_count:].reshape(peer_count, slot_count, 2, half_width)
    returned = lax.all_to_all(remote_grads, "pix", split_axis=0, concat_axis=0, tiled=True)
    returned_rows = jnp.einsum(
        "px,pc->xc",
        send_pick,
        returned.reshape(peer_count * slot_count, 2 * half_width).astype(bf16),
        preferred_element_type=f32,
    )
    local_grads = carried[:row_count] + returned_rows.reshape(row_count, 2, half_width)
    grad_projected = jnp.concatenate(
        [query_grads.reshape(row_count, 1, half_width), local_grads], axis=1
    ).astype(bf16)
    grad_others = ch_exchange(grad_projected)
    projection_term = (
        jnp.einsum("rc,rkd->kcd", pooled_all, grad_projected, preferred_element_type=f32)
        * grad_scale
    )
    early_reduced = pix_scatter((projection_term, mixing_term), mixing_weight.shape[1])
    early_reduced, grad_others = lax.optimization_barrier((early_reduced, grad_others))
    pooled_sum = upstream.astype(f32) + jnp.einsum(
        "rkd,kcd->rc", grad_projected, projections, preferred_element_type=f32
    )
    for grad_other, proj_other in zip(grad_others, proj_others):
        pooled_sum = pooled_sum + jnp.einsum(
            "rkd,kcd->rc", grad_other, proj_other, preferred_element_type=f32
        )
    grad_pooled = pooled_sum.astype(bf16)
    kernel_term = jnp.dot(fine_pixels.T, grad_pooled, preferred_element_type=f32) * grad_scale
    fine_gradient = jnp.dot(grad_pooled, pool_kernel.T, preferred_element_type=f32).astype(bf16)
    kernel_reduced = pix_scatter((kernel_term,), mixing_weight.shape[1])
    projection_gradient, mixing_gradient, kernel_gradient = pix_gather(
        (early_reduced, kernel_reduced), ((projection_term, mixing_term), (kernel_term,))
    )
    return (section_output, fine_gradient, kernel_gradient, projection_gradient, mixing_gradient)


def solution(mesh):
    placed = (
        P("pix", "ch"),
        P("ch", None),
        P(None, None, "ch"),
        P("ch", None),
        P("pix", None),
        P("pix", None),
        P("pix", "ch"),
    )
    return jax.shard_map(
        per_device,
        mesh=mesh,
        in_specs=placed,
        out_specs=(
            P("pix", "ch"),
            P("pix", "ch"),
            P("ch", None),
            P(None, None, "ch"),
            P("ch", None),
        ),
        check_vma=False,
    )
```

```python
import math

import jax
import jax.numpy as jnp
from jax import lax
from jax.sharding import PartitionSpec as P

HD = 64


def pick_table(row_ids, total):
    return (row_ids[:, None] == jnp.arange(total, dtype=jnp.int32)[None, :]).astype(jnp.bfloat16)


def slot_index(neighbour_block, first_row, block_rows):
    present = neighbour_block >= 0
    own_rows = first_row + jnp.arange(block_rows, dtype=jnp.int32)
    slot_rows = jnp.concatenate([own_rows[:, None], jnp.where(present, neighbour_block, 0)], axis=1)
    slot_live = jnp.concatenate([jnp.ones((block_rows, 1), bool), present], axis=1)
    return (slot_rows, slot_live)


def attention_forward(queries, extended, neighbours, row_offset):
    f32 = jnp.float32
    bf16 = jnp.bfloat16
    row_count = queries.shape[0]
    span = queries.shape[1]
    ext_rows = extended.shape[0]
    heads_here = span // HD
    slot_width = neighbours.shape[1] + 1
    score_scale = 1.0 / math.sqrt(HD)
    block_rows = math.gcd(row_count, 512)
    block_count = row_count // block_rows
    query_blocks = queries.reshape(block_count, block_rows, span)
    neighbour_blocks = neighbours.reshape(block_count, block_rows, slot_width - 1)
    flattened = extended.reshape(ext_rows, 2 * span)

    def forward_block(inputs):
        query_block, neighbour_block, first_row = inputs
        slot_rows, slot_live = slot_index(neighbour_block, first_row, block_rows)
        pieces = [flattened[first_row : first_row + block_rows]] + [
            jnp.dot(
                pick_table(slot_rows[:, slot], ext_rows), flattened, preferred_element_type=f32
            ).astype(bf16)
            for slot in range(1, slot_width)
        ]
        gathered = jnp.stack(pieces, axis=1).reshape(block_rows, slot_width, 2, span)
        block_keys = gathered[:, :, 0].reshape(block_rows, slot_width, heads_here, HD)
        block_values = gathered[:, :, 1].reshape(block_rows, slot_width, heads_here, HD)
        scores = (
            jnp.einsum(
                "bhd,bmhd->bhm",
                query_block.reshape(block_rows, heads_here, HD),
                block_keys,
                preferred_element_type=f32,
            )
            * score_scale
        )
        shut = slot_live[:, None, :]
        masked = jnp.where(shut, scores, -1e30)
        largest = jnp.max(masked, axis=2, keepdims=True)
        raised = jnp.where(shut, jnp.exp(masked - largest), 0.0)
        probabilities = raised / jnp.sum(raised, axis=2, keepdims=True)
        weights = probabilities.astype(bf16)
        mixture = jnp.einsum("bhm,bmhd->bhd", weights, block_values, preferred_element_type=f32)
        return (mixture.reshape(block_rows, span).astype(bf16), probabilities, gathered)

    outputs = [
        forward_block((query_blocks[b], neighbour_blocks[b], row_offset + b * block_rows))
        for b in range(block_count)
    ]
    attn_blocks = jnp.stack([out[0] for out in outputs])
    prob_blocks = [out[1] for out in outputs]
    kv_blocks = [out[2] for out in outputs]
    return (attn_blocks.reshape(row_count, span), prob_blocks, kv_blocks)


def attention_backward(
    queries, ext_rows, neighbours, row_offset, grad_attended, prob_blocks, kv_blocks, riders
):
    f32 = jnp.float32
    bf16 = jnp.bfloat16
    row_count = queries.shape[0]
    span = queries.shape[1]
    heads_here = span // HD
    slot_width = neighbours.shape[1] + 1
    score_scale = 1.0 / math.sqrt(HD)
    block_rows = math.gcd(row_count, 512)
    block_count = row_count // block_rows
    query_blocks = queries.reshape(block_count, block_rows, span)
    neighbour_blocks = neighbours.reshape(block_count, block_rows, slot_width - 1)
    grad_blocks = grad_attended.reshape(block_count, block_rows, span)

    def backward_block(carried, inputs):
        query_block, neighbour_block, first_row, grad_block, probabilities, gathered = inputs
        slot_rows, slot_live = slot_index(neighbour_block, first_row, block_rows)
        block_keys = gathered[:, :, 0].reshape(block_rows, slot_width, heads_here, HD).astype(f32)
        block_values = gathered[:, :, 1].reshape(block_rows, slot_width, heads_here, HD).astype(f32)
        grad_mix = grad_block.reshape(block_rows, heads_here, HD).astype(f32)
        grad_weights = jnp.einsum("bhd,bmhd->bhm", grad_mix, block_values)
        grad_scores = (
            probabilities
            * (grad_weights - jnp.sum(probabilities * grad_weights, axis=2, keepdims=True))
            * score_scale
        )
        grad_query = jnp.einsum("bhm,bmhd->bhd", grad_scores, block_keys).reshape(block_rows, span)
        query_wide = query_block.reshape(block_rows, heads_here, HD).astype(f32)
        grad_keys = jnp.einsum("bhm,bhd->bmhd", grad_scores, query_wide)
        rounded = lax.optimization_barrier(probabilities.astype(bf16))
        grad_values = jnp.einsum("bhm,bhd->bmhd", rounded.astype(f32), grad_mix)
        contribution = (
            jnp.stack([grad_keys, grad_values], axis=2)
            .reshape(block_rows, slot_width, 2 * span)
            .astype(bf16)
        )
        for slot in range(1, slot_width):
            carried = carried + jnp.einsum(
                "bx,bc->xc",
                pick_table(slot_rows[:, slot], ext_rows),
                contribution[:, slot],
                preferred_element_type=f32,
            )
        return (carried, (grad_query, contribution[:, 0]))

    carried = jnp.zeros((ext_rows, 2 * span), f32)
    query_grads = []
    for b in range(block_count):
        carried, grad_query = backward_block(
            carried,
            (query_blocks[b], neighbour_blocks[b], row_offset + b * block_rows, grad_blocks[b],
             prob_blocks[b], kv_blocks[b]),
        )
        query_grads.append(grad_query)
        if b == 0:
            carried, riders = lax.optimization_barrier((carried, riders))
    own_grads = jnp.concatenate([pair[1] for pair in query_grads], axis=0)
    query_grads = jnp.stack([pair[0] for pair in query_grads])
    carried = carried.at[:row_count].add(own_grads.astype(f32))
    return (carried.reshape(ext_rows, 2, span), query_grads.reshape(row_count, span), riders)


def ch_exchange(value):
    size = lax.axis_size("ch")
    return [
        lax.ppermute(value, "ch", [(i, (i + shift) % size) for i in range(size)])
        for shift in range(1, size)
    ]


def ch_assemble(own, others, axis):
    size = len(others) + 1
    index = lax.axis_index("ch")
    pieces = [own] + others
    result = None
    for case in range(size):
        ordered = jnp.concatenate([pieces[(case - j) % size] for j in range(size)], axis=axis)
        result = ordered if result is None else jnp.where(index == case, ordered, result)
    return result


def core_swap(value):
    size = lax.axis_size("pix")
    return lax.ppermute(value, "pix", [(i, i ^ 1) for i in range(size)])


def pix_scatter(terms, width):
    size = lax.axis_size("pix")
    core = lax.axis_index("pix") % 2
    flat = jnp.concatenate([term.reshape(-1, width) for term in terms], axis=0)
    rows = flat.shape[0]
    chunk = -(-rows // (2 * size))
    flat = jnp.pad(flat, ((0, 2 * size * chunk - rows), (0, 0)))
    halves = flat.reshape(2, size * chunk, width)
    keep = jnp.where(core == 0, halves[0], halves[1])
    send = jnp.where(core == 0, halves[1], halves[0])
    mine = keep + core_swap(send)
    parts = lax.all_to_all(mine.reshape(size, chunk, width), "pix", 0, 0, tiled=True)
    return jnp.sum(parts.reshape(size // 2, 2, chunk, width), axis=0)


def pix_gather(reduced_groups, term_groups):
    size = lax.axis_size("pix")
    core = lax.axis_index("pix") % 2
    width = reduced_groups[0].shape[-1]
    joined = jnp.concatenate(reduced_groups, axis=1)
    total = joined.shape[1]
    spread = jnp.broadcast_to(joined[None], (size // 2, 2, total, width))
    got = lax.all_to_all(spread.reshape(size, total, width), "pix", 0, 0, tiled=True)
    other = core_swap(got)
    first = jnp.where(core == 0, got, other)
    second = jnp.where(core == 0, other, got)
    results = []
    offset = 0
    for reduced, terms in zip(reduced_groups, term_groups):
        chunk = reduced.shape[1]
        flat = jnp.concatenate(
            [
                first[:, offset : offset + chunk].reshape(size * chunk, width),
                second[:, offset : offset + chunk].reshape(size * chunk, width),
            ],
            axis=0,
        )
        offset += chunk
        row = 0
        for term in terms:
            count = term.size // width
            results.append(flat[row : row + count].reshape(term.shape))
            row += count
    return results


def per_device(
    fine_pixels, pool_kernel, projections, mixing_weight, send_list, neighbours, cotangent
):
    f32 = jnp.float32
    bf16 = jnp.bfloat16
    row_count = fine_pixels.shape[0]
    half_width = projections.shape[2]
    ch_size = lax.axis_size("ch")
    ch_index = lax.axis_index("ch")
    peer_count = lax.axis_size("pix")
    slot_count = send_list.shape[1]
    grad_scale = 1.0 / math.sqrt(row_count * peer_count)
    send_pick = pick_table(send_list.reshape(-1), row_count)
    fine_others = ch_exchange(fine_pixels)
    kernel_others = ch_exchange(pool_kernel)
    pooled_sum = jnp.dot(fine_pixels, pool_kernel, preferred_element_type=f32)
    for fine_other, kernel_other in zip(fine_others, kernel_others):
        pooled_sum = pooled_sum + jnp.dot(fine_other, kernel_other, preferred_element_type=f32)
    pooled_all = pooled_sum.astype(bf16)
    mix_pieces = mixing_weight.reshape(mixing_weight.shape[0], ch_size, half_width)
    mix_sends = [
        jnp.take(mix_pieces, (ch_index + shift) % ch_size, axis=1) for shift in range(1, ch_size)
    ]
    pooled_all, cot_send, proj_send, mix_sends = lax.optimization_barrier(
        (pooled_all, cotangent, projections, mix_sends)
    )
    cot_others = ch_exchange(cot_send)
    proj_others = ch_exchange(proj_send)
    mix_others = [
        lax.ppermute(mix_send, "ch", [(i, (i + shift) % ch_size) for i in range(ch_size)])
        for shift, mix_send in zip(range(1, ch_size), mix_sends)
    ]
    mix_own = jnp.take(mix_pieces, ch_index, axis=1)
    pooled = lax.dynamic_slice_in_dim(pooled_all, ch_index * half_width, half_width, axis=1)
    upstream = ch_assemble(cotangent, cot_others, axis=1)
    projected = jnp.einsum(
        "rc,kcd->rkd", pooled_all, projections, preferred_element_type=f32
    ).astype(bf16)
    queries = projected[:, 0]
    key_value = projected[:, 1:]
    outgoing = (
        jnp.dot(send_pick, key_value.reshape(row_count, 2 * half_width), preferred_element_type=f32)
        .astype(bf16)
        .reshape(peer_count, slot_count, 2, half_width)
    )
    incoming = lax.all_to_all(outgoing, "pix", split_axis=0, concat_axis=0, tiled=True)
    extended = jnp.concatenate(
        [key_value, incoming.reshape(peer_count * slot_count, 2, half_width)], axis=0
    )
    attended, prob_blocks, kv_blocks = attention_forward(queries, extended, neighbours, 0)
    attended_others = ch_exchange(attended)
    grad_attended = jnp.dot(upstream, mixing_weight.T, preferred_element_type=f32).astype(bf16)
    grad_attended, proj_others = lax.optimization_barrier((grad_attended, proj_others))
    mixing_term = jnp.dot(attended.T, upstream, preferred_element_type=f32) * grad_scale
    carried, query_grads, (attended_others, mix_others) = attention_backward(
        queries, extended.shape[0], neighbours, 0, grad_attended, prob_blocks, kv_blocks,
        (attended_others, mix_others),
    )
    branch = jnp.dot(attended, mix_own, preferred_element_type=f32)
    for attended_other, mix_other in zip(attended_others, mix_others):
        branch = branch + jnp.dot(attended_other, mix_other, preferred_element_type=f32)
    section_output = (pooled.astype(f32) + branch).astype(bf16)
    remote_grads = carried[row_count:].reshape(peer_count, slot_count, 2, half_width)
    returned = lax.all_to_all(remote_grads, "pix", split_axis=0, concat_axis=0, tiled=True)
    returned_rows = jnp.einsum(
        "px,pc->xc",
        send_pick,
        returned.reshape(peer_count * slot_count, 2 * half_width).astype(bf16),
        preferred_element_type=f32,
    )
    local_grads = carried[:row_count] + returned_rows.reshape(row_count, 2, half_width)
    grad_projected = jnp.concatenate(
        [query_grads.reshape(row_count, 1, half_width), local_grads], axis=1
    ).astype(bf16)
    grad_others = ch_exchange(grad_projected)
    projection_term = (
        jnp.einsum("rc,rkd->kcd", pooled_all, grad_projected, preferred_element_type=f32)
        * grad_scale
    )
    early_reduced = pix_scatter((projection_term, mixing_term), mixing_weight.shape[1])
    early_reduced, grad_others = lax.optimization_barrier((early_reduced, grad_others))
    pooled_sum = upstream.astype(f32) + jnp.einsum(
        "rkd,kcd->rc", grad_projected, projections, preferred_element_type=f32
    )
    for grad_other, proj_other in zip(grad_others, proj_others):
        pooled_sum = pooled_sum + jnp.einsum(
            "rkd,kcd->rc", grad_other, proj_other, preferred_element_type=f32
        )
    grad_pooled = pooled_sum.astype(bf16)
    kernel_term = jnp.dot(fine_pixels.T, grad_pooled, preferred_element_type=f32) * grad_scale
    fine_gradient = jnp.dot(grad_pooled, pool_kernel.T, preferred_element_type=f32).astype(bf16)
    kernel_reduced = pix_scatter((kernel_term,), mixing_weight.shape[1])
    projection_gradient, mixing_gradient, kernel_gradient = pix_gather(
        (early_reduced, kernel_reduced), ((projection_term, mixing_term), (kernel_term,))
    )
    return (section_output, fine_gradient, kernel_gradient, projection_gradient, mixing_gradient)


def solution(mesh):
    placed = (
        P("pix", "ch"),
        P("ch", None),
        P(None, None, "ch"),
        P("ch", None),
        P("pix", None),
        P("pix", None),
        P("pix", "ch"),
    )
    return jax.shard_map(
        per_device,
        mesh=mesh,
        in_specs=placed,
        out_specs=(
            P("pix", "ch"),
            P("pix", "ch"),
            P("ch", None),
            P(None, None, "ch"),
            P("ch", None),
        ),
        check_vma=False,
    )
```

```python
import math

import jax
import jax.numpy as jnp
from jax import lax
from jax.sharding import PartitionSpec as P

HD = 64


def pick_table(row_ids, total):
    return (row_ids[:, None] == jnp.arange(total, dtype=jnp.int32)[None, :]).astype(jnp.bfloat16)


def slot_index(neighbour_block, first_row, block_rows):
    present = neighbour_block >= 0
    own_rows = first_row + jnp.arange(block_rows, dtype=jnp.int32)
    slot_rows = jnp.concatenate([own_rows[:, None], jnp.where(present, neighbour_block, 0)], axis=1)
    slot_live = jnp.concatenate([jnp.ones((block_rows, 1), bool), present], axis=1)
    return (slot_rows, slot_live)


def attention_forward(queries, extended, neighbours, row_offset):
    f32 = jnp.float32
    bf16 = jnp.bfloat16
    row_count = queries.shape[0]
    span = queries.shape[1]
    ext_rows = extended.shape[0]
    heads_here = span // HD
    slot_width = neighbours.shape[1] + 1
    score_scale = 1.0 / math.sqrt(HD)
    block_rows = math.gcd(row_count, 512)
    block_count = row_count // block_rows
    query_blocks = queries.reshape(block_count, block_rows, span)
    neighbour_blocks = neighbours.reshape(block_count, block_rows, slot_width - 1)
    flattened = extended.reshape(ext_rows, 2 * span)

    def forward_block(inputs):
        query_block, neighbour_block, first_row = inputs
        slot_rows, slot_live = slot_index(neighbour_block, first_row, block_rows)
        pieces = [flattened[first_row : first_row + block_rows]] + [
            jnp.dot(
                pick_table(slot_rows[:, slot], ext_rows), flattened, preferred_element_type=f32
            ).astype(bf16)
            for slot in range(1, slot_width)
        ]
        gathered = jnp.stack(pieces, axis=1).reshape(block_rows, slot_width, 2, span)
        block_keys = gathered[:, :, 0].reshape(block_rows, slot_width, heads_here, HD)
        block_values = gathered[:, :, 1].reshape(block_rows, slot_width, heads_here, HD)
        scores = (
            jnp.einsum(
                "bhd,bmhd->bhm",
                query_block.reshape(block_rows, heads_here, HD),
                block_keys,
                preferred_element_type=f32,
            )
            * score_scale
        )
        shut = slot_live[:, None, :]
        masked = jnp.where(shut, scores, -1e30)
        largest = jnp.max(masked, axis=2, keepdims=True)
        raised = jnp.where(shut, jnp.exp(masked - largest), 0.0)
        probabilities = raised / jnp.sum(raised, axis=2, keepdims=True)
        weights = probabilities.astype(bf16)
        mixture = jnp.einsum("bhm,bmhd->bhd", weights, block_values, preferred_element_type=f32)
        return (mixture.reshape(block_rows, span).astype(bf16), probabilities, gathered)

    outputs = [
        forward_block((query_blocks[b], neighbour_blocks[b], row_offset + b * block_rows))
        for b in range(block_count)
    ]
    attn_blocks = jnp.stack([out[0] for out in outputs])
    prob_blocks = [out[1] for out in outputs]
    kv_blocks = [out[2] for out in outputs]
    return (attn_blocks.reshape(row_count, span), prob_blocks, kv_blocks)


def attention_backward(
    queries, ext_rows, neighbours, row_offset, grad_attended, prob_blocks, kv_blocks, riders
):
    f32 = jnp.float32
    bf16 = jnp.bfloat16
    row_count = queries.shape[0]
    span = queries.shape[1]
    heads_here = span // HD
    slot_width = neighbours.shape[1] + 1
    score_scale = 1.0 / math.sqrt(HD)
    block_rows = math.gcd(row_count, 512)
    block_count = row_count // block_rows
    query_blocks = queries.reshape(block_count, block_rows, span)
    neighbour_blocks = neighbours.reshape(block_count, block_rows, slot_width - 1)
    grad_blocks = grad_attended.reshape(block_count, block_rows, span)

    def backward_block(carried, inputs):
        query_block, neighbour_block, first_row, grad_block, probabilities, gathered = inputs
        slot_rows, slot_live = slot_index(neighbour_block, first_row, block_rows)
        block_keys = gathered[:, :, 0].reshape(block_rows, slot_width, heads_here, HD).astype(f32)
        block_values = gathered[:, :, 1].reshape(block_rows, slot_width, heads_here, HD).astype(f32)
        grad_mix = grad_block.reshape(block_rows, heads_here, HD).astype(f32)
        grad_weights = jnp.einsum("bhd,bmhd->bhm", grad_mix, block_values)
        grad_scores = (
            probabilities
            * (grad_weights - jnp.sum(probabilities * grad_weights, axis=2, keepdims=True))
            * score_scale
        )
        grad_query = jnp.einsum("bhm,bmhd->bhd", grad_scores, block_keys).reshape(block_rows, span)
        query_wide = query_block.reshape(block_rows, heads_here, HD).astype(f32)
        grad_keys = jnp.einsum("bhm,bhd->bmhd", grad_scores, query_wide)
        rounded = lax.optimization_barrier(probabilities.astype(bf16))
        grad_values = jnp.einsum("bhm,bhd->bmhd", rounded.astype(f32), grad_mix)
        contribution = (
            jnp.stack([grad_keys, grad_values], axis=2)
            .reshape(block_rows, slot_width, 2 * span)
            .astype(bf16)
        )
        for slot in range(1, slot_width):
            carried = carried + jnp.einsum(
                "bx,bc->xc",
                pick_table(slot_rows[:, slot], ext_rows),
                contribution[:, slot],
                preferred_element_type=f32,
            )
        return (carried, (grad_query, contribution[:, 0]))

    carried = jnp.zeros((ext_rows, 2 * span), f32)
    query_grads = []
    for b in range(block_count):
        carried, grad_query = backward_block(
            carried,
            (query_blocks[b], neighbour_blocks[b], row_offset + b * block_rows, grad_blocks[b],
             prob_blocks[b], kv_blocks[b]),
        )
        query_grads.append(grad_query)
        if b == 0:
            carried, riders = lax.optimization_barrier((carried, riders))
    own_grads = jnp.concatenate([pair[1] for pair in query_grads], axis=0)
    query_grads = jnp.stack([pair[0] for pair in query_grads])
    carried = carried.at[:row_count].add(own_grads.astype(f32))
    return (carried.reshape(ext_rows, 2, span), query_grads.reshape(row_count, span), riders)


def ch_exchange(value):
    size = lax.axis_size("ch")
    return [
        lax.ppermute(value, "ch", [(i, (i + shift) % size) for i in range(size)])
        for shift in range(1, size)
    ]


def ch_assemble(own, others, axis):
    size = len(others) + 1
    index = lax.axis_index("ch")
    pieces = [own] + others
    result = None
    for case in range(size):
        ordered = jnp.concatenate([pieces[(case - j) % size] for j in range(size)], axis=axis)
        result = ordered if result is None else jnp.where(index == case, ordered, result)
    return result


def core_swap(value):
    size = lax.axis_size("pix")
    return lax.ppermute(value, "pix", [(i, i ^ 1) for i in range(size)])


def pix_scatter(terms, width):
    size = lax.axis_size("pix")
    core = lax.axis_index("pix") % 2
    flat = jnp.concatenate([term.reshape(-1, width) for term in terms], axis=0)
    rows = flat.shape[0]
    chunk = -(-rows // (2 * size))
    flat = jnp.pad(flat, ((0, 2 * size * chunk - rows), (0, 0)))
    halves = flat.reshape(2, size * chunk, width)
    keep = jnp.where(core == 0, halves[0], halves[1])
    send = jnp.where(core == 0, halves[1], halves[0])
    mine = (keep + core_swap(send)).astype(jnp.bfloat16)
    parts = lax.all_to_all(mine.reshape(size, chunk, width), "pix", 0, 0, tiled=True)
    return jnp.sum(parts.reshape(size // 2, 2, chunk, width).astype(jnp.float32), axis=0)


def pix_gather(reduced_groups, term_groups):
    size = lax.axis_size("pix")
    core = lax.axis_index("pix") % 2
    width = reduced_groups[0].shape[-1]
    joined = jnp.concatenate(reduced_groups, axis=1)
    total = joined.shape[1]
    spread = jnp.broadcast_to(joined[None], (size // 2, 2, total, width))
    got = lax.all_to_all(spread.reshape(size, total, width), "pix", 0, 0, tiled=True)
    other = core_swap(got)
    first = jnp.where(core == 0, got, other)
    second = jnp.where(core == 0, other, got)
    results = []
    offset = 0
    for reduced, terms in zip(reduced_groups, term_groups):
        chunk = reduced.shape[1]
        flat = jnp.concatenate(
            [
                first[:, offset : offset + chunk].reshape(size * chunk, width),
                second[:, offset : offset + chunk].reshape(size * chunk, width),
            ],
            axis=0,
        )
        offset += chunk
        row = 0
        for term in terms:
            count = term.size // width
            results.append(flat[row : row + count].reshape(term.shape))
            row += count
    return results


def per_device(
    fine_pixels, pool_kernel, projections, mixing_weight, send_list, neighbours, cotangent
):
    f32 = jnp.float32
    bf16 = jnp.bfloat16
    row_count = fine_pixels.shape[0]
    half_width = projections.shape[2]
    ch_size = lax.axis_size("ch")
    ch_index = lax.axis_index("ch")
    peer_count = lax.axis_size("pix")
    slot_count = send_list.shape[1]
    grad_scale = 1.0 / math.sqrt(row_count * peer_count)
    send_pick = pick_table(send_list.reshape(-1), row_count)
    fine_others = ch_exchange(fine_pixels)
    kernel_others = ch_exchange(pool_kernel)
    pooled_sum = jnp.dot(fine_pixels, pool_kernel, preferred_element_type=f32)
    for fine_other, kernel_other in zip(fine_others, kernel_others):
        pooled_sum = pooled_sum + jnp.dot(fine_other, kernel_other, preferred_element_type=f32)
    pooled_all = pooled_sum.astype(bf16)
    mix_pieces = mixing_weight.reshape(mixing_weight.shape[0], ch_size, half_width)
    mix_sends = [
        jnp.take(mix_pieces, (ch_index + shift) % ch_size, axis=1) for shift in range(1, ch_size)
    ]
    pooled_all, cot_send, proj_send, mix_sends = lax.optimization_barrier(
        (pooled_all, cotangent, projections, mix_sends)
    )
    cot_others = ch_exchange(cot_send)
    proj_others = ch_exchange(proj_send)
    mix_others = [
        lax.ppermute(mix_send, "ch", [(i, (i + shift) % ch_size) for i in range(ch_size)])
        for shift, mix_send in zip(range(1, ch_size), mix_sends)
    ]
    mix_own = jnp.take(mix_pieces, ch_index, axis=1)
    pooled = lax.dynamic_slice_in_dim(pooled_all, ch_index * half_width, half_width, axis=1)
    upstream = ch_assemble(cotangent, cot_others, axis=1)
    projected = jnp.einsum(
        "rc,kcd->rkd", pooled_all, projections, preferred_element_type=f32
    ).astype(bf16)
    queries = projected[:, 0]
    key_value = projected[:, 1:]
    outgoing = (
        jnp.dot(send_pick, key_value.reshape(row_count, 2 * half_width), preferred_element_type=f32)
        .astype(bf16)
        .reshape(peer_count, slot_count, 2, half_width)
    )
    incoming = lax.all_to_all(outgoing, "pix", split_axis=0, concat_axis=0, tiled=True)
    extended = jnp.concatenate(
        [key_value, incoming.reshape(peer_count * slot_count, 2, half_width)], axis=0
    )
    attended, prob_blocks, kv_blocks = attention_forward(queries, extended, neighbours, 0)
    attended_others = ch_exchange(attended)
    grad_attended = jnp.dot(upstream, mixing_weight.T, preferred_element_type=f32).astype(bf16)
    grad_attended, proj_others = lax.optimization_barrier((grad_attended, proj_others))
    mixing_term = jnp.dot(attended.T, upstream, preferred_element_type=f32) * grad_scale
    carried, query_grads, (attended_others, mix_others) = attention_backward(
        queries, extended.shape[0], neighbours, 0, grad_attended, prob_blocks, kv_blocks,
        (attended_others, mix_others),
    )
    branch = jnp.dot(attended, mix_own, preferred_element_type=f32)
    for attended_other, mix_other in zip(attended_others, mix_others):
        branch = branch + jnp.dot(attended_other, mix_other, preferred_element_type=f32)
    section_output = (pooled.astype(f32) + branch).astype(bf16)
    remote_grads = carried[row_count:].reshape(peer_count, slot_count, 2, half_width)
    returned = lax.all_to_all(remote_grads, "pix", split_axis=0, concat_axis=0, tiled=True)
    returned_rows = jnp.einsum(
        "px,pc->xc",
        send_pick,
        returned.reshape(peer_count * slot_count, 2 * half_width).astype(bf16),
        preferred_element_type=f32,
    )
    local_grads = carried[:row_count] + returned_rows.reshape(row_count, 2, half_width)
    grad_projected = jnp.concatenate(
        [query_grads.reshape(row_count, 1, half_width), local_grads], axis=1
    ).astype(bf16)
    grad_others = ch_exchange(grad_projected)
    projection_term = (
        jnp.einsum("rc,rkd->kcd", pooled_all, grad_projected, preferred_element_type=f32)
        * grad_scale
    )
    early_reduced = pix_scatter((projection_term, mixing_term), mixing_weight.shape[1])
    early_reduced, grad_others = lax.optimization_barrier((early_reduced, grad_others))
    pooled_sum = upstream.astype(f32) + jnp.einsum(
        "rkd,kcd->rc", grad_projected, projections, preferred_element_type=f32
    )
    for grad_other, proj_other in zip(grad_others, proj_others):
        pooled_sum = pooled_sum + jnp.einsum(
            "rkd,kcd->rc", grad_other, proj_other, preferred_element_type=f32
        )
    grad_pooled = pooled_sum.astype(bf16)
    kernel_term = jnp.dot(fine_pixels.T, grad_pooled, preferred_element_type=f32) * grad_scale
    fine_gradient = jnp.dot(grad_pooled, pool_kernel.T, preferred_element_type=f32).astype(bf16)
    kernel_reduced = pix_scatter((kernel_term,), mixing_weight.shape[1])
    projection_gradient, mixing_gradient, kernel_gradient = pix_gather(
        (early_reduced, kernel_reduced), ((projection_term, mixing_term), (kernel_term,))
    )
    return (section_output, fine_gradient, kernel_gradient, projection_gradient, mixing_gradient)


def solution(mesh):
    placed = (
        P("pix", "ch"),
        P("ch", None),
        P(None, None, "ch"),
        P("ch", None),
        P("pix", None),
        P("pix", None),
        P("pix", "ch"),
    )
    return jax.shard_map(
        per_device,
        mesh=mesh,
        in_specs=placed,
        out_specs=(
            P("pix", "ch"),
            P("pix", "ch"),
            P("ch", None),
            P(None, None, "ch"),
            P("ch", None),
        ),
        check_vma=False,
    )
```

```python
import math

import jax
import jax.numpy as jnp
from jax import lax
from jax.sharding import PartitionSpec as P

HD = 64


def pick_table(row_ids, total):
    return (row_ids[:, None] == jnp.arange(total, dtype=jnp.int32)[None, :]).astype(jnp.bfloat16)


def slot_index(neighbour_block, first_row, block_rows):
    present = neighbour_block >= 0
    own_rows = first_row + jnp.arange(block_rows, dtype=jnp.int32)
    slot_rows = jnp.concatenate([own_rows[:, None], jnp.where(present, neighbour_block, 0)], axis=1)
    slot_live = jnp.concatenate([jnp.ones((block_rows, 1), bool), present], axis=1)
    return (slot_rows, slot_live)


def attention_forward(queries, key_value, halo, neighbours, row_offset):
    f32 = jnp.float32
    bf16 = jnp.bfloat16
    row_count = queries.shape[0]
    span = queries.shape[1]
    halo_rows = halo.shape[0]
    heads_here = span // HD
    slot_width = neighbours.shape[1] + 1
    score_scale = 1.0 / math.sqrt(HD)
    block_rows = math.gcd(row_count, 512)
    block_count = row_count // block_rows
    query_blocks = queries.reshape(block_count, block_rows, span)
    neighbour_blocks = neighbours.reshape(block_count, block_rows, slot_width - 1)
    local_flat = key_value.reshape(row_count, 2 * span)
    halo_flat = halo.reshape(halo_rows, 2 * span)

    block_parts = []
    for b in range(block_count):
        slot_rows, _ = slot_index(neighbour_blocks[b], row_offset + b * block_rows, block_rows)
        block_parts.append([
            jnp.dot(
                pick_table(slot_rows[:, slot], row_count), local_flat, preferred_element_type=f32
            )
            for slot in range(1, slot_width)
        ])
    block_parts, halo_flat = lax.optimization_barrier((block_parts, halo_flat))

    def forward_block(inputs):
        query_block, neighbour_block, first_row, local_parts = inputs
        slot_rows, slot_live = slot_index(neighbour_block, first_row, block_rows)
        pieces = [local_flat[first_row : first_row + block_rows]] + [
            (
                local_part
                + jnp.dot(
                    pick_table(slot_rows[:, slot] - row_count, halo_rows),
                    halo_flat,
                    preferred_element_type=f32,
                )
            ).astype(bf16)
            for slot, local_part in zip(range(1, slot_width), local_parts)
        ]
        gathered = jnp.stack(pieces, axis=1).reshape(block_rows, slot_width, 2, span)
        block_keys = gathered[:, :, 0].reshape(block_rows, slot_width, heads_here, HD)
        block_values = gathered[:, :, 1].reshape(block_rows, slot_width, heads_here, HD)
        scores = (
            jnp.einsum(
                "bhd,bmhd->bhm",
                query_block.reshape(block_rows, heads_here, HD),
                block_keys,
                preferred_element_type=f32,
            )
            * score_scale
        )
        shut = slot_live[:, None, :]
        masked = jnp.where(shut, scores, -1e30)
        largest = jnp.max(masked, axis=2, keepdims=True)
        raised = jnp.where(shut, jnp.exp(masked - largest), 0.0)
        probabilities = raised / jnp.sum(raised, axis=2, keepdims=True)
        weights = probabilities.astype(bf16)
        mixture = jnp.einsum("bhm,bmhd->bhd", weights, block_values, preferred_element_type=f32)
        return (mixture.reshape(block_rows, span).astype(bf16), probabilities, gathered)

    outputs = [
        forward_block(
            (query_blocks[b], neighbour_blocks[b], row_offset + b * block_rows, block_parts[b])
        )
        for b in range(block_count)
    ]
    attn_blocks = jnp.stack([out[0] for out in outputs])
    prob_blocks = [out[1] for out in outputs]
    kv_blocks = [out[2] for out in outputs]
    return (attn_blocks.reshape(row_count, span), prob_blocks, kv_blocks)


def attention_backward(
    queries, ext_rows, neighbours, row_offset, grad_attended, prob_blocks, kv_blocks, riders
):
    f32 = jnp.float32
    bf16 = jnp.bfloat16
    row_count = queries.shape[0]
    span = queries.shape[1]
    heads_here = span // HD
    slot_width = neighbours.shape[1] + 1
    score_scale = 1.0 / math.sqrt(HD)
    block_rows = math.gcd(row_count, 512)
    block_count = row_count // block_rows
    query_blocks = queries.reshape(block_count, block_rows, span)
    neighbour_blocks = neighbours.reshape(block_count, block_rows, slot_width - 1)
    grad_blocks = grad_attended.reshape(block_count, block_rows, span)

    def backward_block(carried, inputs):
        query_block, neighbour_block, first_row, grad_block, probabilities, gathered = inputs
        slot_rows, slot_live = slot_index(neighbour_block, first_row, block_rows)
        block_keys = gathered[:, :, 0].reshape(block_rows, slot_width, heads_here, HD).astype(f32)
        block_values = gathered[:, :, 1].reshape(block_rows, slot_width, heads_here, HD).astype(f32)
        grad_mix = grad_block.reshape(block_rows, heads_here, HD).astype(f32)
        grad_weights = jnp.einsum("bhd,bmhd->bhm", grad_mix, block_values)
        grad_scores = (
            probabilities
            * (grad_weights - jnp.sum(probabilities * grad_weights, axis=2, keepdims=True))
            * score_scale
        )
        grad_query = jnp.einsum("bhm,bmhd->bhd", grad_scores, block_keys).reshape(block_rows, span)
        query_wide = query_block.reshape(block_rows, heads_here, HD).astype(f32)
        grad_keys = jnp.einsum("bhm,bhd->bmhd", grad_scores, query_wide)
        rounded = lax.optimization_barrier(probabilities.astype(bf16))
        grad_values = jnp.einsum("bhm,bhd->bmhd", rounded.astype(f32), grad_mix)
        contribution = (
            jnp.stack([grad_keys, grad_values], axis=2)
            .reshape(block_rows, slot_width, 2 * span)
            .astype(bf16)
        )
        for slot in range(1, slot_width):
            carried = carried + jnp.einsum(
                "bx,bc->xc",
                pick_table(slot_rows[:, slot], ext_rows),
                contribution[:, slot],
                preferred_element_type=f32,
            )
        return (carried, (grad_query, contribution[:, 0]))

    carried = jnp.zeros((ext_rows, 2 * span), f32)
    query_grads = []
    for b in range(block_count):
        carried, grad_query = backward_block(
            carried,
            (query_blocks[b], neighbour_blocks[b], row_offset + b * block_rows, grad_blocks[b],
             prob_blocks[b], kv_blocks[b]),
        )
        query_grads.append(grad_query)
        if b == 0:
            carried, riders = lax.optimization_barrier((carried, riders))
    own_grads = jnp.concatenate([pair[1] for pair in query_grads], axis=0)
    query_grads = jnp.stack([pair[0] for pair in query_grads])
    carried = carried.at[:row_count].add(own_grads.astype(f32))
    return (carried.reshape(ext_rows, 2, span), query_grads.reshape(row_count, span), riders)


def ch_exchange(value):
    size = lax.axis_size("ch")
    return [
        lax.ppermute(value, "ch", [(i, (i + shift) % size) for i in range(size)])
        for shift in range(1, size)
    ]


def ch_assemble(own, others, axis):
    size = len(others) + 1
    index = lax.axis_index("ch")
    pieces = [own] + others
    result = None
    for case in range(size):
        ordered = jnp.concatenate([pieces[(case - j) % size] for j in range(size)], axis=axis)
        result = ordered if result is None else jnp.where(index == case, ordered, result)
    return result


def core_swap(value):
    size = lax.axis_size("pix")
    return lax.ppermute(value, "pix", [(i, i ^ 1) for i in range(size)])


def pix_scatter(terms, width):
    size = lax.axis_size("pix")
    core = lax.axis_index("pix") % 2
    flat = jnp.concatenate([term.reshape(-1, width) for term in terms], axis=0)
    rows = flat.shape[0]
    chunk = -(-rows // (2 * size))
    flat = jnp.pad(flat, ((0, 2 * size * chunk - rows), (0, 0)))
    halves = flat.reshape(2, size * chunk, width)
    keep = jnp.where(core == 0, halves[0], halves[1])
    send = jnp.where(core == 0, halves[1], halves[0])
    mine = keep + core_swap(send)
    parts = lax.all_to_all(mine.reshape(size, chunk, width), "pix", 0, 0, tiled=True)
    return jnp.sum(parts.reshape(size // 2, 2, chunk, width), axis=0)


def pix_gather(reduced_groups, term_groups):
    size = lax.axis_size("pix")
    core = lax.axis_index("pix") % 2
    width = reduced_groups[0].shape[-1]
    joined = jnp.concatenate(reduced_groups, axis=1)
    total = joined.shape[1]
    spread = jnp.broadcast_to(joined[None], (size // 2, 2, total, width))
    got = lax.all_to_all(spread.reshape(size, total, width), "pix", 0, 0, tiled=True)
    other = core_swap(got)
    first = jnp.where(core == 0, got, other)
    second = jnp.where(core == 0, other, got)
    results = []
    offset = 0
    for reduced, terms in zip(reduced_groups, term_groups):
        chunk = reduced.shape[1]
        flat = jnp.concatenate(
            [
                first[:, offset : offset + chunk].reshape(size * chunk, width),
                second[:, offset : offset + chunk].reshape(size * chunk, width),
            ],
            axis=0,
        )
        offset += chunk
        row = 0
        for term in terms:
            count = term.size // width
            results.append(flat[row : row + count].reshape(term.shape))
            row += count
    return results


def per_device(
    fine_pixels, pool_kernel, projections, mixing_weight, send_list, neighbours, cotangent
):
    f32 = jnp.float32
    bf16 = jnp.bfloat16
    row_count = fine_pixels.shape[0]
    half_width = projections.shape[2]
    ch_size = lax.axis_size("ch")
    ch_index = lax.axis_index("ch")
    peer_count = lax.axis_size("pix")
    slot_count = send_list.shape[1]
    grad_scale = 1.0 / math.sqrt(row_count * peer_count)
    send_pick = pick_table(send_list.reshape(-1), row_count)
    fine_others = ch_exchange(fine_pixels)
    kernel_others = ch_exchange(pool_kernel)
    pooled_sum = jnp.dot(fine_pixels, pool_kernel, preferred_element_type=f32)
    for fine_other, kernel_other in zip(fine_others, kernel_others):
        pooled_sum = pooled_sum + jnp.dot(fine_other, kernel_other, preferred_element_type=f32)
    pooled_all = pooled_sum.astype(bf16)
    mix_pieces = mixing_weight.reshape(mixing_weight.shape[0], ch_size, half_width)
    mix_sends = [
        jnp.take(mix_pieces, (ch_index + shift) % ch_size, axis=1) for shift in range(1, ch_size)
    ]
    pooled_all, cot_send, proj_send, mix_sends = lax.optimization_barrier(
        (pooled_all, cotangent, projections, mix_sends)
    )
    cot_others = ch_exchange(cot_send)
    proj_others = ch_exchange(proj_send)
    mix_others = [
        lax.ppermute(mix_send, "ch", [(i, (i + shift) % ch_size) for i in range(ch_size)])
        for shift, mix_send in zip(range(1, ch_size), mix_sends)
    ]
    mix_own = jnp.take(mix_pieces, ch_index, axis=1)
    pooled = lax.dynamic_slice_in_dim(pooled_all, ch_index * half_width, half_width, axis=1)
    upstream = ch_assemble(cotangent, cot_others, axis=1)
    projected = jnp.einsum(
        "rc,kcd->rkd", pooled_all, projections, preferred_element_type=f32
    ).astype(bf16)
    queries = projected[:, 0]
    key_value = projected[:, 1:]
    outgoing = (
        jnp.dot(send_pick, key_value.reshape(row_count, 2 * half_width), preferred_element_type=f32)
        .astype(bf16)
        .reshape(peer_count, slot_count, 2, half_width)
    )
    incoming = lax.all_to_all(outgoing, "pix", split_axis=0, concat_axis=0, tiled=True)
    halo = incoming.reshape(peer_count * slot_count, 2, half_width)
    attended, prob_blocks, kv_blocks = attention_forward(queries, key_value, halo, neighbours, 0)
    attended_others = ch_exchange(attended)
    grad_attended = jnp.dot(upstream, mixing_weight.T, preferred_element_type=f32).astype(bf16)
    grad_attended, proj_others = lax.optimization_barrier((grad_attended, proj_others))
    mixing_term = jnp.dot(attended.T, upstream, preferred_element_type=f32) * grad_scale
    carried, query_grads, (attended_others, mix_others) = attention_backward(
        queries, row_count + halo.shape[0], neighbours, 0, grad_attended, prob_blocks, kv_blocks,
        (attended_others, mix_others),
    )
    branch = jnp.dot(attended, mix_own, preferred_element_type=f32)
    for attended_other, mix_other in zip(attended_others, mix_others):
        branch = branch + jnp.dot(attended_other, mix_other, preferred_element_type=f32)
    section_output = (pooled.astype(f32) + branch).astype(bf16)
    remote_grads = carried[row_count:].reshape(peer_count, slot_count, 2, half_width)
    returned = lax.all_to_all(remote_grads, "pix", split_axis=0, concat_axis=0, tiled=True)
    returned_rows = jnp.einsum(
        "px,pc->xc",
        send_pick,
        returned.reshape(peer_count * slot_count, 2 * half_width).astype(bf16),
        preferred_element_type=f32,
    )
    local_grads = carried[:row_count] + returned_rows.reshape(row_count, 2, half_width)
    grad_projected = jnp.concatenate(
        [query_grads.reshape(row_count, 1, half_width), local_grads], axis=1
    ).astype(bf16)
    grad_others = ch_exchange(grad_projected)
    projection_term = (
        jnp.einsum("rc,rkd->kcd", pooled_all, grad_projected, preferred_element_type=f32)
        * grad_scale
    )
    early_reduced = pix_scatter((projection_term, mixing_term), mixing_weight.shape[1])
    early_reduced, grad_others = lax.optimization_barrier((early_reduced, grad_others))
    pooled_sum = upstream.astype(f32) + jnp.einsum(
        "rkd,kcd->rc", grad_projected, projections, preferred_element_type=f32
    )
    for grad_other, proj_other in zip(grad_others, proj_others):
        pooled_sum = pooled_sum + jnp.einsum(
            "rkd,kcd->rc", grad_other, proj_other, preferred_element_type=f32
        )
    grad_pooled = pooled_sum.astype(bf16)
    kernel_term = jnp.dot(fine_pixels.T, grad_pooled, preferred_element_type=f32) * grad_scale
    fine_gradient = jnp.dot(grad_pooled, pool_kernel.T, preferred_element_type=f32).astype(bf16)
    kernel_reduced = pix_scatter((kernel_term,), mixing_weight.shape[1])
    projection_gradient, mixing_gradient, kernel_gradient = pix_gather(
        (early_reduced, kernel_reduced), ((projection_term, mixing_term), (kernel_term,))
    )
    return (section_output, fine_gradient, kernel_gradient, projection_gradient, mixing_gradient)


def solution(mesh):
    placed = (
        P("pix", "ch"),
        P("ch", None),
        P(None, None, "ch"),
        P("ch", None),
        P("pix", None),
        P("pix", None),
        P("pix", "ch"),
    )
    return jax.shard_map(
        per_device,
        mesh=mesh,
        in_specs=placed,
        out_specs=(
            P("pix", "ch"),
            P("pix", "ch"),
            P("ch", None),
            P(None, None, "ch"),
            P("ch", None),
        ),
        check_vma=False,
    )
```

```python
import math

import jax
import jax.numpy as jnp
from jax import lax
from jax.sharding import PartitionSpec as P

HD = 64


def pick_table(row_ids, total):
    return (row_ids[:, None] == jnp.arange(total, dtype=jnp.int32)[None, :]).astype(jnp.bfloat16)


def slot_index(neighbour_block, first_row, block_rows):
    present = neighbour_block >= 0
    own_rows = first_row + jnp.arange(block_rows, dtype=jnp.int32)
    slot_rows = jnp.concatenate([own_rows[:, None], jnp.where(present, neighbour_block, 0)], axis=1)
    slot_live = jnp.concatenate([jnp.ones((block_rows, 1), bool), present], axis=1)
    return (slot_rows, slot_live)


def attention_forward(queries, extended, neighbours, row_offset):
    f32 = jnp.float32
    bf16 = jnp.bfloat16
    row_count = queries.shape[0]
    span = queries.shape[1]
    ext_rows = extended.shape[0]
    heads_here = span // HD
    slot_width = neighbours.shape[1] + 1
    score_scale = 1.0 / math.sqrt(HD)
    block_rows = math.gcd(row_count, 512)
    block_count = row_count // block_rows
    query_blocks = queries.reshape(block_count, block_rows, span)
    neighbour_blocks = neighbours.reshape(block_count, block_rows, slot_width - 1)
    flattened = extended.reshape(ext_rows, 2 * span)

    def forward_block(inputs):
        query_block, neighbour_block, first_row = inputs
        slot_rows, slot_live = slot_index(neighbour_block, first_row, block_rows)
        pieces = [flattened[first_row : first_row + block_rows]] + [
            jnp.dot(
                pick_table(slot_rows[:, slot], ext_rows), flattened, preferred_element_type=f32
            ).astype(bf16)
            for slot in range(1, slot_width)
        ]
        gathered = jnp.stack(pieces, axis=1).reshape(block_rows, slot_width, 2, span)
        block_keys = gathered[:, :, 0].reshape(block_rows, slot_width, heads_here, HD)
        block_values = gathered[:, :, 1].reshape(block_rows, slot_width, heads_here, HD)
        scores = (
            jnp.einsum(
                "bhd,bmhd->bhm",
                query_block.reshape(block_rows, heads_here, HD),
                block_keys,
                preferred_element_type=f32,
            )
            * score_scale
        )
        shut = slot_live[:, None, :]
        masked = jnp.where(shut, scores, -1e30)
        largest = jnp.max(masked, axis=2, keepdims=True)
        raised = jnp.where(shut, jnp.exp(masked - largest), 0.0)
        probabilities = raised / jnp.sum(raised, axis=2, keepdims=True)
        weights = probabilities.astype(bf16)
        mixture = jnp.einsum("bhm,bmhd->bhd", weights, block_values, preferred_element_type=f32)
        return (mixture.reshape(block_rows, span).astype(bf16), probabilities, gathered)

    outputs = [
        forward_block((query_blocks[b], neighbour_blocks[b], row_offset + b * block_rows))
        for b in range(block_count)
    ]
    attn_blocks = jnp.stack([out[0] for out in outputs])
    prob_blocks = [out[1] for out in outputs]
    kv_blocks = [out[2] for out in outputs]
    return (attn_blocks.reshape(row_count, span), prob_blocks, kv_blocks)


def attention_backward(
    queries, ext_rows, neighbours, row_offset, grad_attended, prob_blocks, kv_blocks, riders
):
    f32 = jnp.float32
    bf16 = jnp.bfloat16
    row_count = queries.shape[0]
    span = queries.shape[1]
    heads_here = span // HD
    slot_width = neighbours.shape[1] + 1
    score_scale = 1.0 / math.sqrt(HD)
    block_rows = math.gcd(row_count, 512)
    block_count = row_count // block_rows
    query_blocks = queries.reshape(block_count, block_rows, span)
    neighbour_blocks = neighbours.reshape(block_count, block_rows, slot_width - 1)
    grad_blocks = grad_attended.reshape(block_count, block_rows, span)

    def backward_block(carried, inputs):
        query_block, neighbour_block, first_row, grad_block, probabilities, gathered = inputs
        slot_rows, slot_live = slot_index(neighbour_block, first_row, block_rows)
        block_keys = gathered[:, :, 0].reshape(block_rows, slot_width, heads_here, HD).astype(f32)
        block_values = gathered[:, :, 1].reshape(block_rows, slot_width, heads_here, HD).astype(f32)
        grad_mix = grad_block.reshape(block_rows, heads_here, HD).astype(f32)
        grad_weights = jnp.einsum("bhd,bmhd->bhm", grad_mix, block_values)
        grad_scores = (
            probabilities
            * (grad_weights - jnp.sum(probabilities * grad_weights, axis=2, keepdims=True))
            * score_scale
        )
        grad_query = jnp.einsum("bhm,bmhd->bhd", grad_scores, block_keys).reshape(block_rows, span)
        query_wide = query_block.reshape(block_rows, heads_here, HD).astype(f32)
        grad_keys = jnp.einsum("bhm,bhd->bmhd", grad_scores, query_wide)
        rounded = lax.optimization_barrier(probabilities.astype(bf16))
        grad_values = jnp.einsum("bhm,bhd->bmhd", rounded.astype(f32), grad_mix)
        contribution = (
            jnp.stack([grad_keys, grad_values], axis=2)
            .reshape(block_rows, slot_width, 2 * span)
            .astype(bf16)
        )
        for slot in range(1, slot_width):
            carried = carried + jnp.einsum(
                "bx,bc->xc",
                pick_table(slot_rows[:, slot], ext_rows),
                contribution[:, slot],
                preferred_element_type=f32,
            )
        return (carried, (grad_query, contribution[:, 0]))

    carried = jnp.zeros((ext_rows, 2 * span), f32)
    query_grads = []
    for b in range(block_count):
        carried, grad_query = backward_block(
            carried,
            (query_blocks[b], neighbour_blocks[b], row_offset + b * block_rows, grad_blocks[b],
             prob_blocks[b], kv_blocks[b]),
        )
        query_grads.append(grad_query)
        if b == 0:
            carried, riders = lax.optimization_barrier((carried, riders))
    own_grads = jnp.concatenate([pair[1] for pair in query_grads], axis=0)
    query_grads = jnp.stack([pair[0] for pair in query_grads])
    carried = carried.at[:row_count].add(own_grads.astype(f32))
    return (carried.reshape(ext_rows, 2, span), query_grads.reshape(row_count, span), riders)


def ch_exchange(value):
    size = lax.axis_size("ch")
    return [
        lax.ppermute(value, "ch", [(i, (i + shift) % size) for i in range(size)])
        for shift in range(1, size)
    ]


def ch_assemble(own, others, axis):
    size = len(others) + 1
    index = lax.axis_index("ch")
    pieces = [own] + others
    result = None
    for case in range(size):
        ordered = jnp.concatenate([pieces[(case - j) % size] for j in range(size)], axis=axis)
        result = ordered if result is None else jnp.where(index == case, ordered, result)
    return result


def core_swap(value):
    size = lax.axis_size("pix")
    return lax.ppermute(value, "pix", [(i, i ^ 1) for i in range(size)])


def pix_scatter(terms, width):
    size = lax.axis_size("pix")
    core = lax.axis_index("pix") % 2
    flat = jnp.concatenate([term.reshape(-1, width) for term in terms], axis=0)
    rows = flat.shape[0]
    chunk = -(-rows // (2 * size))
    flat = jnp.pad(flat, ((0, 2 * size * chunk - rows), (0, 0)))
    halves = flat.reshape(2, size * chunk, width)
    keep = jnp.where(core == 0, halves[0], halves[1])
    send = jnp.where(core == 0, halves[1], halves[0])
    mine = keep + core_swap(send)
    parts = lax.all_to_all(mine.reshape(size, chunk, width), "pix", 0, 0, tiled=True)
    return jnp.sum(parts.reshape(size // 2, 2, chunk, width), axis=0)


def pix_gather(reduced_groups, term_groups):
    size = lax.axis_size("pix")
    core = lax.axis_index("pix") % 2
    width = reduced_groups[0].shape[-1]
    joined = jnp.concatenate(reduced_groups, axis=1)
    total = joined.shape[1]
    spread = jnp.broadcast_to(joined[None], (size // 2, 2, total, width))
    got = lax.all_to_all(spread.reshape(size, total, width), "pix", 0, 0, tiled=True)
    other = core_swap(got)
    first = jnp.where(core == 0, got, other)
    second = jnp.where(core == 0, other, got)
    results = []
    offset = 0
    for reduced, terms in zip(reduced_groups, term_groups):
        chunk = reduced.shape[1]
        flat = jnp.concatenate(
            [
                first[:, offset : offset + chunk].reshape(size * chunk, width),
                second[:, offset : offset + chunk].reshape(size * chunk, width),
            ],
            axis=0,
        )
        offset += chunk
        row = 0
        for term in terms:
            count = term.size // width
            results.append(flat[row : row + count].reshape(term.shape))
            row += count
    return results


def per_device(
    fine_pixels, pool_kernel, projections, mixing_weight, send_list, neighbours, cotangent
):
    f32 = jnp.float32
    bf16 = jnp.bfloat16
    row_count = fine_pixels.shape[0]
    half_width = projections.shape[2]
    ch_size = lax.axis_size("ch")
    ch_index = lax.axis_index("ch")
    peer_count = lax.axis_size("pix")
    slot_count = send_list.shape[1]
    grad_scale = 1.0 / math.sqrt(row_count * peer_count)
    send_pick = pick_table(send_list.reshape(-1), row_count)
    fine_others = ch_exchange(fine_pixels)
    kernel_others = ch_exchange(pool_kernel)
    pooled_sum = jnp.dot(fine_pixels, pool_kernel, preferred_element_type=f32)
    for fine_other, kernel_other in zip(fine_others, kernel_others):
        pooled_sum = pooled_sum + jnp.dot(fine_other, kernel_other, preferred_element_type=f32)
    pooled_all = pooled_sum.astype(bf16)
    mix_pieces = mixing_weight.reshape(mixing_weight.shape[0], ch_size, half_width)
    mix_sends = [
        jnp.take(mix_pieces, (ch_index + shift) % ch_size, axis=1) for shift in range(1, ch_size)
    ]
    pooled_all, cot_send, proj_send, mix_sends = lax.optimization_barrier(
        (pooled_all, cotangent, projections, mix_sends)
    )
    cot_others = ch_exchange(cot_send)
    proj_others = ch_exchange(proj_send)
    mix_others = [
        lax.ppermute(mix_send, "ch", [(i, (i + shift) % ch_size) for i in range(ch_size)])
        for shift, mix_send in zip(range(1, ch_size), mix_sends)
    ]
    mix_own = jnp.take(mix_pieces, ch_index, axis=1)
    pooled = lax.dynamic_slice_in_dim(pooled_all, ch_index * half_width, half_width, axis=1)
    upstream = ch_assemble(cotangent, cot_others, axis=1)
    projected = jnp.einsum(
        "rc,kcd->rkd", pooled_all, projections, preferred_element_type=f32
    ).astype(bf16)
    queries = projected[:, 0]
    key_value = projected[:, 1:]
    outgoing = (
        jnp.dot(send_pick, key_value.reshape(row_count, 2 * half_width), preferred_element_type=f32)
        .astype(bf16)
        .reshape(peer_count, slot_count, 2, half_width)
    )
    incoming = lax.all_to_all(outgoing, "pix", split_axis=0, concat_axis=0, tiled=True)
    extended = jnp.concatenate(
        [key_value, incoming.reshape(peer_count * slot_count, 2, half_width)], axis=0
    )
    attended, prob_blocks, kv_blocks = attention_forward(queries, extended, neighbours, 0)
    attended_others = ch_exchange(attended)
    grad_attended = jnp.dot(upstream, mixing_weight.T, preferred_element_type=f32).astype(bf16)
    mixing_term = jnp.dot(attended.T, upstream, preferred_element_type=f32) * grad_scale
    carried, query_grads, (attended_others, mix_others, proj_others) = attention_backward(
        queries, extended.shape[0], neighbours, 0, grad_attended, prob_blocks, kv_blocks,
        (attended_others, mix_others, proj_others),
    )
    branch = jnp.dot(attended, mix_own, preferred_element_type=f32)
    for attended_other, mix_other in zip(attended_others, mix_others):
        branch = branch + jnp.dot(attended_other, mix_other, preferred_element_type=f32)
    section_output = (pooled.astype(f32) + branch).astype(bf16)
    remote_grads = carried[row_count:].reshape(peer_count, slot_count, 2, half_width)
    returned = lax.all_to_all(remote_grads, "pix", split_axis=0, concat_axis=0, tiled=True)
    returned_rows = jnp.einsum(
        "px,pc->xc",
        send_pick,
        returned.reshape(peer_count * slot_count, 2 * half_width).astype(bf16),
        preferred_element_type=f32,
    )
    local_grads = carried[:row_count] + returned_rows.reshape(row_count, 2, half_width)
    grad_projected = jnp.concatenate(
        [query_grads.reshape(row_count, 1, half_width), local_grads], axis=1
    ).astype(bf16)
    grad_others = ch_exchange(grad_projected)
    projection_term = (
        jnp.einsum("rc,rkd->kcd", pooled_all, grad_projected, preferred_element_type=f32)
        * grad_scale
    )
    early_reduced = pix_scatter((projection_term, mixing_term), mixing_weight.shape[1])
    early_reduced, grad_others = lax.optimization_barrier((early_reduced, grad_others))
    pooled_sum = upstream.astype(f32) + jnp.einsum(
        "rkd,kcd->rc", grad_projected, projections, preferred_element_type=f32
    )
    for grad_other, proj_other in zip(grad_others, proj_others):
        pooled_sum = pooled_sum + jnp.einsum(
            "rkd,kcd->rc", grad_other, proj_other, preferred_element_type=f32
        )
    grad_pooled = pooled_sum.astype(bf16)
    kernel_term = jnp.dot(fine_pixels.T, grad_pooled, preferred_element_type=f32) * grad_scale
    fine_gradient = jnp.dot(grad_pooled, pool_kernel.T, preferred_element_type=f32).astype(bf16)
    kernel_reduced = pix_scatter((kernel_term,), mixing_weight.shape[1])
    projection_gradient, mixing_gradient, kernel_gradient = pix_gather(
        (early_reduced, kernel_reduced), ((projection_term, mixing_term), (kernel_term,))
    )
    return (section_output, fine_gradient, kernel_gradient, projection_gradient, mixing_gradient)


def solution(mesh):
    placed = (
        P("pix", "ch"),
        P("ch", None),
        P(None, None, "ch"),
        P("ch", None),
        P("pix", None),
        P("pix", None),
        P("pix", "ch"),
    )
    return jax.shard_map(
        per_device,
        mesh=mesh,
        in_specs=placed,
        out_specs=(
            P("pix", "ch"),
            P("pix", "ch"),
            P("ch", None),
            P(None, None, "ch"),
            P("ch", None),
        ),
        check_vma=False,
    )
```

```python
import math

import jax
import jax.numpy as jnp
from jax import lax
from jax.sharding import PartitionSpec as P

HD = 64


def pick_table(row_ids, total):
    return (row_ids[:, None] == jnp.arange(total, dtype=jnp.int32)[None, :]).astype(jnp.bfloat16)


def slot_index(neighbour_block, first_row, block_rows):
    present = neighbour_block >= 0
    own_rows = first_row + jnp.arange(block_rows, dtype=jnp.int32)
    slot_rows = jnp.concatenate([own_rows[:, None], jnp.where(present, neighbour_block, 0)], axis=1)
    slot_live = jnp.concatenate([jnp.ones((block_rows, 1), bool), present], axis=1)
    return (slot_rows, slot_live)


def attention_forward(queries, extended, neighbours, row_offset, riders):
    f32 = jnp.float32
    bf16 = jnp.bfloat16
    row_count = queries.shape[0]
    span = queries.shape[1]
    ext_rows = extended.shape[0]
    heads_here = span // HD
    slot_width = neighbours.shape[1] + 1
    score_scale = 1.0 / math.sqrt(HD)
    block_rows = math.gcd(row_count, 512)
    block_count = row_count // block_rows
    query_blocks = queries.reshape(block_count, block_rows, span)
    neighbour_blocks = neighbours.reshape(block_count, block_rows, slot_width - 1)
    flattened = extended.reshape(ext_rows, 2 * span)

    def forward_block(inputs):
        query_block, neighbour_block, first_row = inputs
        slot_rows, slot_live = slot_index(neighbour_block, first_row, block_rows)
        pieces = [flattened[first_row : first_row + block_rows]] + [
            jnp.dot(
                pick_table(slot_rows[:, slot], ext_rows), flattened, preferred_element_type=f32
            ).astype(bf16)
            for slot in range(1, slot_width)
        ]
        gathered = jnp.stack(pieces, axis=1).reshape(block_rows, slot_width, 2, span)
        block_keys = gathered[:, :, 0].reshape(block_rows, slot_width, heads_here, HD)
        block_values = gathered[:, :, 1].reshape(block_rows, slot_width, heads_here, HD)
        scores = (
            jnp.einsum(
                "bhd,bmhd->bhm",
                query_block.reshape(block_rows, heads_here, HD),
                block_keys,
                preferred_element_type=f32,
            )
            * score_scale
        )
        shut = slot_live[:, None, :]
        masked = jnp.where(shut, scores, -1e30)
        largest = jnp.max(masked, axis=2, keepdims=True)
        raised = jnp.where(shut, jnp.exp(masked - largest), 0.0)
        probabilities = raised / jnp.sum(raised, axis=2, keepdims=True)
        weights = probabilities.astype(bf16)
        mixture = jnp.einsum("bhm,bmhd->bhd", weights, block_values, preferred_element_type=f32)
        return (mixture.reshape(block_rows, span).astype(bf16), probabilities, gathered)

    outputs = []
    for b in range(block_count):
        out = forward_block((query_blocks[b], neighbour_blocks[b], row_offset + b * block_rows))
        if b == 0:
            out, riders = lax.optimization_barrier((out, riders))
        outputs.append(out)
    attn_blocks = jnp.stack([out[0] for out in outputs])
    prob_blocks = [out[1] for out in outputs]
    kv_blocks = [out[2] for out in outputs]
    return (attn_blocks.reshape(row_count, span), prob_blocks, kv_blocks, riders)


def attention_backward(
    queries, ext_rows, neighbours, row_offset, grad_attended, prob_blocks, kv_blocks, riders
):
    f32 = jnp.float32
    bf16 = jnp.bfloat16
    row_count = queries.shape[0]
    span = queries.shape[1]
    heads_here = span // HD
    slot_width = neighbours.shape[1] + 1
    score_scale = 1.0 / math.sqrt(HD)
    block_rows = math.gcd(row_count, 512)
    block_count = row_count // block_rows
    query_blocks = queries.reshape(block_count, block_rows, span)
    neighbour_blocks = neighbours.reshape(block_count, block_rows, slot_width - 1)
    grad_blocks = grad_attended.reshape(block_count, block_rows, span)

    def backward_block(carried, inputs):
        query_block, neighbour_block, first_row, grad_block, probabilities, gathered = inputs
        slot_rows, slot_live = slot_index(neighbour_block, first_row, block_rows)
        block_keys = gathered[:, :, 0].reshape(block_rows, slot_width, heads_here, HD).astype(f32)
        block_values = gathered[:, :, 1].reshape(block_rows, slot_width, heads_here, HD).astype(f32)
        grad_mix = grad_block.reshape(block_rows, heads_here, HD).astype(f32)
        grad_weights = jnp.einsum("bhd,bmhd->bhm", grad_mix, block_values)
        grad_scores = (
            probabilities
            * (grad_weights - jnp.sum(probabilities * grad_weights, axis=2, keepdims=True))
            * score_scale
        )
        grad_query = jnp.einsum("bhm,bmhd->bhd", grad_scores, block_keys).reshape(block_rows, span)
        query_wide = query_block.reshape(block_rows, heads_here, HD).astype(f32)
        grad_keys = jnp.einsum("bhm,bhd->bmhd", grad_scores, query_wide)
        rounded = lax.optimization_barrier(probabilities.astype(bf16))
        grad_values = jnp.einsum("bhm,bhd->bmhd", rounded.astype(f32), grad_mix)
        contribution = (
            jnp.stack([grad_keys, grad_values], axis=2)
            .reshape(block_rows, slot_width, 2 * span)
            .astype(bf16)
        )
        for slot in range(1, slot_width):
            carried = carried + jnp.einsum(
                "bx,bc->xc",
                pick_table(slot_rows[:, slot], ext_rows),
                contribution[:, slot],
                preferred_element_type=f32,
            )
        return (carried, (grad_query, contribution[:, 0]))

    carried = jnp.zeros((ext_rows, 2 * span), f32)
    query_grads = []
    for b in range(block_count):
        carried, grad_query = backward_block(
            carried,
            (query_blocks[b], neighbour_blocks[b], row_offset + b * block_rows, grad_blocks[b],
             prob_blocks[b], kv_blocks[b]),
        )
        query_grads.append(grad_query)
        if b == 0:
            carried, riders = lax.optimization_barrier((carried, riders))
    own_grads = jnp.concatenate([pair[1] for pair in query_grads], axis=0)
    query_grads = jnp.stack([pair[0] for pair in query_grads])
    carried = carried.at[:row_count].add(own_grads.astype(f32))
    return (carried.reshape(ext_rows, 2, span), query_grads.reshape(row_count, span), riders)


def ch_exchange(value):
    size = lax.axis_size("ch")
    return [
        lax.ppermute(value, "ch", [(i, (i + shift) % size) for i in range(size)])
        for shift in range(1, size)
    ]


def ch_assemble(own, others, axis):
    size = len(others) + 1
    index = lax.axis_index("ch")
    pieces = [own] + others
    result = None
    for case in range(size):
        ordered = jnp.concatenate([pieces[(case - j) % size] for j in range(size)], axis=axis)
        result = ordered if result is None else jnp.where(index == case, ordered, result)
    return result


def core_swap(value):
    size = lax.axis_size("pix")
    return lax.ppermute(value, "pix", [(i, i ^ 1) for i in range(size)])


def pix_scatter(terms, width):
    size = lax.axis_size("pix")
    core = lax.axis_index("pix") % 2
    flat = jnp.concatenate([term.reshape(-1, width) for term in terms], axis=0)
    rows = flat.shape[0]
    chunk = -(-rows // (2 * size))
    flat = jnp.pad(flat, ((0, 2 * size * chunk - rows), (0, 0)))
    halves = flat.reshape(2, size * chunk, width)
    keep = jnp.where(core == 0, halves[0], halves[1])
    send = jnp.where(core == 0, halves[1], halves[0])
    mine = keep + core_swap(send)
    parts = lax.all_to_all(mine.reshape(size, chunk, width), "pix", 0, 0, tiled=True)
    return jnp.sum(parts.reshape(size // 2, 2, chunk, width), axis=0)


def pix_gather(reduced_groups, term_groups):
    size = lax.axis_size("pix")
    core = lax.axis_index("pix") % 2
    width = reduced_groups[0].shape[-1]
    joined = jnp.concatenate(reduced_groups, axis=1)
    total = joined.shape[1]
    spread = jnp.broadcast_to(joined[None], (size // 2, 2, total, width))
    got = lax.all_to_all(spread.reshape(size, total, width), "pix", 0, 0, tiled=True)
    other = core_swap(got)
    first = jnp.where(core == 0, got, other)
    second = jnp.where(core == 0, other, got)
    results = []
    offset = 0
    for reduced, terms in zip(reduced_groups, term_groups):
        chunk = reduced.shape[1]
        flat = jnp.concatenate(
            [
                first[:, offset : offset + chunk].reshape(size * chunk, width),
                second[:, offset : offset + chunk].reshape(size * chunk, width),
            ],
            axis=0,
        )
        offset += chunk
        row = 0
        for term in terms:
            count = term.size // width
            results.append(flat[row : row + count].reshape(term.shape))
            row += count
    return results


def per_device(
    fine_pixels, pool_kernel, projections, mixing_weight, send_list, neighbours, cotangent
):
    f32 = jnp.float32
    bf16 = jnp.bfloat16
    row_count = fine_pixels.shape[0]
    half_width = projections.shape[2]
    ch_size = lax.axis_size("ch")
    ch_index = lax.axis_index("ch")
    peer_count = lax.axis_size("pix")
    slot_count = send_list.shape[1]
    grad_scale = 1.0 / math.sqrt(row_count * peer_count)
    send_pick = pick_table(send_list.reshape(-1), row_count)
    fine_others = ch_exchange(fine_pixels)
    kernel_others = ch_exchange(pool_kernel)
    pooled_sum = jnp.dot(fine_pixels, pool_kernel, preferred_element_type=f32)
    for fine_other, kernel_other in zip(fine_others, kernel_others):
        pooled_sum = pooled_sum + jnp.dot(fine_other, kernel_other, preferred_element_type=f32)
    pooled_all = pooled_sum.astype(bf16)
    mix_pieces = mixing_weight.reshape(mixing_weight.shape[0], ch_size, half_width)
    mix_sends = [
        jnp.take(mix_pieces, (ch_index + shift) % ch_size, axis=1) for shift in range(1, ch_size)
    ]
    pooled_all, cot_send, proj_send, mix_sends = lax.optimization_barrier(
        (pooled_all, cotangent, projections, mix_sends)
    )
    cot_others = ch_exchange(cot_send)
    proj_others = ch_exchange(proj_send)
    mix_others = [
        lax.ppermute(mix_send, "ch", [(i, (i + shift) % ch_size) for i in range(ch_size)])
        for shift, mix_send in zip(range(1, ch_size), mix_sends)
    ]
    mix_own = jnp.take(mix_pieces, ch_index, axis=1)
    pooled = lax.dynamic_slice_in_dim(pooled_all, ch_index * half_width, half_width, axis=1)
    projected = jnp.einsum(
        "rc,kcd->rkd", pooled_all, projections, preferred_element_type=f32
    ).astype(bf16)
    queries = projected[:, 0]
    key_value = projected[:, 1:]
    outgoing = (
        jnp.dot(send_pick, key_value.reshape(row_count, 2 * half_width), preferred_element_type=f32)
        .astype(bf16)
        .reshape(peer_count, slot_count, 2, half_width)
    )
    incoming = lax.all_to_all(outgoing, "pix", split_axis=0, concat_axis=0, tiled=True)
    extended = jnp.concatenate(
        [key_value, incoming.reshape(peer_count * slot_count, 2, half_width)], axis=0
    )
    attended, prob_blocks, kv_blocks, cot_others = attention_forward(
        queries, extended, neighbours, 0, cot_others
    )
    upstream = ch_assemble(cotangent, cot_others, axis=1)
    attended_others = ch_exchange(attended)
    grad_attended = jnp.dot(upstream, mixing_weight.T, preferred_element_type=f32).astype(bf16)
    mixing_term = jnp.dot(attended.T, upstream, preferred_element_type=f32) * grad_scale
    carried, query_grads, (attended_others, mix_others, proj_others) = attention_backward(
        queries, extended.shape[0], neighbours, 0, grad_attended, prob_blocks, kv_blocks,
        (attended_others, mix_others, proj_others),
    )
    branch = jnp.dot(attended, mix_own, preferred_element_type=f32)
    for attended_other, mix_other in zip(attended_others, mix_others):
        branch = branch + jnp.dot(attended_other, mix_other, preferred_element_type=f32)
    section_output = (pooled.astype(f32) + branch).astype(bf16)
    remote_grads = carried[row_count:].reshape(peer_count, slot_count, 2, half_width)
    returned = lax.all_to_all(remote_grads, "pix", split_axis=0, concat_axis=0, tiled=True)
    returned_rows = jnp.einsum(
        "px,pc->xc",
        send_pick,
        returned.reshape(peer_count * slot_count, 2 * half_width).astype(bf16),
        preferred_element_type=f32,
    )
    local_grads = carried[:row_count] + returned_rows.reshape(row_count, 2, half_width)
    grad_projected = jnp.concatenate(
        [query_grads.reshape(row_count, 1, half_width), local_grads], axis=1
    ).astype(bf16)
    grad_others = ch_exchange(grad_projected)
    projection_term = (
        jnp.einsum("rc,rkd->kcd", pooled_all, grad_projected, preferred_element_type=f32)
        * grad_scale
    )
    early_reduced = pix_scatter((projection_term, mixing_term), mixing_weight.shape[1])
    early_reduced, grad_others = lax.optimization_barrier((early_reduced, grad_others))
    pooled_sum = upstream.astype(f32) + jnp.einsum(
        "rkd,kcd->rc", grad_projected, projections, preferred_element_type=f32
    )
    for grad_other, proj_other in zip(grad_others, proj_others):
        pooled_sum = pooled_sum + jnp.einsum(
            "rkd,kcd->rc", grad_other, proj_other, preferred_element_type=f32
        )
    grad_pooled = pooled_sum.astype(bf16)
    kernel_term = jnp.dot(fine_pixels.T, grad_pooled, preferred_element_type=f32) * grad_scale
    fine_gradient = jnp.dot(grad_pooled, pool_kernel.T, preferred_element_type=f32).astype(bf16)
    kernel_reduced = pix_scatter((kernel_term,), mixing_weight.shape[1])
    projection_gradient, mixing_gradient, kernel_gradient = pix_gather(
        (early_reduced, kernel_reduced), ((projection_term, mixing_term), (kernel_term,))
    )
    return (section_output, fine_gradient, kernel_gradient, projection_gradient, mixing_gradient)


def solution(mesh):
    placed = (
        P("pix", "ch"),
        P("ch", None),
        P(None, None, "ch"),
        P("ch", None),
        P("pix", None),
        P("pix", None),
        P("pix", "ch"),
    )
    return jax.shard_map(
        per_device,
        mesh=mesh,
        in_specs=placed,
        out_specs=(
            P("pix", "ch"),
            P("pix", "ch"),
            P("ch", None),
            P(None, None, "ch"),
            P("ch", None),
        ),
        check_vma=False,
    )
```

```python
import math

import jax
import jax.numpy as jnp
from jax import lax
from jax.sharding import PartitionSpec as P

HD = 64


def pick_table(row_ids, total):
    return (row_ids[:, None] == jnp.arange(total, dtype=jnp.int32)[None, :]).astype(jnp.bfloat16)


def slot_index(neighbour_block, first_row, block_rows):
    present = neighbour_block >= 0
    own_rows = first_row + jnp.arange(block_rows, dtype=jnp.int32)
    slot_rows = jnp.concatenate([own_rows[:, None], jnp.where(present, neighbour_block, 0)], axis=1)
    slot_live = jnp.concatenate([jnp.ones((block_rows, 1), bool), present], axis=1)
    return (slot_rows, slot_live)


def attention_forward(queries, extended, neighbours, row_offset):
    f32 = jnp.float32
    bf16 = jnp.bfloat16
    row_count = queries.shape[0]
    span = queries.shape[1]
    ext_rows = extended.shape[0]
    heads_here = span // HD
    slot_width = neighbours.shape[1] + 1
    score_scale = 1.0 / math.sqrt(HD)
    block_rows = math.gcd(row_count, 512)
    block_count = row_count // block_rows
    query_blocks = queries.reshape(block_count, block_rows, span)
    neighbour_blocks = neighbours.reshape(block_count, block_rows, slot_width - 1)
    flattened = extended.reshape(ext_rows, 2 * span)

    def forward_block(inputs):
        query_block, neighbour_block, first_row = inputs
        slot_rows, slot_live = slot_index(neighbour_block, first_row, block_rows)
        pieces = [flattened[first_row : first_row + block_rows]] + [
            jnp.dot(
                pick_table(slot_rows[:, slot], ext_rows), flattened, preferred_element_type=f32
            ).astype(bf16)
            for slot in range(1, slot_width)
        ]
        gathered = jnp.stack(pieces, axis=1).reshape(block_rows, slot_width, 2, span)
        block_keys = gathered[:, :, 0].reshape(block_rows, slot_width, heads_here, HD)
        block_values = gathered[:, :, 1].reshape(block_rows, slot_width, heads_here, HD)
        scores = (
            jnp.einsum(
                "bhd,bmhd->bhm",
                query_block.reshape(block_rows, heads_here, HD),
                block_keys,
                preferred_element_type=f32,
            )
            * score_scale
        )
        shut = slot_live[:, None, :]
        masked = jnp.where(shut, scores, -1e30)
        largest = jnp.max(masked, axis=2, keepdims=True)
        raised = jnp.where(shut, jnp.exp(masked - largest), 0.0)
        probabilities = raised / jnp.sum(raised, axis=2, keepdims=True)
        weights = probabilities.astype(bf16)
        mixture = jnp.einsum("bhm,bmhd->bhd", weights, block_values, preferred_element_type=f32)
        return (mixture.reshape(block_rows, span).astype(bf16), probabilities, gathered)

    outputs = [
        forward_block((query_blocks[b], neighbour_blocks[b], row_offset + b * block_rows))
        for b in range(block_count)
    ]
    attn_blocks = jnp.stack([out[0] for out in outputs])
    prob_blocks = [out[1] for out in outputs]
    kv_blocks = [out[2] for out in outputs]
    return (attn_blocks.reshape(row_count, span), prob_blocks, kv_blocks)


def attention_backward(
    queries, ext_rows, neighbours, row_offset, grad_attended, prob_blocks, kv_blocks, riders
):
    f32 = jnp.float32
    bf16 = jnp.bfloat16
    row_count = queries.shape[0]
    span = queries.shape[1]
    heads_here = span // HD
    slot_width = neighbours.shape[1] + 1
    score_scale = 1.0 / math.sqrt(HD)
    block_rows = math.gcd(row_count, 512)
    block_count = row_count // block_rows
    query_blocks = queries.reshape(block_count, block_rows, span)
    neighbour_blocks = neighbours.reshape(block_count, block_rows, slot_width - 1)
    grad_blocks = grad_attended.reshape(block_count, block_rows, span)

    def backward_block(carried, inputs):
        query_block, neighbour_block, first_row, grad_block, probabilities, gathered = inputs
        slot_rows, slot_live = slot_index(neighbour_block, first_row, block_rows)
        block_keys = gathered[:, :, 0].reshape(block_rows, slot_width, heads_here, HD).astype(f32)
        block_values = gathered[:, :, 1].reshape(block_rows, slot_width, heads_here, HD).astype(f32)
        grad_mix = grad_block.reshape(block_rows, heads_here, HD).astype(f32)
        grad_weights = jnp.einsum("bhd,bmhd->bhm", grad_mix, block_values)
        grad_scores = (
            probabilities
            * (grad_weights - jnp.sum(probabilities * grad_weights, axis=2, keepdims=True))
            * score_scale
        )
        grad_query = jnp.einsum("bhm,bmhd->bhd", grad_scores, block_keys).reshape(block_rows, span)
        query_wide = query_block.reshape(block_rows, heads_here, HD).astype(f32)
        grad_keys = jnp.einsum("bhm,bhd->bmhd", grad_scores, query_wide)
        rounded = lax.optimization_barrier(probabilities.astype(bf16))
        grad_values = jnp.einsum("bhm,bhd->bmhd", rounded.astype(f32), grad_mix)
        contribution = (
            jnp.stack([grad_keys, grad_values], axis=2)
            .reshape(block_rows, slot_width, 2 * span)
            .astype(bf16)
        )
        for slot in range(1, slot_width):
            carried = carried + jnp.einsum(
                "bx,bc->xc",
                pick_table(slot_rows[:, slot], ext_rows),
                contribution[:, slot],
                preferred_element_type=f32,
            )
        return (carried, (grad_query, contribution[:, 0]))

    carried = jnp.zeros((ext_rows, 2 * span), f32)
    query_grads = []
    for b in range(block_count):
        carried, grad_query = backward_block(
            carried,
            (query_blocks[b], neighbour_blocks[b], row_offset + b * block_rows, grad_blocks[b],
             prob_blocks[b], kv_blocks[b]),
        )
        query_grads.append(grad_query)
        if b == block_count - 1:
            carried, riders = lax.optimization_barrier((carried, riders))
    own_grads = jnp.concatenate([pair[1] for pair in query_grads], axis=0)
    query_grads = jnp.stack([pair[0] for pair in query_grads])
    carried = carried.at[:row_count].add(own_grads.astype(f32))
    return (carried.reshape(ext_rows, 2, span), query_grads.reshape(row_count, span), riders)


def ch_exchange(value):
    size = lax.axis_size("ch")
    return [
        lax.ppermute(value, "ch", [(i, (i + shift) % size) for i in range(size)])
        for shift in range(1, size)
    ]


def ch_assemble(own, others, axis):
    size = len(others) + 1
    index = lax.axis_index("ch")
    pieces = [own] + others
    result = None
    for case in range(size):
        ordered = jnp.concatenate([pieces[(case - j) % size] for j in range(size)], axis=axis)
        result = ordered if result is None else jnp.where(index == case, ordered, result)
    return result


def core_swap(value):
    size = lax.axis_size("pix")
    return lax.ppermute(value, "pix", [(i, i ^ 1) for i in range(size)])


def pix_scatter(terms, width):
    size = lax.axis_size("pix")
    core = lax.axis_index("pix") % 2
    flat = jnp.concatenate([term.reshape(-1, width) for term in terms], axis=0)
    rows = flat.shape[0]
    chunk = -(-rows // (2 * size))
    flat = jnp.pad(flat, ((0, 2 * size * chunk - rows), (0, 0)))
    halves = flat.reshape(2, size * chunk, width)
    keep = jnp.where(core == 0, halves[0], halves[1])
    send = jnp.where(core == 0, halves[1], halves[0])
    mine = keep + core_swap(send)
    parts = lax.all_to_all(mine.reshape(size, chunk, width), "pix", 0, 0, tiled=True)
    return jnp.sum(parts.reshape(size // 2, 2, chunk, width), axis=0)


def pix_gather(reduced_groups, term_groups):
    size = lax.axis_size("pix")
    core = lax.axis_index("pix") % 2
    width = reduced_groups[0].shape[-1]
    joined = jnp.concatenate(reduced_groups, axis=1)
    total = joined.shape[1]
    spread = jnp.broadcast_to(joined[None], (size // 2, 2, total, width))
    got = lax.all_to_all(spread.reshape(size, total, width), "pix", 0, 0, tiled=True)
    other = core_swap(got)
    first = jnp.where(core == 0, got, other)
    second = jnp.where(core == 0, other, got)
    results = []
    offset = 0
    for reduced, terms in zip(reduced_groups, term_groups):
        chunk = reduced.shape[1]
        flat = jnp.concatenate(
            [
                first[:, offset : offset + chunk].reshape(size * chunk, width),
                second[:, offset : offset + chunk].reshape(size * chunk, width),
            ],
            axis=0,
        )
        offset += chunk
        row = 0
        for term in terms:
            count = term.size // width
            results.append(flat[row : row + count].reshape(term.shape))
            row += count
    return results


def per_device(
    fine_pixels, pool_kernel, projections, mixing_weight, send_list, neighbours, cotangent
):
    f32 = jnp.float32
    bf16 = jnp.bfloat16
    row_count = fine_pixels.shape[0]
    half_width = projections.shape[2]
    ch_size = lax.axis_size("ch")
    ch_index = lax.axis_index("ch")
    peer_count = lax.axis_size("pix")
    slot_count = send_list.shape[1]
    grad_scale = 1.0 / math.sqrt(row_count * peer_count)
    send_pick = pick_table(send_list.reshape(-1), row_count)
    fine_others = ch_exchange(fine_pixels)
    kernel_others = ch_exchange(pool_kernel)
    pooled_sum = jnp.dot(fine_pixels, pool_kernel, preferred_element_type=f32)
    for fine_other, kernel_other in zip(fine_others, kernel_others):
        pooled_sum = pooled_sum + jnp.dot(fine_other, kernel_other, preferred_element_type=f32)
    pooled_all = pooled_sum.astype(bf16)
    mix_pieces = mixing_weight.reshape(mixing_weight.shape[0], ch_size, half_width)
    mix_sends = [
        jnp.take(mix_pieces, (ch_index + shift) % ch_size, axis=1) for shift in range(1, ch_size)
    ]
    pooled_all, cot_send, proj_send, mix_sends = lax.optimization_barrier(
        (pooled_all, cotangent, projections, mix_sends)
    )
    cot_others = ch_exchange(cot_send)
    proj_others = ch_exchange(proj_send)
    mix_others = [
        lax.ppermute(mix_send, "ch", [(i, (i + shift) % ch_size) for i in range(ch_size)])
        for shift, mix_send in zip(range(1, ch_size), mix_sends)
    ]
    mix_own = jnp.take(mix_pieces, ch_index, axis=1)
    pooled = lax.dynamic_slice_in_dim(pooled_all, ch_index * half_width, half_width, axis=1)
    upstream = ch_assemble(cotangent, cot_others, axis=1)
    projected = jnp.einsum(
        "rc,kcd->rkd", pooled_all, projections, preferred_element_type=f32
    ).astype(bf16)
    queries = projected[:, 0]
    key_value = projected[:, 1:]
    outgoing = (
        jnp.dot(send_pick, key_value.reshape(row_count, 2 * half_width), preferred_element_type=f32)
        .astype(bf16)
        .reshape(peer_count, slot_count, 2, half_width)
    )
    incoming = lax.all_to_all(outgoing, "pix", split_axis=0, concat_axis=0, tiled=True)
    extended = jnp.concatenate(
        [key_value, incoming.reshape(peer_count * slot_count, 2, half_width)], axis=0
    )
    attended, prob_blocks, kv_blocks = attention_forward(queries, extended, neighbours, 0)
    attended_others = ch_exchange(attended)
    grad_attended = jnp.dot(upstream, mixing_weight.T, preferred_element_type=f32).astype(bf16)
    mixing_term = jnp.dot(attended.T, upstream, preferred_element_type=f32) * grad_scale
    carried, query_grads, (attended_others, mix_others, proj_others) = attention_backward(
        queries, extended.shape[0], neighbours, 0, grad_attended, prob_blocks, kv_blocks,
        (attended_others, mix_others, proj_others),
    )
    branch = jnp.dot(attended, mix_own, preferred_element_type=f32)
    for attended_other, mix_other in zip(attended_others, mix_others):
        branch = branch + jnp.dot(attended_other, mix_other, preferred_element_type=f32)
    section_output = (pooled.astype(f32) + branch).astype(bf16)
    remote_grads = carried[row_count:].reshape(peer_count, slot_count, 2, half_width)
    returned = lax.all_to_all(remote_grads, "pix", split_axis=0, concat_axis=0, tiled=True)
    returned_rows = jnp.einsum(
        "px,pc->xc",
        send_pick,
        returned.reshape(peer_count * slot_count, 2 * half_width).astype(bf16),
        preferred_element_type=f32,
    )
    local_grads = carried[:row_count] + returned_rows.reshape(row_count, 2, half_width)
    grad_projected = jnp.concatenate(
        [query_grads.reshape(row_count, 1, half_width), local_grads], axis=1
    ).astype(bf16)
    grad_others = ch_exchange(grad_projected)
    projection_term = (
        jnp.einsum("rc,rkd->kcd", pooled_all, grad_projected, preferred_element_type=f32)
        * grad_scale
    )
    early_reduced = pix_scatter((projection_term, mixing_term), mixing_weight.shape[1])
    early_reduced, grad_others = lax.optimization_barrier((early_reduced, grad_others))
    pooled_sum = upstream.astype(f32) + jnp.einsum(
        "rkd,kcd->rc", grad_projected, projections, preferred_element_type=f32
    )
    for grad_other, proj_other in zip(grad_others, proj_others):
        pooled_sum = pooled_sum + jnp.einsum(
            "rkd,kcd->rc", grad_other, proj_other, preferred_element_type=f32
        )
    grad_pooled = pooled_sum.astype(bf16)
    kernel_term = jnp.dot(fine_pixels.T, grad_pooled, preferred_element_type=f32) * grad_scale
    fine_gradient = jnp.dot(grad_pooled, pool_kernel.T, preferred_element_type=f32).astype(bf16)
    kernel_reduced = pix_scatter((kernel_term,), mixing_weight.shape[1])
    projection_gradient, mixing_gradient, kernel_gradient = pix_gather(
        (early_reduced, kernel_reduced), ((projection_term, mixing_term), (kernel_term,))
    )
    return (section_output, fine_gradient, kernel_gradient, projection_gradient, mixing_gradient)


def solution(mesh):
    placed = (
        P("pix", "ch"),
        P("ch", None),
        P(None, None, "ch"),
        P("ch", None),
        P("pix", None),
        P("pix", None),
        P("pix", "ch"),
    )
    return jax.shard_map(
        per_device,
        mesh=mesh,
        in_specs=placed,
        out_specs=(
            P("pix", "ch"),
            P("pix", "ch"),
            P("ch", None),
            P(None, None, "ch"),
            P("ch", None),
        ),
        check_vma=False,
    )
```

```python
import math

import jax
import jax.numpy as jnp
from jax import lax
from jax.sharding import PartitionSpec as P

HD = 64


def pick_table(row_ids, total):
    return (row_ids[:, None] == jnp.arange(total, dtype=jnp.int32)[None, :]).astype(jnp.bfloat16)


def slot_index(neighbour_block, first_row, block_rows):
    present = neighbour_block >= 0
    own_rows = first_row + jnp.arange(block_rows, dtype=jnp.int32)
    slot_rows = jnp.concatenate([own_rows[:, None], jnp.where(present, neighbour_block, 0)], axis=1)
    slot_live = jnp.concatenate([jnp.ones((block_rows, 1), bool), present], axis=1)
    return (slot_rows, slot_live)


def attention_forward(queries, extended, neighbours, row_offset):
    f32 = jnp.float32
    bf16 = jnp.bfloat16
    row_count = queries.shape[0]
    span = queries.shape[1]
    ext_rows = extended.shape[0]
    heads_here = span // HD
    slot_width = neighbours.shape[1] + 1
    score_scale = 1.0 / math.sqrt(HD)
    block_rows = math.gcd(row_count, 512)
    block_count = row_count // block_rows
    query_blocks = queries.reshape(block_count, block_rows, span)
    neighbour_blocks = neighbours.reshape(block_count, block_rows, slot_width - 1)
    flattened = extended.reshape(ext_rows, 2 * span)

    def forward_block(inputs):
        query_block, neighbour_block, first_row = inputs
        slot_rows, slot_live = slot_index(neighbour_block, first_row, block_rows)
        pieces = [flattened[first_row : first_row + block_rows]] + [
            jnp.dot(
                pick_table(slot_rows[:, slot], ext_rows), flattened, preferred_element_type=f32
            ).astype(bf16)
            for slot in range(1, slot_width)
        ]
        gathered = jnp.stack(pieces, axis=1).reshape(block_rows, slot_width, 2, span)
        block_keys = gathered[:, :, 0].reshape(block_rows, slot_width, heads_here, HD)
        block_values = gathered[:, :, 1].reshape(block_rows, slot_width, heads_here, HD)
        scores = (
            jnp.einsum(
                "bhd,bmhd->bhm",
                query_block.reshape(block_rows, heads_here, HD),
                block_keys,
                preferred_element_type=f32,
            )
            * score_scale
        )
        shut = slot_live[:, None, :]
        masked = jnp.where(shut, scores, -1e30)
        largest = jnp.max(masked, axis=2, keepdims=True)
        raised = jnp.where(shut, jnp.exp(masked - largest), 0.0)
        probabilities = raised / jnp.sum(raised, axis=2, keepdims=True)
        weights = probabilities.astype(bf16)
        mixture = jnp.einsum("bhm,bmhd->bhd", weights, block_values, preferred_element_type=f32)
        return (mixture.reshape(block_rows, span).astype(bf16), probabilities, gathered)

    outputs = [
        forward_block((query_blocks[b], neighbour_blocks[b], row_offset + b * block_rows))
        for b in range(block_count)
    ]
    attn_blocks = jnp.stack([out[0] for out in outputs])
    prob_blocks = [out[1] for out in outputs]
    kv_blocks = [out[2] for out in outputs]
    return (attn_blocks.reshape(row_count, span), prob_blocks, kv_blocks)


def attention_backward(
    queries, ext_rows, neighbours, row_offset, grad_attended, prob_blocks, kv_blocks, riders
):
    f32 = jnp.float32
    bf16 = jnp.bfloat16
    row_count = queries.shape[0]
    span = queries.shape[1]
    heads_here = span // HD
    slot_width = neighbours.shape[1] + 1
    score_scale = 1.0 / math.sqrt(HD)
    block_rows = math.gcd(row_count, 512)
    block_count = row_count // block_rows
    query_blocks = queries.reshape(block_count, block_rows, span)
    neighbour_blocks = neighbours.reshape(block_count, block_rows, slot_width - 1)
    grad_blocks = grad_attended.reshape(block_count, block_rows, span)

    def backward_block(carried, inputs):
        query_block, neighbour_block, first_row, grad_block, probabilities, gathered = inputs
        slot_rows, slot_live = slot_index(neighbour_block, first_row, block_rows)
        block_keys = gathered[:, :, 0].reshape(block_rows, slot_width, heads_here, HD).astype(f32)
        block_values = gathered[:, :, 1].reshape(block_rows, slot_width, heads_here, HD).astype(f32)
        grad_mix = grad_block.reshape(block_rows, heads_here, HD).astype(f32)
        grad_weights = jnp.einsum("bhd,bmhd->bhm", grad_mix, block_values)
        grad_scores = (
            probabilities
            * (grad_weights - jnp.sum(probabilities * grad_weights, axis=2, keepdims=True))
            * score_scale
        )
        grad_query = jnp.einsum("bhm,bmhd->bhd", grad_scores, block_keys).reshape(block_rows, span)
        query_wide = query_block.reshape(block_rows, heads_here, HD).astype(f32)
        grad_keys = jnp.einsum("bhm,bhd->bmhd", grad_scores, query_wide)
        rounded = lax.optimization_barrier(probabilities.astype(bf16))
        grad_values = jnp.einsum("bhm,bhd->bmhd", rounded.astype(f32), grad_mix)
        contribution = (
            jnp.stack([grad_keys, grad_values], axis=2)
            .reshape(block_rows, slot_width, 2 * span)
            .astype(bf16)
        )
        for slot in range(1, slot_width):
            carried = carried + jnp.einsum(
                "bx,bc->xc",
                pick_table(slot_rows[:, slot], ext_rows),
                contribution[:, slot],
                preferred_element_type=f32,
            )
        return (carried, (grad_query, contribution[:, 0]))

    carried = jnp.zeros((ext_rows, 2 * span), f32)
    query_grads = []
    for b in range(block_count):
        carried, grad_query = backward_block(
            carried,
            (query_blocks[b], neighbour_blocks[b], row_offset + b * block_rows, grad_blocks[b],
             prob_blocks[b], kv_blocks[b]),
        )
        query_grads.append(grad_query)
        if b == 0:
            carried, riders = lax.optimization_barrier((carried, riders))
    own_grads = jnp.concatenate([pair[1] for pair in query_grads], axis=0)
    query_grads = jnp.stack([pair[0] for pair in query_grads])
    carried = carried.at[:row_count].add(own_grads.astype(f32))
    return (carried.reshape(ext_rows, 2, span), query_grads.reshape(row_count, span), riders)


def ch_exchange(value):
    size = lax.axis_size("ch")
    return [
        lax.ppermute(value, "ch", [(i, (i + shift) % size) for i in range(size)])
        for shift in range(1, size)
    ]


def ch_assemble(own, others, axis):
    size = len(others) + 1
    index = lax.axis_index("ch")
    pieces = [own] + others
    result = None
    for case in range(size):
        ordered = jnp.concatenate([pieces[(case - j) % size] for j in range(size)], axis=axis)
        result = ordered if result is None else jnp.where(index == case, ordered, result)
    return result


def core_swap(value):
    size = lax.axis_size("pix")
    return lax.ppermute(value, "pix", [(i, i ^ 1) for i in range(size)])


def pix_scatter(terms, width):
    size = lax.axis_size("pix")
    core = lax.axis_index("pix") % 2
    flat = jnp.concatenate([term.reshape(-1, width) for term in terms], axis=0)
    rows = flat.shape[0]
    chunk = -(-rows // (2 * size))
    flat = jnp.pad(flat, ((0, 2 * size * chunk - rows), (0, 0)))
    halves = flat.reshape(2, size * chunk, width)
    keep = jnp.where(core == 0, halves[0], halves[1])
    send = jnp.where(core == 0, halves[1], halves[0])
    mine = keep + core_swap(send)
    parts = lax.all_to_all(mine.reshape(size, chunk, width), "pix", 0, 0, tiled=True)
    return jnp.sum(parts.reshape(size // 2, 2, chunk, width), axis=0)


def pix_gather(reduced_groups, term_groups):
    size = lax.axis_size("pix")
    core = lax.axis_index("pix") % 2
    width = reduced_groups[0].shape[-1]
    joined = jnp.concatenate(reduced_groups, axis=1)
    total = joined.shape[1]
    spread = jnp.broadcast_to(joined[None], (size // 2, 2, total, width))
    got = lax.all_to_all(spread.reshape(size, total, width), "pix", 0, 0, tiled=True)
    other = core_swap(got)
    first = jnp.where(core == 0, got, other)
    second = jnp.where(core == 0, other, got)
    results = []
    offset = 0
    for reduced, terms in zip(reduced_groups, term_groups):
        chunk = reduced.shape[1]
        flat = jnp.concatenate(
            [
                first[:, offset : offset + chunk].reshape(size * chunk, width),
                second[:, offset : offset + chunk].reshape(size * chunk, width),
            ],
            axis=0,
        )
        offset += chunk
        row = 0
        for term in terms:
            count = term.size // width
            results.append(flat[row : row + count].reshape(term.shape))
            row += count
    return results


def per_device(
    fine_pixels, pool_kernel, projections, mixing_weight, send_list, neighbours, cotangent
):
    f32 = jnp.float32
    bf16 = jnp.bfloat16
    row_count = fine_pixels.shape[0]
    half_width = projections.shape[2]
    ch_size = lax.axis_size("ch")
    ch_index = lax.axis_index("ch")
    peer_count = lax.axis_size("pix")
    slot_count = send_list.shape[1]
    grad_scale = 1.0 / math.sqrt(row_count * peer_count)
    send_pick = pick_table(send_list.reshape(-1), row_count)
    half_rows = row_count // 2
    fine_tops = ch_exchange(fine_pixels[:half_rows])
    fine_bottoms = ch_exchange(fine_pixels[half_rows:])
    kernel_others = ch_exchange(pool_kernel)
    pooled_top = jnp.dot(fine_pixels[:half_rows], pool_kernel, preferred_element_type=f32)
    pooled_bottom = jnp.dot(fine_pixels[half_rows:], pool_kernel, preferred_element_type=f32)
    for fine_top, fine_bottom, kernel_other in zip(fine_tops, fine_bottoms, kernel_others):
        pooled_top = pooled_top + jnp.dot(fine_top, kernel_other, preferred_element_type=f32)
        pooled_bottom = pooled_bottom + jnp.dot(
            fine_bottom, kernel_other, preferred_element_type=f32
        )
    pooled_sum = jnp.concatenate([pooled_top, pooled_bottom], axis=0)
    pooled_all = pooled_sum.astype(bf16)
    mix_pieces = mixing_weight.reshape(mixing_weight.shape[0], ch_size, half_width)
    mix_sends = [
        jnp.take(mix_pieces, (ch_index + shift) % ch_size, axis=1) for shift in range(1, ch_size)
    ]
    pooled_all, cot_send, proj_send, mix_sends = lax.optimization_barrier(
        (pooled_all, cotangent, projections, mix_sends)
    )
    cot_others = ch_exchange(cot_send)
    proj_others = ch_exchange(proj_send)
    mix_others = [
        lax.ppermute(mix_send, "ch", [(i, (i + shift) % ch_size) for i in range(ch_size)])
        for shift, mix_send in zip(range(1, ch_size), mix_sends)
    ]
    mix_own = jnp.take(mix_pieces, ch_index, axis=1)
    pooled = lax.dynamic_slice_in_dim(pooled_all, ch_index * half_width, half_width, axis=1)
    upstream = ch_assemble(cotangent, cot_others, axis=1)
    projected = jnp.einsum(
        "rc,kcd->rkd", pooled_all, projections, preferred_element_type=f32
    ).astype(bf16)
    queries = projected[:, 0]
    key_value = projected[:, 1:]
    outgoing = (
        jnp.dot(send_pick, key_value.reshape(row_count, 2 * half_width), preferred_element_type=f32)
        .astype(bf16)
        .reshape(peer_count, slot_count, 2, half_width)
    )
    incoming = lax.all_to_all(outgoing, "pix", split_axis=0, concat_axis=0, tiled=True)
    extended = jnp.concatenate(
        [key_value, incoming.reshape(peer_count * slot_count, 2, half_width)], axis=0
    )
    attended, prob_blocks, kv_blocks = attention_forward(queries, extended, neighbours, 0)
    attended_others = ch_exchange(attended)
    grad_attended = jnp.dot(upstream, mixing_weight.T, preferred_element_type=f32).astype(bf16)
    mixing_term = jnp.dot(attended.T, upstream, preferred_element_type=f32) * grad_scale
    carried, query_grads, (attended_others, mix_others, proj_others) = attention_backward(
        queries, extended.shape[0], neighbours, 0, grad_attended, prob_blocks, kv_blocks,
        (attended_others, mix_others, proj_others),
    )
    branch = jnp.dot(attended, mix_own, preferred_element_type=f32)
    for attended_other, mix_other in zip(attended_others, mix_others):
        branch = branch + jnp.dot(attended_other, mix_other, preferred_element_type=f32)
    section_output = (pooled.astype(f32) + branch).astype(bf16)
    remote_grads = carried[row_count:].reshape(peer_count, slot_count, 2, half_width)
    returned = lax.all_to_all(remote_grads, "pix", split_axis=0, concat_axis=0, tiled=True)
    returned_rows = jnp.einsum(
        "px,pc->xc",
        send_pick,
        returned.reshape(peer_count * slot_count, 2 * half_width).astype(bf16),
        preferred_element_type=f32,
    )
    local_grads = carried[:row_count] + returned_rows.reshape(row_count, 2, half_width)
    grad_projected = jnp.concatenate(
        [query_grads.reshape(row_count, 1, half_width), local_grads], axis=1
    ).astype(bf16)
    grad_others = ch_exchange(grad_projected)
    projection_term = (
        jnp.einsum("rc,rkd->kcd", pooled_all, grad_projected, preferred_element_type=f32)
        * grad_scale
    )
    early_reduced = pix_scatter((projection_term, mixing_term), mixing_weight.shape[1])
    early_reduced, grad_others = lax.optimization_barrier((early_reduced, grad_others))
    pooled_sum = upstream.astype(f32) + jnp.einsum(
        "rkd,kcd->rc", grad_projected, projections, preferred_element_type=f32
    )
    for grad_other, proj_other in zip(grad_others, proj_others):
        pooled_sum = pooled_sum + jnp.einsum(
            "rkd,kcd->rc", grad_other, proj_other, preferred_element_type=f32
        )
    grad_pooled = pooled_sum.astype(bf16)
    kernel_term = jnp.dot(fine_pixels.T, grad_pooled, preferred_element_type=f32) * grad_scale
    fine_gradient = jnp.dot(grad_pooled, pool_kernel.T, preferred_element_type=f32).astype(bf16)
    kernel_reduced = pix_scatter((kernel_term,), mixing_weight.shape[1])
    projection_gradient, mixing_gradient, kernel_gradient = pix_gather(
        (early_reduced, kernel_reduced), ((projection_term, mixing_term), (kernel_term,))
    )
    return (section_output, fine_gradient, kernel_gradient, projection_gradient, mixing_gradient)


def solution(mesh):
    placed = (
        P("pix", "ch"),
        P("ch", None),
        P(None, None, "ch"),
        P("ch", None),
        P("pix", None),
        P("pix", None),
        P("pix", "ch"),
    )
    return jax.shard_map(
        per_device,
        mesh=mesh,
        in_specs=placed,
        out_specs=(
            P("pix", "ch"),
            P("pix", "ch"),
            P("ch", None),
            P(None, None, "ch"),
            P("ch", None),
        ),
        check_vma=False,
    )
```

```python
import math

import jax
import jax.numpy as jnp
from jax import lax
from jax.sharding import PartitionSpec as P

HD = 64


def pick_table(row_ids, total):
    return (row_ids[:, None] == jnp.arange(total, dtype=jnp.int32)[None, :]).astype(jnp.bfloat16)


def slot_index(neighbour_block, first_row, block_rows):
    present = neighbour_block >= 0
    own_rows = first_row + jnp.arange(block_rows, dtype=jnp.int32)
    slot_rows = jnp.concatenate([own_rows[:, None], jnp.where(present, neighbour_block, 0)], axis=1)
    slot_live = jnp.concatenate([jnp.ones((block_rows, 1), bool), present], axis=1)
    return (slot_rows, slot_live)


def attention_forward(queries, extended, neighbours, row_offset):
    f32 = jnp.float32
    bf16 = jnp.bfloat16
    row_count = queries.shape[0]
    span = queries.shape[1]
    ext_rows = extended.shape[0]
    heads_here = span // HD
    slot_width = neighbours.shape[1] + 1
    score_scale = 1.0 / math.sqrt(HD)
    block_rows = math.gcd(row_count, 512)
    block_count = row_count // block_rows
    query_blocks = queries.reshape(block_count, block_rows, span)
    neighbour_blocks = neighbours.reshape(block_count, block_rows, slot_width - 1)
    flattened = extended.reshape(ext_rows, 2 * span)

    def forward_block(inputs):
        query_block, neighbour_block, first_row = inputs
        slot_rows, slot_live = slot_index(neighbour_block, first_row, block_rows)
        pieces = [flattened[first_row : first_row + block_rows]] + [
            jnp.dot(
                pick_table(slot_rows[:, slot], ext_rows), flattened, preferred_element_type=f32
            ).astype(bf16)
            for slot in range(1, slot_width)
        ]
        gathered = jnp.stack(pieces, axis=1).reshape(block_rows, slot_width, 2, span)
        block_keys = gathered[:, :, 0].reshape(block_rows, slot_width, heads_here, HD)
        block_values = gathered[:, :, 1].reshape(block_rows, slot_width, heads_here, HD)
        scores = (
            jnp.einsum(
                "bhd,bmhd->bhm",
                query_block.reshape(block_rows, heads_here, HD),
                block_keys,
                preferred_element_type=f32,
            )
            * score_scale
        )
        shut = slot_live[:, None, :]
        masked = jnp.where(shut, scores, -1e30)
        largest = jnp.max(masked, axis=2, keepdims=True)
        raised = jnp.where(shut, jnp.exp(masked - largest), 0.0)
        probabilities = raised / jnp.sum(raised, axis=2, keepdims=True)
        weights = probabilities.astype(bf16)
        mixture = jnp.einsum("bhm,bmhd->bhd", weights, block_values, preferred_element_type=f32)
        return (mixture.reshape(block_rows, span).astype(bf16), probabilities, gathered)

    outputs = [
        forward_block((query_blocks[b], neighbour_blocks[b], row_offset + b * block_rows))
        for b in range(block_count)
    ]
    attn_blocks = jnp.stack([out[0] for out in outputs])
    prob_blocks = [out[1] for out in outputs]
    kv_blocks = [out[2] for out in outputs]
    return (attn_blocks.reshape(row_count, span), prob_blocks, kv_blocks)


def attention_backward(
    queries, ext_rows, neighbours, row_offset, grad_attended, prob_blocks, kv_blocks, riders
):
    f32 = jnp.float32
    bf16 = jnp.bfloat16
    row_count = queries.shape[0]
    span = queries.shape[1]
    heads_here = span // HD
    slot_width = neighbours.shape[1] + 1
    score_scale = 1.0 / math.sqrt(HD)
    block_rows = math.gcd(row_count, 512)
    block_count = row_count // block_rows
    query_blocks = queries.reshape(block_count, block_rows, span)
    neighbour_blocks = neighbours.reshape(block_count, block_rows, slot_width - 1)
    grad_blocks = grad_attended.reshape(block_count, block_rows, span)

    def backward_block(carried, inputs):
        query_block, neighbour_block, first_row, grad_block, probabilities, gathered = inputs
        slot_rows, slot_live = slot_index(neighbour_block, first_row, block_rows)
        block_keys = gathered[:, :, 0].reshape(block_rows, slot_width, heads_here, HD).astype(f32)
        block_values = gathered[:, :, 1].reshape(block_rows, slot_width, heads_here, HD).astype(f32)
        grad_mix = grad_block.reshape(block_rows, heads_here, HD).astype(f32)
        grad_weights = jnp.einsum("bhd,bmhd->bhm", grad_mix, block_values)
        grad_scores = (
            probabilities
            * (grad_weights - jnp.sum(probabilities * grad_weights, axis=2, keepdims=True))
            * score_scale
        )
        grad_query = jnp.einsum("bhm,bmhd->bhd", grad_scores, block_keys).reshape(block_rows, span)
        query_wide = query_block.reshape(block_rows, heads_here, HD).astype(f32)
        grad_keys = jnp.einsum("bhm,bhd->bmhd", grad_scores, query_wide)
        rounded = lax.optimization_barrier(probabilities.astype(bf16))
        grad_values = jnp.einsum("bhm,bhd->bmhd", rounded.astype(f32), grad_mix)
        contribution = (
            jnp.stack([grad_keys, grad_values], axis=2)
            .reshape(block_rows, slot_width, 2 * span)
            .astype(bf16)
        )
        for slot in range(1, slot_width):
            carried = carried + jnp.einsum(
                "bx,bc->xc",
                pick_table(slot_rows[:, slot], ext_rows),
                contribution[:, slot],
                preferred_element_type=f32,
            )
        return (carried, (grad_query, contribution[:, 0]))

    carried = jnp.zeros((ext_rows, 2 * span), f32)
    query_grads = []
    for b in range(block_count):
        carried, grad_query = backward_block(
            carried,
            (query_blocks[b], neighbour_blocks[b], row_offset + b * block_rows, grad_blocks[b],
             prob_blocks[b], kv_blocks[b]),
        )
        query_grads.append(grad_query)
        if b == 0:
            carried, riders = lax.optimization_barrier((carried, riders))
    own_grads = jnp.concatenate([pair[1] for pair in query_grads], axis=0)
    query_grads = jnp.stack([pair[0] for pair in query_grads])
    carried = carried.at[:row_count].add(own_grads.astype(f32))
    return (carried.reshape(ext_rows, 2, span), query_grads.reshape(row_count, span), riders)


def ch_exchange(value):
    size = lax.axis_size("ch")
    return [
        lax.ppermute(value, "ch", [(i, (i + shift) % size) for i in range(size)])
        for shift in range(1, size)
    ]


def ch_assemble(own, others, axis):
    size = len(others) + 1
    index = lax.axis_index("ch")
    pieces = [own] + others
    result = None
    for case in range(size):
        ordered = jnp.concatenate([pieces[(case - j) % size] for j in range(size)], axis=axis)
        result = ordered if result is None else jnp.where(index == case, ordered, result)
    return result


def core_swap(value):
    size = lax.axis_size("pix")
    return lax.ppermute(value, "pix", [(i, i ^ 1) for i in range(size)])


def pix_scatter(terms, width):
    size = lax.axis_size("pix")
    core = lax.axis_index("pix") % 2
    flat = jnp.concatenate([term.reshape(-1, width) for term in terms], axis=0)
    rows = flat.shape[0]
    chunk = -(-rows // (2 * size))
    flat = jnp.pad(flat, ((0, 2 * size * chunk - rows), (0, 0)))
    halves = flat.reshape(2, size * chunk, width)
    keep = jnp.where(core == 0, halves[0], halves[1])
    send = jnp.where(core == 0, halves[1], halves[0])
    mine = keep + core_swap(send)
    parts = lax.all_to_all(mine.reshape(size, chunk, width), "pix", 0, 0, tiled=True)
    return jnp.sum(parts.reshape(size // 2, 2, chunk, width), axis=0)


def pix_gather(reduced_groups, term_groups):
    size = lax.axis_size("pix")
    core = lax.axis_index("pix") % 2
    width = reduced_groups[0].shape[-1]
    joined = jnp.concatenate(reduced_groups, axis=1)
    total = joined.shape[1]
    spread = jnp.broadcast_to(joined[None], (size // 2, 2, total, width))
    got = lax.all_to_all(spread.reshape(size, total, width), "pix", 0, 0, tiled=True)
    other = core_swap(got)
    first = jnp.where(core == 0, got, other)
    second = jnp.where(core == 0, other, got)
    results = []
    offset = 0
    for reduced, terms in zip(reduced_groups, term_groups):
        chunk = reduced.shape[1]
        flat = jnp.concatenate(
            [
                first[:, offset : offset + chunk].reshape(size * chunk, width),
                second[:, offset : offset + chunk].reshape(size * chunk, width),
            ],
            axis=0,
        )
        offset += chunk
        row = 0
        for term in terms:
            count = term.size // width
            results.append(flat[row : row + count].reshape(term.shape))
            row += count
    return results


def per_device(
    fine_pixels, pool_kernel, projections, mixing_weight, send_list, neighbours, cotangent
):
    f32 = jnp.float32
    bf16 = jnp.bfloat16
    row_count = fine_pixels.shape[0]
    half_width = projections.shape[2]
    ch_size = lax.axis_size("ch")
    ch_index = lax.axis_index("ch")
    peer_count = lax.axis_size("pix")
    slot_count = send_list.shape[1]
    grad_scale = 1.0 / math.sqrt(row_count * peer_count)
    send_pick = pick_table(send_list.reshape(-1), row_count)
    fine_others = ch_exchange(fine_pixels)
    kernel_others = ch_exchange(pool_kernel)
    pooled_sum = jnp.dot(fine_pixels, pool_kernel, preferred_element_type=f32)
    for fine_other, kernel_other in zip(fine_others, kernel_others):
        pooled_sum = pooled_sum + jnp.dot(fine_other, kernel_other, preferred_element_type=f32)
    pooled_all = pooled_sum.astype(bf16)
    mix_pieces = mixing_weight.reshape(mixing_weight.shape[0], ch_size, half_width)
    mix_sends = [
        jnp.take(mix_pieces, (ch_index + shift) % ch_size, axis=1) for shift in range(1, ch_size)
    ]
    pooled_all, cot_send, proj_send, mix_sends = lax.optimization_barrier(
        (pooled_all, cotangent, projections, mix_sends)
    )
    cot_others = ch_exchange(cot_send)
    proj_others = ch_exchange(proj_send)
    mix_others = [
        lax.ppermute(mix_send, "ch", [(i, (i + shift) % ch_size) for i in range(ch_size)])
        for shift, mix_send in zip(range(1, ch_size), mix_sends)
    ]
    mix_own = jnp.take(mix_pieces, ch_index, axis=1)
    pooled = lax.dynamic_slice_in_dim(pooled_all, ch_index * half_width, half_width, axis=1)
    upstream = ch_assemble(cotangent, cot_others, axis=1)
    projected = jnp.einsum(
        "rc,kcd->rkd", pooled_all, projections, preferred_element_type=f32
    ).astype(bf16)
    queries = projected[:, 0]
    key_value = projected[:, 1:]
    outgoing = (
        jnp.dot(send_pick, key_value.reshape(row_count, 2 * half_width), preferred_element_type=f32)
        .astype(bf16)
        .reshape(peer_count, slot_count, 2, half_width)
    )
    incoming = lax.all_to_all(outgoing, "pix", split_axis=0, concat_axis=0, tiled=True)
    extended = jnp.concatenate(
        [key_value, incoming.reshape(peer_count * slot_count, 2, half_width)], axis=0
    )
    attended, prob_blocks, kv_blocks = attention_forward(queries, extended, neighbours, 0)
    attended_others = ch_exchange(attended)
    grad_attended = jnp.dot(upstream, mixing_weight.T, preferred_element_type=f32).astype(bf16)
    mixing_term = jnp.dot(attended.T, upstream, preferred_element_type=f32) * grad_scale
    carried, query_grads, (attended_others, mix_others, proj_others) = attention_backward(
        queries, extended.shape[0], neighbours, 0, grad_attended, prob_blocks, kv_blocks,
        (attended_others, mix_others, proj_others),
    )
    branch = jnp.dot(attended, mix_own, preferred_element_type=f32)
    for attended_other, mix_other in zip(attended_others, mix_others):
        branch = branch + jnp.dot(attended_other, mix_other, preferred_element_type=f32)
    section_output = (pooled.astype(f32) + branch).astype(bf16)
    remote_grads = carried[row_count:].reshape(peer_count, slot_count, 2, half_width)
    returned = lax.all_to_all(remote_grads, "pix", split_axis=0, concat_axis=0, tiled=True)
    returned_rows = jnp.einsum(
        "px,pc->xc",
        send_pick,
        returned.reshape(peer_count * slot_count, 2 * half_width).astype(bf16),
        preferred_element_type=f32,
    )
    local_grads = carried[:row_count] + returned_rows.reshape(row_count, 2, half_width)
    grad_projected = jnp.concatenate(
        [query_grads.reshape(row_count, 1, half_width), local_grads], axis=1
    ).astype(bf16)
    grad_others = ch_exchange(grad_projected)
    projection_term = (
        jnp.einsum("rc,rkd->kcd", pooled_all, grad_projected, preferred_element_type=f32)
        * grad_scale
    )
    early_reduced = pix_scatter((projection_term, mixing_term), mixing_weight.shape[1])
    pooled_sum = upstream.astype(f32) + jnp.einsum(
        "rkd,kcd->rc", grad_projected, projections, preferred_element_type=f32
    )
    for grad_other, proj_other in zip(grad_others, proj_others):
        pooled_sum = pooled_sum + jnp.einsum(
            "rkd,kcd->rc", grad_other, proj_other, preferred_element_type=f32
        )
    grad_pooled = pooled_sum.astype(bf16)
    kernel_term = jnp.dot(fine_pixels.T, grad_pooled, preferred_element_type=f32) * grad_scale
    fine_gradient = jnp.dot(grad_pooled, pool_kernel.T, preferred_element_type=f32).astype(bf16)
    kernel_reduced = pix_scatter((kernel_term,), mixing_weight.shape[1])
    projection_gradient, mixing_gradient, kernel_gradient = pix_gather(
        (early_reduced, kernel_reduced), ((projection_term, mixing_term), (kernel_term,))
    )
    return (section_output, fine_gradient, kernel_gradient, projection_gradient, mixing_gradient)


def solution(mesh):
    placed = (
        P("pix", "ch"),
        P("ch", None),
        P(None, None, "ch"),
        P("ch", None),
        P("pix", None),
        P("pix", None),
        P("pix", "ch"),
    )
    return jax.shard_map(
        per_device,
        mesh=mesh,
        in_specs=placed,
        out_specs=(
            P("pix", "ch"),
            P("pix", "ch"),
            P("ch", None),
            P(None, None, "ch"),
            P("ch", None),
        ),
        check_vma=False,
    )
```

```python
import math

import jax
import jax.numpy as jnp
from jax import lax
from jax.sharding import PartitionSpec as P

HD = 64


def pick_table(row_ids, total):
    return (row_ids[:, None] == jnp.arange(total, dtype=jnp.int32)[None, :]).astype(jnp.bfloat16)


def slot_index(neighbour_block, first_row, block_rows):
    present = neighbour_block >= 0
    own_rows = first_row + jnp.arange(block_rows, dtype=jnp.int32)
    slot_rows = jnp.concatenate([own_rows[:, None], jnp.where(present, neighbour_block, 0)], axis=1)
    slot_live = jnp.concatenate([jnp.ones((block_rows, 1), bool), present], axis=1)
    return (slot_rows, slot_live)


def attention_forward(queries, extended, neighbours, row_offset):
    f32 = jnp.float32
    bf16 = jnp.bfloat16
    row_count = queries.shape[0]
    span = queries.shape[1]
    ext_rows = extended.shape[0]
    heads_here = span // HD
    slot_width = neighbours.shape[1] + 1
    score_scale = 1.0 / math.sqrt(HD)
    block_rows = math.gcd(row_count, 512)
    block_count = row_count // block_rows
    query_blocks = queries.reshape(block_count, block_rows, span)
    neighbour_blocks = neighbours.reshape(block_count, block_rows, slot_width - 1)
    flattened = extended.reshape(ext_rows, 2 * span)

    def forward_block(inputs):
        query_block, neighbour_block, first_row = inputs
        slot_rows, slot_live = slot_index(neighbour_block, first_row, block_rows)
        pieces = [flattened[first_row : first_row + block_rows]] + [
            jnp.dot(
                pick_table(slot_rows[:, slot], ext_rows), flattened, preferred_element_type=f32
            ).astype(bf16)
            for slot in range(1, slot_width)
        ]
        gathered = jnp.stack(pieces, axis=1).reshape(block_rows, slot_width, 2, span)
        block_keys = gathered[:, :, 0].reshape(block_rows, slot_width, heads_here, HD)
        block_values = gathered[:, :, 1].reshape(block_rows, slot_width, heads_here, HD)
        scores = (
            jnp.einsum(
                "bhd,bmhd->bhm",
                query_block.reshape(block_rows, heads_here, HD),
                block_keys,
                preferred_element_type=f32,
            )
            * score_scale
        )
        shut = slot_live[:, None, :]
        masked = jnp.where(shut, scores, -1e30)
        largest = jnp.max(masked, axis=2, keepdims=True)
        raised = jnp.where(shut, jnp.exp(masked - largest), 0.0)
        probabilities = raised / jnp.sum(raised, axis=2, keepdims=True)
        weights = probabilities.astype(bf16)
        mixture = jnp.einsum("bhm,bmhd->bhd", weights, block_values, preferred_element_type=f32)
        return (mixture.reshape(block_rows, span).astype(bf16), probabilities, gathered)

    outputs = [
        forward_block((query_blocks[b], neighbour_blocks[b], row_offset + b * block_rows))
        for b in range(block_count)
    ]
    attn_blocks = jnp.stack([out[0] for out in outputs])
    prob_blocks = [out[1] for out in outputs]
    kv_blocks = [out[2] for out in outputs]
    return (attn_blocks.reshape(row_count, span), prob_blocks, kv_blocks)


def attention_backward(
    queries, ext_rows, neighbours, row_offset, grad_attended, prob_blocks, kv_blocks, riders
):
    f32 = jnp.float32
    bf16 = jnp.bfloat16
    row_count = queries.shape[0]
    span = queries.shape[1]
    heads_here = span // HD
    slot_width = neighbours.shape[1] + 1
    score_scale = 1.0 / math.sqrt(HD)
    block_rows = math.gcd(row_count, 512)
    block_count = row_count // block_rows
    query_blocks = queries.reshape(block_count, block_rows, span)
    neighbour_blocks = neighbours.reshape(block_count, block_rows, slot_width - 1)
    grad_blocks = grad_attended.reshape(block_count, block_rows, span)

    def backward_block(carried, inputs):
        query_block, neighbour_block, first_row, grad_block, probabilities, gathered = inputs
        slot_rows, slot_live = slot_index(neighbour_block, first_row, block_rows)
        block_keys = gathered[:, :, 0].reshape(block_rows, slot_width, heads_here, HD).astype(f32)
        block_values = gathered[:, :, 1].reshape(block_rows, slot_width, heads_here, HD).astype(f32)
        grad_mix = grad_block.reshape(block_rows, heads_here, HD).astype(f32)
        grad_weights = jnp.einsum("bhd,bmhd->bhm", grad_mix, block_values)
        grad_scores = (
            probabilities
            * (grad_weights - jnp.sum(probabilities * grad_weights, axis=2, keepdims=True))
            * score_scale
        )
        grad_query = jnp.einsum("bhm,bmhd->bhd", grad_scores, block_keys).reshape(block_rows, span)
        query_wide = query_block.reshape(block_rows, heads_here, HD).astype(f32)
        grad_keys = jnp.einsum("bhm,bhd->bmhd", grad_scores, query_wide)
        rounded = lax.optimization_barrier(probabilities.astype(bf16))
        grad_values = jnp.einsum("bhm,bhd->bmhd", rounded.astype(f32), grad_mix)
        contribution = (
            jnp.stack([grad_keys, grad_values], axis=2)
            .reshape(block_rows, slot_width, 2 * span)
            .astype(bf16)
        )
        for slot in range(1, slot_width):
            carried = carried + jnp.einsum(
                "bx,bc->xc",
                pick_table(slot_rows[:, slot], ext_rows),
                contribution[:, slot],
                preferred_element_type=f32,
            )
        return (carried, (grad_query, contribution[:, 0]))

    carried = jnp.zeros((ext_rows, 2 * span), f32)
    query_grads = []
    for b in range(block_count):
        carried, grad_query = backward_block(
            carried,
            (query_blocks[b], neighbour_blocks[b], row_offset + b * block_rows, grad_blocks[b],
             prob_blocks[b], kv_blocks[b]),
        )
        query_grads.append(grad_query)
        if b == 0:
            carried, riders = lax.optimization_barrier((carried, riders))
    own_grads = jnp.concatenate([pair[1] for pair in query_grads], axis=0)
    query_grads = jnp.stack([pair[0] for pair in query_grads])
    carried = carried.at[:row_count].add(own_grads.astype(f32))
    return (carried.reshape(ext_rows, 2, span), query_grads.reshape(row_count, span), riders)


def ch_exchange(value):
    size = lax.axis_size("ch")
    return [
        lax.ppermute(value, "ch", [(i, (i + shift) % size) for i in range(size)])
        for shift in range(1, size)
    ]


def ch_assemble(own, others, axis):
    size = len(others) + 1
    index = lax.axis_index("ch")
    pieces = [own] + others
    result = None
    for case in range(size):
        ordered = jnp.concatenate([pieces[(case - j) % size] for j in range(size)], axis=axis)
        result = ordered if result is None else jnp.where(index == case, ordered, result)
    return result


def core_swap(value):
    size = lax.axis_size("pix")
    return lax.ppermute(value, "pix", [(i, i ^ 1) for i in range(size)])


def pix_scatter(terms, width):
    size = lax.axis_size("pix")
    core = lax.axis_index("pix") % 2
    flat = jnp.concatenate([term.reshape(-1, width) for term in terms], axis=0)
    rows = flat.shape[0]
    chunk = -(-rows // (2 * size))
    flat = jnp.pad(flat, ((0, 2 * size * chunk - rows), (0, 0)))
    halves = flat.reshape(2, size * chunk, width)
    keep = jnp.where(core == 0, halves[0], halves[1])
    send = jnp.where(core == 0, halves[1], halves[0])
    mine = keep + core_swap(send)
    parts = lax.all_to_all(mine.reshape(size, chunk, width), "pix", 0, 0, tiled=True)
    return jnp.sum(parts.reshape(size // 2, 2, chunk, width), axis=0)


def pix_gather(reduced_groups, term_groups):
    size = lax.axis_size("pix")
    core = lax.axis_index("pix") % 2
    width = reduced_groups[0].shape[-1]
    joined = jnp.concatenate(reduced_groups, axis=1)
    total = joined.shape[1]
    spread = jnp.broadcast_to(joined[None], (size // 2, 2, total, width))
    got = lax.all_to_all(spread.reshape(size, total, width), "pix", 0, 0, tiled=True)
    other = core_swap(got)
    first = jnp.where(core == 0, got, other)
    second = jnp.where(core == 0, other, got)
    results = []
    offset = 0
    for reduced, terms in zip(reduced_groups, term_groups):
        chunk = reduced.shape[1]
        flat = jnp.concatenate(
            [
                first[:, offset : offset + chunk].reshape(size * chunk, width),
                second[:, offset : offset + chunk].reshape(size * chunk, width),
            ],
            axis=0,
        )
        offset += chunk
        row = 0
        for term in terms:
            count = term.size // width
            results.append(flat[row : row + count].reshape(term.shape))
            row += count
    return results


def per_device(
    fine_pixels, pool_kernel, projections, mixing_weight, send_list, neighbours, cotangent
):
    f32 = jnp.float32
    bf16 = jnp.bfloat16
    row_count = fine_pixels.shape[0]
    half_width = projections.shape[2]
    ch_size = lax.axis_size("ch")
    ch_index = lax.axis_index("ch")
    peer_count = lax.axis_size("pix")
    slot_count = send_list.shape[1]
    grad_scale = 1.0 / math.sqrt(row_count * peer_count)
    send_pick = pick_table(send_list.reshape(-1), row_count)
    fine_others = ch_exchange(fine_pixels)
    kernel_others = ch_exchange(pool_kernel)
    pooled_sum = jnp.dot(fine_pixels, pool_kernel, preferred_element_type=f32)
    for fine_other, kernel_other in zip(fine_others, kernel_others):
        pooled_sum = pooled_sum + jnp.dot(fine_other, kernel_other, preferred_element_type=f32)
    pooled_all = pooled_sum.astype(bf16)
    mix_pieces = mixing_weight.reshape(mixing_weight.shape[0], ch_size, half_width)
    mix_sends = [
        jnp.take(mix_pieces, (ch_index + shift) % ch_size, axis=1) for shift in range(1, ch_size)
    ]
    pooled_all, cot_send, proj_send, mix_sends = lax.optimization_barrier(
        (pooled_all, cotangent, projections, mix_sends)
    )
    cot_others = ch_exchange(cot_send)
    proj_others = ch_exchange(proj_send)
    mix_others = [
        lax.ppermute(mix_send, "ch", [(i, (i + shift) % ch_size) for i in range(ch_size)])
        for shift, mix_send in zip(range(1, ch_size), mix_sends)
    ]
    mix_own = jnp.take(mix_pieces, ch_index, axis=1)
    pooled = lax.dynamic_slice_in_dim(pooled_all, ch_index * half_width, half_width, axis=1)
    upstream = ch_assemble(cotangent, cot_others, axis=1)
    projected = jnp.einsum(
        "rc,kcd->rkd", pooled_all, projections, preferred_element_type=f32
    ).astype(bf16)
    queries = projected[:, 0]
    key_value = projected[:, 1:]
    outgoing = (
        jnp.dot(send_pick, key_value.reshape(row_count, 2 * half_width), preferred_element_type=f32)
        .astype(bf16)
        .reshape(peer_count, slot_count, 2, half_width)
    )
    incoming = lax.all_to_all(outgoing, "pix", split_axis=0, concat_axis=0, tiled=True)
    extended = jnp.concatenate(
        [key_value, incoming.reshape(peer_count * slot_count, 2, half_width)], axis=0
    )
    attended, prob_blocks, kv_blocks = attention_forward(queries, extended, neighbours, 0)
    attended_others = ch_exchange(attended)
    grad_attended = jnp.dot(upstream, mixing_weight.T, preferred_element_type=f32).astype(bf16)
    mixing_term = jnp.dot(attended.T, upstream, preferred_element_type=f32) * grad_scale
    carried, query_grads, (attended_others, mix_others, proj_others) = attention_backward(
        queries, extended.shape[0], neighbours, 0, grad_attended, prob_blocks, kv_blocks,
        (attended_others, mix_others, proj_others),
    )
    branch = jnp.dot(attended, mix_own, preferred_element_type=f32)
    for attended_other, mix_other in zip(attended_others, mix_others):
        branch = branch + jnp.dot(attended_other, mix_other, preferred_element_type=f32)
    section_output = (pooled.astype(f32) + branch).astype(bf16)
    query_part = query_grads.astype(bf16)
    query_others = ch_exchange(query_part)
    remote_grads = carried[row_count:].reshape(peer_count, slot_count, 2, half_width)
    returned = lax.all_to_all(remote_grads, "pix", split_axis=0, concat_axis=0, tiled=True)
    returned_rows = jnp.einsum(
        "px,pc->xc",
        send_pick,
        returned.reshape(peer_count * slot_count, 2 * half_width).astype(bf16),
        preferred_element_type=f32,
    )
    local_grads = carried[:row_count] + returned_rows.reshape(row_count, 2, half_width)
    grad_projected = jnp.concatenate(
        [query_grads.reshape(row_count, 1, half_width), local_grads], axis=1
    ).astype(bf16)
    grad_others = ch_exchange(local_grads.astype(bf16))
    projection_term = (
        jnp.einsum("rc,rkd->kcd", pooled_all, grad_projected, preferred_element_type=f32)
        * grad_scale
    )
    early_reduced = pix_scatter((projection_term, mixing_term), mixing_weight.shape[1])
    pooled_sum = upstream.astype(f32) + jnp.einsum(
        "rkd,kcd->rc", grad_projected, projections, preferred_element_type=f32
    )
    for query_other, grad_other, proj_other in zip(query_others, grad_others, proj_others):
        pooled_sum = pooled_sum + jnp.einsum(
            "rd,cd->rc", query_other, proj_other[0], preferred_element_type=f32
        )
        pooled_sum = pooled_sum + jnp.einsum(
            "rkd,kcd->rc", grad_other, proj_other[1:], preferred_element_type=f32
        )
    grad_pooled = pooled_sum.astype(bf16)
    kernel_term = jnp.dot(fine_pixels.T, grad_pooled, preferred_element_type=f32) * grad_scale
    fine_gradient = jnp.dot(grad_pooled, pool_kernel.T, preferred_element_type=f32).astype(bf16)
    kernel_reduced = pix_scatter((kernel_term,), mixing_weight.shape[1])
    projection_gradient, mixing_gradient, kernel_gradient = pix_gather(
        (early_reduced, kernel_reduced), ((projection_term, mixing_term), (kernel_term,))
    )
    return (section_output, fine_gradient, kernel_gradient, projection_gradient, mixing_gradient)


def solution(mesh):
    placed = (
        P("pix", "ch"),
        P("ch", None),
        P(None, None, "ch"),
        P("ch", None),
        P("pix", None),
        P("pix", None),
        P("pix", "ch"),
    )
    return jax.shard_map(
        per_device,
        mesh=mesh,
        in_specs=placed,
        out_specs=(
            P("pix", "ch"),
            P("pix", "ch"),
            P("ch", None),
            P(None, None, "ch"),
            P("ch", None),
        ),
        check_vma=False,
    )
```

```python
import math

import jax
import jax.numpy as jnp
from jax import lax
from jax.sharding import PartitionSpec as P

HD = 64


def pick_table(row_ids, total):
    return (row_ids[:, None] == jnp.arange(total, dtype=jnp.int32)[None, :]).astype(jnp.bfloat16)


def slot_index(neighbour_block, first_row, block_rows):
    present = neighbour_block >= 0
    own_rows = first_row + jnp.arange(block_rows, dtype=jnp.int32)
    slot_rows = jnp.concatenate([own_rows[:, None], jnp.where(present, neighbour_block, 0)], axis=1)
    slot_live = jnp.concatenate([jnp.ones((block_rows, 1), bool), present], axis=1)
    return (slot_rows, slot_live)


def attention_forward(queries, extended, neighbours, row_offset):
    f32 = jnp.float32
    bf16 = jnp.bfloat16
    row_count = queries.shape[0]
    span = queries.shape[1]
    ext_rows = extended.shape[0]
    heads_here = span // HD
    slot_width = neighbours.shape[1] + 1
    score_scale = 1.0 / math.sqrt(HD)
    block_rows = math.gcd(row_count, 512)
    block_count = row_count // block_rows
    query_blocks = queries.reshape(block_count, block_rows, span)
    neighbour_blocks = neighbours.reshape(block_count, block_rows, slot_width - 1)
    flattened = extended.reshape(ext_rows, 2 * span)

    def forward_block(inputs):
        query_block, neighbour_block, first_row = inputs
        slot_rows, slot_live = slot_index(neighbour_block, first_row, block_rows)
        pieces = [flattened[first_row : first_row + block_rows]] + [
            jnp.dot(
                pick_table(slot_rows[:, slot], ext_rows), flattened, preferred_element_type=f32
            ).astype(bf16)
            for slot in range(1, slot_width)
        ]
        gathered = jnp.stack(pieces, axis=1).reshape(block_rows, slot_width, 2, span)
        block_keys = gathered[:, :, 0].reshape(block_rows, slot_width, heads_here, HD)
        block_values = gathered[:, :, 1].reshape(block_rows, slot_width, heads_here, HD)
        scores = (
            jnp.einsum(
                "bhd,bmhd->bhm",
                query_block.reshape(block_rows, heads_here, HD),
                block_keys,
                preferred_element_type=f32,
            )
            * score_scale
        )
        shut = slot_live[:, None, :]
        masked = jnp.where(shut, scores, -1e30)
        largest = jnp.max(masked, axis=2, keepdims=True)
        raised = jnp.where(shut, jnp.exp(masked - largest), 0.0)
        probabilities = raised / jnp.sum(raised, axis=2, keepdims=True)
        weights = probabilities.astype(bf16)
        mixture = jnp.einsum("bhm,bmhd->bhd", weights, block_values, preferred_element_type=f32)
        return (mixture.reshape(block_rows, span).astype(bf16), probabilities, gathered)

    outputs = [
        forward_block((query_blocks[b], neighbour_blocks[b], row_offset + b * block_rows))
        for b in range(block_count)
    ]
    attn_blocks = jnp.stack([out[0] for out in outputs])
    prob_blocks = [out[1] for out in outputs]
    kv_blocks = [out[2] for out in outputs]
    return (attn_blocks.reshape(row_count, span), prob_blocks, kv_blocks)


def attention_backward(
    queries, ext_rows, neighbours, row_offset, grad_attended, prob_blocks, kv_blocks, riders
):
    f32 = jnp.float32
    bf16 = jnp.bfloat16
    row_count = queries.shape[0]
    span = queries.shape[1]
    heads_here = span // HD
    slot_width = neighbours.shape[1] + 1
    score_scale = 1.0 / math.sqrt(HD)
    block_rows = math.gcd(row_count, 512)
    block_count = row_count // block_rows
    query_blocks = queries.reshape(block_count, block_rows, span)
    neighbour_blocks = neighbours.reshape(block_count, block_rows, slot_width - 1)
    grad_blocks = grad_attended.reshape(block_count, block_rows, span)

    def backward_block(carried, inputs):
        query_block, neighbour_block, first_row, grad_block, probabilities, gathered = inputs
        slot_rows, slot_live = slot_index(neighbour_block, first_row, block_rows)
        block_keys = gathered[:, :, 0].reshape(block_rows, slot_width, heads_here, HD).astype(f32)
        block_values = gathered[:, :, 1].reshape(block_rows, slot_width, heads_here, HD).astype(f32)
        grad_mix = grad_block.reshape(block_rows, heads_here, HD).astype(f32)
        grad_weights = jnp.einsum("bhd,bmhd->bhm", grad_mix, block_values)
        grad_scores = (
            probabilities
            * (grad_weights - jnp.sum(probabilities * grad_weights, axis=2, keepdims=True))
            * score_scale
        )
        grad_query = jnp.einsum("bhm,bmhd->bhd", grad_scores, block_keys).reshape(block_rows, span)
        query_wide = query_block.reshape(block_rows, heads_here, HD).astype(f32)
        grad_keys = jnp.einsum("bhm,bhd->bmhd", grad_scores, query_wide)
        rounded = lax.optimization_barrier(probabilities.astype(bf16))
        grad_values = jnp.einsum("bhm,bhd->bmhd", rounded.astype(f32), grad_mix)
        contribution = (
            jnp.stack([grad_keys, grad_values], axis=2)
            .reshape(block_rows, slot_width, 2 * span)
            .astype(bf16)
        )
        for slot in range(1, slot_width):
            carried = carried + jnp.einsum(
                "bx,bc->xc",
                pick_table(slot_rows[:, slot], ext_rows),
                contribution[:, slot],
                preferred_element_type=f32,
            )
        return (carried, (grad_query, contribution[:, 0]))

    carried = jnp.zeros((ext_rows, 2 * span), f32)
    query_grads = []
    for b in range(block_count):
        carried, grad_query = backward_block(
            carried,
            (query_blocks[b], neighbour_blocks[b], row_offset + b * block_rows, grad_blocks[b],
             prob_blocks[b], kv_blocks[b]),
        )
        query_grads.append(grad_query)
        if b == block_count - 1:
            carried, riders = lax.optimization_barrier((carried, riders))
    own_grads = jnp.concatenate([pair[1] for pair in query_grads], axis=0)
    query_grads = jnp.stack([pair[0] for pair in query_grads])
    carried = carried.at[:row_count].add(own_grads.astype(f32))
    return (carried.reshape(ext_rows, 2, span), query_grads.reshape(row_count, span), riders)


def ch_exchange(value):
    size = lax.axis_size("ch")
    return [
        lax.ppermute(value, "ch", [(i, (i + shift) % size) for i in range(size)])
        for shift in range(1, size)
    ]


def ch_assemble(own, others, axis):
    size = len(others) + 1
    index = lax.axis_index("ch")
    pieces = [own] + others
    result = None
    for case in range(size):
        ordered = jnp.concatenate([pieces[(case - j) % size] for j in range(size)], axis=axis)
        result = ordered if result is None else jnp.where(index == case, ordered, result)
    return result


def core_swap(value):
    size = lax.axis_size("pix")
    return lax.ppermute(value, "pix", [(i, i ^ 1) for i in range(size)])


def pix_scatter(terms, width):
    size = lax.axis_size("pix")
    core = lax.axis_index("pix") % 2
    flat = jnp.concatenate([term.reshape(-1, width) for term in terms], axis=0)
    rows = flat.shape[0]
    chunk = -(-rows // (2 * size))
    flat = jnp.pad(flat, ((0, 2 * size * chunk - rows), (0, 0)))
    halves = flat.reshape(2, size * chunk, width)
    keep = jnp.where(core == 0, halves[0], halves[1])
    send = jnp.where(core == 0, halves[1], halves[0])
    mine = keep + core_swap(send)
    parts = lax.all_to_all(mine.reshape(size, chunk, width), "pix", 0, 0, tiled=True)
    return jnp.sum(parts.reshape(size // 2, 2, chunk, width), axis=0)


def pix_gather(reduced_groups, term_groups):
    size = lax.axis_size("pix")
    core = lax.axis_index("pix") % 2
    width = reduced_groups[0].shape[-1]
    joined = jnp.concatenate(reduced_groups, axis=1)
    total = joined.shape[1]
    spread = jnp.broadcast_to(joined[None], (size // 2, 2, total, width))
    got = lax.all_to_all(spread.reshape(size, total, width), "pix", 0, 0, tiled=True)
    other = core_swap(got)
    first = jnp.where(core == 0, got, other)
    second = jnp.where(core == 0, other, got)
    results = []
    offset = 0
    for reduced, terms in zip(reduced_groups, term_groups):
        chunk = reduced.shape[1]
        flat = jnp.concatenate(
            [
                first[:, offset : offset + chunk].reshape(size * chunk, width),
                second[:, offset : offset + chunk].reshape(size * chunk, width),
            ],
            axis=0,
        )
        offset += chunk
        row = 0
        for term in terms:
            count = term.size // width
            results.append(flat[row : row + count].reshape(term.shape))
            row += count
    return results


def per_device(
    fine_pixels, pool_kernel, projections, mixing_weight, send_list, neighbours, cotangent
):
    f32 = jnp.float32
    bf16 = jnp.bfloat16
    row_count = fine_pixels.shape[0]
    half_width = projections.shape[2]
    ch_size = lax.axis_size("ch")
    ch_index = lax.axis_index("ch")
    peer_count = lax.axis_size("pix")
    slot_count = send_list.shape[1]
    grad_scale = 1.0 / math.sqrt(row_count * peer_count)
    send_pick = pick_table(send_list.reshape(-1), row_count)
    fine_others = ch_exchange(fine_pixels)
    kernel_others = ch_exchange(pool_kernel)
    pooled_sum = jnp.dot(fine_pixels, pool_kernel, preferred_element_type=f32)
    for fine_other, kernel_other in zip(fine_others, kernel_others):
        pooled_sum = pooled_sum + jnp.dot(fine_other, kernel_other, preferred_element_type=f32)
    pooled_all = pooled_sum.astype(bf16)
    mix_pieces = mixing_weight.reshape(mixing_weight.shape[0], ch_size, half_width)
    mix_sends = [
        jnp.take(mix_pieces, (ch_index + shift) % ch_size, axis=1) for shift in range(1, ch_size)
    ]
    pooled_all, cot_send, proj_send, mix_sends = lax.optimization_barrier(
        (pooled_all, cotangent, projections, mix_sends)
    )
    cot_others = ch_exchange(cot_send)
    proj_others = ch_exchange(proj_send)
    mix_others = [
        lax.ppermute(mix_send, "ch", [(i, (i + shift) % ch_size) for i in range(ch_size)])
        for shift, mix_send in zip(range(1, ch_size), mix_sends)
    ]
    mix_own = jnp.take(mix_pieces, ch_index, axis=1)
    pooled = lax.dynamic_slice_in_dim(pooled_all, ch_index * half_width, half_width, axis=1)
    upstream = ch_assemble(cotangent, cot_others, axis=1)
    projected = jnp.einsum(
        "rc,kcd->rkd", pooled_all, projections, preferred_element_type=f32
    ).astype(bf16)
    queries = projected[:, 0]
    key_value = projected[:, 1:]
    outgoing = (
        jnp.dot(send_pick, key_value.reshape(row_count, 2 * half_width), preferred_element_type=f32)
        .astype(bf16)
        .reshape(peer_count, slot_count, 2, half_width)
    )
    incoming = lax.all_to_all(outgoing, "pix", split_axis=0, concat_axis=0, tiled=True)
    extended = jnp.concatenate(
        [key_value, incoming.reshape(peer_count * slot_count, 2, half_width)], axis=0
    )
    attended, prob_blocks, kv_blocks = attention_forward(queries, extended, neighbours, 0)
    attended_others = ch_exchange(attended)
    grad_attended = jnp.dot(upstream, mixing_weight.T, preferred_element_type=f32).astype(bf16)
    mixing_term = jnp.dot(attended.T, upstream, preferred_element_type=f32) * grad_scale
    carried, query_grads, (attended_others, mix_others, proj_others) = attention_backward(
        queries, extended.shape[0], neighbours, 0, grad_attended, prob_blocks, kv_blocks,
        (attended_others, mix_others, proj_others),
    )
    branch = jnp.dot(attended, mix_own, preferred_element_type=f32)
    for attended_other, mix_other in zip(attended_others, mix_others):
        branch = branch + jnp.dot(attended_other, mix_other, preferred_element_type=f32)
    section_output = (pooled.astype(f32) + branch).astype(bf16)
    remote_grads = carried[row_count:].reshape(peer_count, slot_count, 2, half_width)
    returned = lax.all_to_all(remote_grads, "pix", split_axis=0, concat_axis=0, tiled=True)
    returned_rows = jnp.einsum(
        "px,pc->xc",
        send_pick,
        returned.reshape(peer_count * slot_count, 2 * half_width).astype(bf16),
        preferred_element_type=f32,
    )
    local_grads = carried[:row_count] + returned_rows.reshape(row_count, 2, half_width)
    grad_projected = jnp.concatenate(
        [query_grads.reshape(row_count, 1, half_width), local_grads], axis=1
    ).astype(bf16)
    grad_others = ch_exchange(grad_projected)
    projection_term = (
        jnp.einsum("rc,rkd->kcd", pooled_all, grad_projected, preferred_element_type=f32)
        * grad_scale
    )
    early_reduced = pix_scatter((projection_term, mixing_term), mixing_weight.shape[1])
    pooled_sum = upstream.astype(f32) + jnp.einsum(
        "rkd,kcd->rc", grad_projected, projections, preferred_element_type=f32
    )
    for grad_other, proj_other in zip(grad_others, proj_others):
        pooled_sum = pooled_sum + jnp.einsum(
            "rkd,kcd->rc", grad_other, proj_other, preferred_element_type=f32
        )
    grad_pooled = pooled_sum.astype(bf16)
    kernel_term = jnp.dot(fine_pixels.T, grad_pooled, preferred_element_type=f32) * grad_scale
    fine_gradient = jnp.dot(grad_pooled, pool_kernel.T, preferred_element_type=f32).astype(bf16)
    kernel_reduced = pix_scatter((kernel_term,), mixing_weight.shape[1])
    projection_gradient, mixing_gradient, kernel_gradient = pix_gather(
        (early_reduced, kernel_reduced), ((projection_term, mixing_term), (kernel_term,))
    )
    return (section_output, fine_gradient, kernel_gradient, projection_gradient, mixing_gradient)


def solution(mesh):
    placed = (
        P("pix", "ch"),
        P("ch", None),
        P(None, None, "ch"),
        P("ch", None),
        P("pix", None),
        P("pix", None),
        P("pix", "ch"),
    )
    return jax.shard_map(
        per_device,
        mesh=mesh,
        in_specs=placed,
        out_specs=(
            P("pix", "ch"),
            P("pix", "ch"),
            P("ch", None),
            P(None, None, "ch"),
            P("ch", None),
        ),
        check_vma=False,
    )
```

```python
import math

import jax
import jax.numpy as jnp
from jax import lax
from jax.sharding import PartitionSpec as P

HD = 64


def pick_table(row_ids, total):
    return (row_ids[:, None] == jnp.arange(total, dtype=jnp.int32)[None, :]).astype(jnp.bfloat16)


def slot_index(neighbour_block, first_row, block_rows):
    present = neighbour_block >= 0
    own_rows = first_row + jnp.arange(block_rows, dtype=jnp.int32)
    slot_rows = jnp.concatenate([own_rows[:, None], jnp.where(present, neighbour_block, 0)], axis=1)
    slot_live = jnp.concatenate([jnp.ones((block_rows, 1), bool), present], axis=1)
    return (slot_rows, slot_live)


def attention_forward(queries, extended, neighbours, row_offset):
    f32 = jnp.float32
    bf16 = jnp.bfloat16
    row_count = queries.shape[0]
    span = queries.shape[1]
    ext_rows = extended.shape[0]
    heads_here = span // HD
    slot_width = neighbours.shape[1] + 1
    score_scale = 1.0 / math.sqrt(HD)
    block_rows = math.gcd(row_count, 512)
    block_count = row_count // block_rows
    query_blocks = queries.reshape(block_count, block_rows, span)
    neighbour_blocks = neighbours.reshape(block_count, block_rows, slot_width - 1)
    flattened = extended.reshape(ext_rows, 2 * span)

    def forward_block(inputs):
        query_block, neighbour_block, first_row = inputs
        slot_rows, slot_live = slot_index(neighbour_block, first_row, block_rows)
        pieces = [flattened[first_row : first_row + block_rows]] + [
            jnp.dot(
                pick_table(slot_rows[:, slot], ext_rows), flattened, preferred_element_type=f32
            ).astype(bf16)
            for slot in range(1, slot_width)
        ]
        gathered = jnp.stack(pieces, axis=1).reshape(block_rows, slot_width, 2, span)
        block_keys = gathered[:, :, 0].reshape(block_rows, slot_width, heads_here, HD)
        block_values = gathered[:, :, 1].reshape(block_rows, slot_width, heads_here, HD)
        scores = (
            jnp.einsum(
                "bhd,bmhd->bhm",
                query_block.reshape(block_rows, heads_here, HD),
                block_keys,
                preferred_element_type=f32,
            )
            * score_scale
        )
        shut = slot_live[:, None, :]
        masked = jnp.where(shut, scores, -1e30)
        largest = jnp.max(masked, axis=2, keepdims=True)
        raised = jnp.where(shut, jnp.exp(masked - largest), 0.0)
        probabilities = raised / jnp.sum(raised, axis=2, keepdims=True)
        weights = probabilities.astype(bf16)
        mixture = jnp.einsum("bhm,bmhd->bhd", weights, block_values, preferred_element_type=f32)
        return (mixture.reshape(block_rows, span).astype(bf16), probabilities, gathered)

    outputs = [
        forward_block((query_blocks[b], neighbour_blocks[b], row_offset + b * block_rows))
        for b in range(block_count)
    ]
    attn_blocks = jnp.stack([out[0] for out in outputs])
    prob_blocks = [out[1] for out in outputs]
    kv_blocks = [out[2] for out in outputs]
    return (attn_blocks.reshape(row_count, span), prob_blocks, kv_blocks)


def attention_backward(
    queries, ext_rows, neighbours, row_offset, grad_attended, prob_blocks, kv_blocks, riders
):
    f32 = jnp.float32
    bf16 = jnp.bfloat16
    row_count = queries.shape[0]
    span = queries.shape[1]
    heads_here = span // HD
    slot_width = neighbours.shape[1] + 1
    score_scale = 1.0 / math.sqrt(HD)
    block_rows = math.gcd(row_count, 512)
    block_count = row_count // block_rows
    query_blocks = queries.reshape(block_count, block_rows, span)
    neighbour_blocks = neighbours.reshape(block_count, block_rows, slot_width - 1)
    grad_blocks = grad_attended.reshape(block_count, block_rows, span)

    def backward_block(carried, inputs):
        query_block, neighbour_block, first_row, grad_block, probabilities, gathered = inputs
        slot_rows, slot_live = slot_index(neighbour_block, first_row, block_rows)
        block_keys = gathered[:, :, 0].reshape(block_rows, slot_width, heads_here, HD).astype(f32)
        block_values = gathered[:, :, 1].reshape(block_rows, slot_width, heads_here, HD).astype(f32)
        grad_mix = grad_block.reshape(block_rows, heads_here, HD).astype(f32)
        grad_weights = jnp.einsum("bhd,bmhd->bhm", grad_mix, block_values)
        grad_scores = (
            probabilities
            * (grad_weights - jnp.sum(probabilities * grad_weights, axis=2, keepdims=True))
            * score_scale
        )
        grad_query = jnp.einsum("bhm,bmhd->bhd", grad_scores, block_keys).reshape(block_rows, span)
        query_wide = query_block.reshape(block_rows, heads_here, HD).astype(f32)
        grad_keys = jnp.einsum("bhm,bhd->bmhd", grad_scores, query_wide)
        rounded = lax.optimization_barrier(probabilities.astype(bf16))
        grad_values = jnp.einsum("bhm,bhd->bmhd", rounded.astype(f32), grad_mix)
        contribution = (
            jnp.stack([grad_keys, grad_values], axis=2)
            .reshape(block_rows, slot_width, 2 * span)
            .astype(bf16)
        )
        for slot in range(1, slot_width):
            carried = carried + jnp.einsum(
                "bx,bc->xc",
                pick_table(slot_rows[:, slot], ext_rows),
                contribution[:, slot],
                preferred_element_type=f32,
            )
        return (carried, (grad_query, contribution[:, 0]))

    carried = jnp.zeros((ext_rows, 2 * span), f32)
    query_grads = []
    for b in range(block_count):
        carried, grad_query = backward_block(
            carried,
            (query_blocks[b], neighbour_blocks[b], row_offset + b * block_rows, grad_blocks[b],
             prob_blocks[b], kv_blocks[b]),
        )
        query_grads.append(grad_query)
        if b == 0:
            carried, riders = lax.optimization_barrier((carried, riders))
    own_grads = jnp.concatenate([pair[1] for pair in query_grads], axis=0)
    query_grads = jnp.stack([pair[0] for pair in query_grads])
    carried = carried.at[:row_count].add(own_grads.astype(f32))
    return (carried.reshape(ext_rows, 2, span), query_grads.reshape(row_count, span), riders)


def ch_exchange(value):
    size = lax.axis_size("ch")
    return [
        lax.ppermute(value, "ch", [(i, (i + shift) % size) for i in range(size)])
        for shift in range(1, size)
    ]


def ch_assemble(own, others, axis):
    size = len(others) + 1
    index = lax.axis_index("ch")
    pieces = [own] + others
    result = None
    for case in range(size):
        ordered = jnp.concatenate([pieces[(case - j) % size] for j in range(size)], axis=axis)
        result = ordered if result is None else jnp.where(index == case, ordered, result)
    return result


def core_swap(value):
    size = lax.axis_size("pix")
    return lax.ppermute(value, "pix", [(i, i ^ 1) for i in range(size)])


def pix_scatter(terms, width):
    size = lax.axis_size("pix")
    core = lax.axis_index("pix") % 2
    flat = jnp.concatenate([term.reshape(-1, width) for term in terms], axis=0)
    rows = flat.shape[0]
    chunk = -(-rows // (2 * size))
    flat = jnp.pad(flat, ((0, 2 * size * chunk - rows), (0, 0)))
    halves = flat.reshape(2, size * chunk, width)
    keep = jnp.where(core == 0, halves[0], halves[1])
    send = jnp.where(core == 0, halves[1], halves[0])
    mine = keep + core_swap(send)
    parts = lax.all_to_all(mine.reshape(size, chunk, width), "pix", 0, 0, tiled=True)
    return jnp.sum(parts.reshape(size // 2, 2, chunk, width), axis=0)


def pix_gather(reduced_groups, term_groups):
    size = lax.axis_size("pix")
    core = lax.axis_index("pix") % 2
    width = reduced_groups[0].shape[-1]
    joined = jnp.concatenate(reduced_groups, axis=1)
    total = joined.shape[1]
    spread = jnp.broadcast_to(joined[None], (size // 2, 2, total, width))
    got = lax.all_to_all(spread.reshape(size, total, width), "pix", 0, 0, tiled=True)
    other = core_swap(got)
    first = jnp.where(core == 0, got, other)
    second = jnp.where(core == 0, other, got)
    results = []
    offset = 0
    for reduced, terms in zip(reduced_groups, term_groups):
        chunk = reduced.shape[1]
        flat = jnp.concatenate(
            [
                first[:, offset : offset + chunk].reshape(size * chunk, width),
                second[:, offset : offset + chunk].reshape(size * chunk, width),
            ],
            axis=0,
        )
        offset += chunk
        row = 0
        for term in terms:
            count = term.size // width
            results.append(flat[row : row + count].reshape(term.shape))
            row += count
    return results


def per_device(
    fine_pixels, pool_kernel, projections, mixing_weight, send_list, neighbours, cotangent
):
    f32 = jnp.float32
    bf16 = jnp.bfloat16
    row_count = fine_pixels.shape[0]
    half_width = projections.shape[2]
    ch_size = lax.axis_size("ch")
    ch_index = lax.axis_index("ch")
    peer_count = lax.axis_size("pix")
    slot_count = send_list.shape[1]
    grad_scale = 1.0 / math.sqrt(row_count * peer_count)
    send_pick = pick_table(send_list.reshape(-1), row_count)
    fine_others = ch_exchange(fine_pixels)
    kernel_others = ch_exchange(pool_kernel)
    pooled_sum = jnp.dot(fine_pixels, pool_kernel, preferred_element_type=f32)
    for fine_other, kernel_other in zip(fine_others, kernel_others):
        pooled_sum = pooled_sum + jnp.dot(fine_other, kernel_other, preferred_element_type=f32)
    pooled_all = pooled_sum.astype(bf16)
    mix_pieces = mixing_weight.reshape(mixing_weight.shape[0], ch_size, half_width)
    mix_sends = [
        jnp.take(mix_pieces, (ch_index + shift) % ch_size, axis=1) for shift in range(1, ch_size)
    ]
    pooled_all, proj_send, mix_sends = lax.optimization_barrier(
        (pooled_all, projections, mix_sends)
    )
    cot_others = ch_exchange(cotangent)
    proj_others = ch_exchange(proj_send)
    mix_others = [
        lax.ppermute(mix_send, "ch", [(i, (i + shift) % ch_size) for i in range(ch_size)])
        for shift, mix_send in zip(range(1, ch_size), mix_sends)
    ]
    mix_own = jnp.take(mix_pieces, ch_index, axis=1)
    pooled = lax.dynamic_slice_in_dim(pooled_all, ch_index * half_width, half_width, axis=1)
    upstream = ch_assemble(cotangent, cot_others, axis=1)
    projected = jnp.einsum(
        "rc,kcd->rkd", pooled_all, projections, preferred_element_type=f32
    ).astype(bf16)
    queries = projected[:, 0]
    key_value = projected[:, 1:]
    outgoing = (
        jnp.dot(send_pick, key_value.reshape(row_count, 2 * half_width), preferred_element_type=f32)
        .astype(bf16)
        .reshape(peer_count, slot_count, 2, half_width)
    )
    incoming = lax.all_to_all(outgoing, "pix", split_axis=0, concat_axis=0, tiled=True)
    extended = jnp.concatenate(
        [key_value, incoming.reshape(peer_count * slot_count, 2, half_width)], axis=0
    )
    attended, prob_blocks, kv_blocks = attention_forward(queries, extended, neighbours, 0)
    attended_others = ch_exchange(attended)
    grad_attended = jnp.dot(upstream, mixing_weight.T, preferred_element_type=f32).astype(bf16)
    mixing_term = jnp.dot(attended.T, upstream, preferred_element_type=f32) * grad_scale
    carried, query_grads, (attended_others, mix_others, proj_others) = attention_backward(
        queries, extended.shape[0], neighbours, 0, grad_attended, prob_blocks, kv_blocks,
        (attended_others, mix_others, proj_others),
    )
    branch = jnp.dot(attended, mix_own, preferred_element_type=f32)
    for attended_other, mix_other in zip(attended_others, mix_others):
        branch = branch + jnp.dot(attended_other, mix_other, preferred_element_type=f32)
    section_output = (pooled.astype(f32) + branch).astype(bf16)
    remote_grads = carried[row_count:].reshape(peer_count, slot_count, 2, half_width)
    returned = lax.all_to_all(remote_grads, "pix", split_axis=0, concat_axis=0, tiled=True)
    returned_rows = jnp.einsum(
        "px,pc->xc",
        send_pick,
        returned.reshape(peer_count * slot_count, 2 * half_width).astype(bf16),
        preferred_element_type=f32,
    )
    local_grads = carried[:row_count] + returned_rows.reshape(row_count, 2, half_width)
    grad_projected = jnp.concatenate(
        [query_grads.reshape(row_count, 1, half_width), local_grads], axis=1
    ).astype(bf16)
    grad_others = ch_exchange(grad_projected)
    projection_term = (
        jnp.einsum("rc,rkd->kcd", pooled_all, grad_projected, preferred_element_type=f32)
        * grad_scale
    )
    early_reduced = pix_scatter((projection_term, mixing_term), mixing_weight.shape[1])
    pooled_sum = upstream.astype(f32) + jnp.einsum(
        "rkd,kcd->rc", grad_projected, projections, preferred_element_type=f32
    )
    for grad_other, proj_other in zip(grad_others, proj_others):
        pooled_sum = pooled_sum + jnp.einsum(
            "rkd,kcd->rc", grad_other, proj_other, preferred_element_type=f32
        )
    grad_pooled = pooled_sum.astype(bf16)
    kernel_term = jnp.dot(fine_pixels.T, grad_pooled, preferred_element_type=f32) * grad_scale
    fine_gradient = jnp.dot(grad_pooled, pool_kernel.T, preferred_element_type=f32).astype(bf16)
    kernel_reduced = pix_scatter((kernel_term,), mixing_weight.shape[1])
    projection_gradient, mixing_gradient, kernel_gradient = pix_gather(
        (early_reduced, kernel_reduced), ((projection_term, mixing_term), (kernel_term,))
    )
    return (section_output, fine_gradient, kernel_gradient, projection_gradient, mixing_gradient)


def solution(mesh):
    placed = (
        P("pix", "ch"),
        P("ch", None),
        P(None, None, "ch"),
        P("ch", None),
        P("pix", None),
        P("pix", None),
        P("pix", "ch"),
    )
    return jax.shard_map(
        per_device,
        mesh=mesh,
        in_specs=placed,
        out_specs=(
            P("pix", "ch"),
            P("pix", "ch"),
            P("ch", None),
            P(None, None, "ch"),
            P("ch", None),
        ),
        check_vma=False,
    )
```

```python
import math

import jax
import jax.numpy as jnp
from jax import lax
from jax.sharding import PartitionSpec as P

HD = 64


def pick_table(row_ids, total):
    return (row_ids[:, None] == jnp.arange(total, dtype=jnp.int32)[None, :]).astype(jnp.bfloat16)


def slot_index(neighbour_block, first_row, block_rows):
    present = neighbour_block >= 0
    own_rows = first_row + jnp.arange(block_rows, dtype=jnp.int32)
    slot_rows = jnp.concatenate([own_rows[:, None], jnp.where(present, neighbour_block, 0)], axis=1)
    slot_live = jnp.concatenate([jnp.ones((block_rows, 1), bool), present], axis=1)
    return (slot_rows, slot_live)


def attention_forward(queries, extended, neighbours, row_offset):
    f32 = jnp.float32
    bf16 = jnp.bfloat16
    row_count = queries.shape[0]
    span = queries.shape[1]
    ext_rows = extended.shape[0]
    heads_here = span // HD
    slot_width = neighbours.shape[1] + 1
    score_scale = 1.0 / math.sqrt(HD)
    block_rows = math.gcd(row_count, 512)
    block_count = row_count // block_rows
    query_blocks = queries.reshape(block_count, block_rows, span)
    neighbour_blocks = neighbours.reshape(block_count, block_rows, slot_width - 1)
    flattened = extended.reshape(ext_rows, 2 * span)

    def forward_block(inputs):
        query_block, neighbour_block, first_row = inputs
        slot_rows, slot_live = slot_index(neighbour_block, first_row, block_rows)
        pieces = [flattened[first_row : first_row + block_rows]] + [
            jnp.dot(
                pick_table(slot_rows[:, slot], ext_rows), flattened, preferred_element_type=f32
            ).astype(bf16)
            for slot in range(1, slot_width)
        ]
        gathered = jnp.stack(pieces, axis=1).reshape(block_rows, slot_width, 2, span)
        block_keys = gathered[:, :, 0].reshape(block_rows, slot_width, heads_here, HD)
        block_values = gathered[:, :, 1].reshape(block_rows, slot_width, heads_here, HD)
        scores = (
            jnp.einsum(
                "bhd,bmhd->bhm",
                query_block.reshape(block_rows, heads_here, HD),
                block_keys,
                preferred_element_type=f32,
            )
            * score_scale
        )
        shut = slot_live[:, None, :]
        masked = jnp.where(shut, scores, -1e30)
        largest = jnp.max(masked, axis=2, keepdims=True)
        raised = jnp.where(shut, jnp.exp(masked - largest), 0.0)
        probabilities = raised / jnp.sum(raised, axis=2, keepdims=True)
        weights = probabilities.astype(bf16)
        mixture = jnp.einsum("bhm,bmhd->bhd", weights, block_values, preferred_element_type=f32)
        return (mixture.reshape(block_rows, span).astype(bf16), probabilities, gathered)

    outputs = [
        forward_block((query_blocks[b], neighbour_blocks[b], row_offset + b * block_rows))
        for b in range(block_count)
    ]
    attn_blocks = jnp.stack([out[0] for out in outputs])
    prob_blocks = [out[1] for out in outputs]
    kv_blocks = [out[2] for out in outputs]
    return (attn_blocks.reshape(row_count, span), prob_blocks, kv_blocks)


def attention_backward(
    queries, ext_rows, neighbours, row_offset, grad_attended, prob_blocks, kv_blocks, riders
):
    f32 = jnp.float32
    bf16 = jnp.bfloat16
    row_count = queries.shape[0]
    span = queries.shape[1]
    heads_here = span // HD
    slot_width = neighbours.shape[1] + 1
    score_scale = 1.0 / math.sqrt(HD)
    block_rows = math.gcd(row_count, 512)
    block_count = row_count // block_rows
    query_blocks = queries.reshape(block_count, block_rows, span)
    neighbour_blocks = neighbours.reshape(block_count, block_rows, slot_width - 1)
    grad_blocks = grad_attended.reshape(block_count, block_rows, span)

    def backward_block(carried, inputs):
        query_block, neighbour_block, first_row, grad_block, probabilities, gathered = inputs
        slot_rows, slot_live = slot_index(neighbour_block, first_row, block_rows)
        block_keys = gathered[:, :, 0].reshape(block_rows, slot_width, heads_here, HD).astype(f32)
        block_values = gathered[:, :, 1].reshape(block_rows, slot_width, heads_here, HD).astype(f32)
        grad_mix = grad_block.reshape(block_rows, heads_here, HD).astype(f32)
        grad_weights = jnp.einsum("bhd,bmhd->bhm", grad_mix, block_values)
        grad_scores = (
            probabilities
            * (grad_weights - jnp.sum(probabilities * grad_weights, axis=2, keepdims=True))
            * score_scale
        )
        grad_query = jnp.einsum("bhm,bmhd->bhd", grad_scores, block_keys).reshape(block_rows, span)
        query_wide = query_block.reshape(block_rows, heads_here, HD).astype(f32)
        grad_keys = jnp.einsum("bhm,bhd->bmhd", grad_scores, query_wide)
        rounded = lax.optimization_barrier(probabilities.astype(bf16))
        grad_values = jnp.einsum("bhm,bhd->bmhd", rounded.astype(f32), grad_mix)
        contribution = (
            jnp.stack([grad_keys, grad_values], axis=2)
            .reshape(block_rows, slot_width, 2 * span)
            .astype(bf16)
        )
        for slot in range(1, slot_width):
            carried = carried + jnp.einsum(
                "bx,bc->xc",
                pick_table(slot_rows[:, slot], ext_rows),
                contribution[:, slot],
                preferred_element_type=f32,
            )
        return (carried, (grad_query, contribution[:, 0]))

    carried = jnp.zeros((ext_rows, 2 * span), f32)
    query_grads = []
    for b in range(block_count):
        carried, grad_query = backward_block(
            carried,
            (query_blocks[b], neighbour_blocks[b], row_offset + b * block_rows, grad_blocks[b],
             prob_blocks[b], kv_blocks[b]),
        )
        query_grads.append(grad_query)
        if b == block_count - 1:
            carried, riders = lax.optimization_barrier((carried, riders))
    own_grads = jnp.concatenate([pair[1] for pair in query_grads], axis=0)
    query_grads = jnp.stack([pair[0] for pair in query_grads])
    carried = carried.at[:row_count].add(own_grads.astype(f32))
    return (carried.reshape(ext_rows, 2, span), query_grads.reshape(row_count, span), riders)


def ch_exchange(value):
    size = lax.axis_size("ch")
    return [
        lax.ppermute(value, "ch", [(i, (i + shift) % size) for i in range(size)])
        for shift in range(1, size)
    ]


def ch_assemble(own, others, axis):
    size = len(others) + 1
    index = lax.axis_index("ch")
    pieces = [own] + others
    result = None
    for case in range(size):
        ordered = jnp.concatenate([pieces[(case - j) % size] for j in range(size)], axis=axis)
        result = ordered if result is None else jnp.where(index == case, ordered, result)
    return result


def core_swap(value):
    size = lax.axis_size("pix")
    return lax.ppermute(value, "pix", [(i, i ^ 1) for i in range(size)])


def pix_scatter(terms, width):
    size = lax.axis_size("pix")
    core = lax.axis_index("pix") % 2
    flat = jnp.concatenate([term.reshape(-1, width) for term in terms], axis=0)
    rows = flat.shape[0]
    chunk = -(-rows // (2 * size))
    flat = jnp.pad(flat, ((0, 2 * size * chunk - rows), (0, 0)))
    halves = flat.reshape(2, size * chunk, width)
    keep = jnp.where(core == 0, halves[0], halves[1])
    send = jnp.where(core == 0, halves[1], halves[0])
    mine = keep + core_swap(send)
    parts = lax.all_to_all(mine.reshape(size, chunk, width), "pix", 0, 0, tiled=True)
    return jnp.sum(parts.reshape(size // 2, 2, chunk, width), axis=0)


def pix_gather(reduced_groups, term_groups):
    size = lax.axis_size("pix")
    core = lax.axis_index("pix") % 2
    width = reduced_groups[0].shape[-1]
    joined = jnp.concatenate(reduced_groups, axis=1)
    total = joined.shape[1]
    spread = jnp.broadcast_to(joined[None], (size // 2, 2, total, width))
    got = lax.all_to_all(spread.reshape(size, total, width), "pix", 0, 0, tiled=True)
    other = core_swap(got)
    first = jnp.where(core == 0, got, other)
    second = jnp.where(core == 0, other, got)
    results = []
    offset = 0
    for reduced, terms in zip(reduced_groups, term_groups):
        chunk = reduced.shape[1]
        flat = jnp.concatenate(
            [
                first[:, offset : offset + chunk].reshape(size * chunk, width),
                second[:, offset : offset + chunk].reshape(size * chunk, width),
            ],
            axis=0,
        )
        offset += chunk
        row = 0
        for term in terms:
            count = term.size // width
            results.append(flat[row : row + count].reshape(term.shape))
            row += count
    return results


def per_device(
    fine_pixels, pool_kernel, projections, mixing_weight, send_list, neighbours, cotangent
):
    f32 = jnp.float32
    bf16 = jnp.bfloat16
    row_count = fine_pixels.shape[0]
    half_width = projections.shape[2]
    ch_size = lax.axis_size("ch")
    ch_index = lax.axis_index("ch")
    peer_count = lax.axis_size("pix")
    slot_count = send_list.shape[1]
    grad_scale = 1.0 / math.sqrt(row_count * peer_count)
    send_pick = pick_table(send_list.reshape(-1), row_count)
    fine_others = ch_exchange(fine_pixels)
    kernel_others = ch_exchange(pool_kernel)
    pooled_sum = jnp.dot(fine_pixels, pool_kernel, preferred_element_type=f32)
    for fine_other, kernel_other in zip(fine_others, kernel_others):
        pooled_sum = pooled_sum + jnp.dot(fine_other, kernel_other, preferred_element_type=f32)
    pooled_all = pooled_sum.astype(bf16)
    mix_pieces = mixing_weight.reshape(mixing_weight.shape[0], ch_size, half_width)
    mix_sends = [
        jnp.take(mix_pieces, (ch_index + shift) % ch_size, axis=1) for shift in range(1, ch_size)
    ]
    pooled_all, proj_send, mix_sends = lax.optimization_barrier(
        (pooled_all, projections, mix_sends)
    )
    cot_others = ch_exchange(cotangent)
    proj_others = ch_exchange(proj_send)
    mix_others = [
        lax.ppermute(mix_send, "ch", [(i, (i + shift) % ch_size) for i in range(ch_size)])
        for shift, mix_send in zip(range(1, ch_size), mix_sends)
    ]
    mix_own = jnp.take(mix_pieces, ch_index, axis=1)
    pooled = lax.dynamic_slice_in_dim(pooled_all, ch_index * half_width, half_width, axis=1)
    upstream = ch_assemble(cotangent, cot_others, axis=1)
    projected = jnp.einsum(
        "rc,kcd->rkd", pooled_all, projections, preferred_element_type=f32
    ).astype(bf16)
    queries = projected[:, 0]
    key_value = projected[:, 1:]
    outgoing = (
        jnp.dot(send_pick, key_value.reshape(row_count, 2 * half_width), preferred_element_type=f32)
        .astype(bf16)
        .reshape(peer_count, slot_count, 2, half_width)
    )
    incoming = lax.all_to_all(outgoing, "pix", split_axis=0, concat_axis=0, tiled=True)
    extended = jnp.concatenate(
        [key_value, incoming.reshape(peer_count * slot_count, 2, half_width)], axis=0
    )
    attended, prob_blocks, kv_blocks = attention_forward(queries, extended, neighbours, 0)
    attended_others = ch_exchange(attended)
    grad_attended = jnp.dot(upstream, mixing_weight.T, preferred_element_type=f32).astype(bf16)
    mixing_term = jnp.dot(attended.T, upstream, preferred_element_type=f32) * grad_scale
    carried, query_grads, (attended_others, mix_others, proj_others) = attention_backward(
        queries, extended.shape[0], neighbours, 0, grad_attended, prob_blocks, kv_blocks,
        (attended_others, mix_others, proj_others),
    )
    branch = jnp.dot(attended, mix_own, preferred_element_type=f32)
    for attended_other, mix_other in zip(attended_others, mix_others):
        branch = branch + jnp.dot(attended_other, mix_other, preferred_element_type=f32)
    section_output = (pooled.astype(f32) + branch).astype(bf16)
    remote_grads = carried[row_count:].reshape(peer_count, slot_count, 2, half_width)
    returned = lax.all_to_all(remote_grads, "pix", split_axis=0, concat_axis=0, tiled=True)
    returned_rows = jnp.einsum(
        "px,pc->xc",
        send_pick,
        returned.reshape(peer_count * slot_count, 2 * half_width).astype(bf16),
        preferred_element_type=f32,
    )
    local_grads = carried[:row_count] + returned_rows.reshape(row_count, 2, half_width)
    grad_projected = jnp.concatenate(
        [query_grads.reshape(row_count, 1, half_width), local_grads], axis=1
    ).astype(bf16)
    grad_others = ch_exchange(grad_projected)
    projection_term = (
        jnp.einsum("rc,rkd->kcd", pooled_all, grad_projected, preferred_element_type=f32)
        * grad_scale
    )
    early_reduced = pix_scatter((projection_term, mixing_term), mixing_weight.shape[1])
    pooled_sum = upstream.astype(f32) + jnp.einsum(
        "rkd,kcd->rc", grad_projected, projections, preferred_element_type=f32
    )
    for grad_other, proj_other in zip(grad_others, proj_others):
        pooled_sum = pooled_sum + jnp.einsum(
            "rkd,kcd->rc", grad_other, proj_other, preferred_element_type=f32
        )
    grad_pooled = pooled_sum.astype(bf16)
    kernel_term = jnp.dot(fine_pixels.T, grad_pooled, preferred_element_type=f32) * grad_scale
    fine_gradient = jnp.dot(grad_pooled, pool_kernel.T, preferred_element_type=f32).astype(bf16)
    kernel_reduced = pix_scatter((kernel_term,), mixing_weight.shape[1])
    projection_gradient, mixing_gradient, kernel_gradient = pix_gather(
        (early_reduced, kernel_reduced), ((projection_term, mixing_term), (kernel_term,))
    )
    return (section_output, fine_gradient, kernel_gradient, projection_gradient, mixing_gradient)


def solution(mesh):
    placed = (
        P("pix", "ch"),
        P("ch", None),
        P(None, None, "ch"),
        P("ch", None),
        P("pix", None),
        P("pix", None),
        P("pix", "ch"),
    )
    return jax.shard_map(
        per_device,
        mesh=mesh,
        in_specs=placed,
        out_specs=(
            P("pix", "ch"),
            P("pix", "ch"),
            P("ch", None),
            P(None, None, "ch"),
            P("ch", None),
        ),
        check_vma=False,
    )
```
